32 devices in a mesh: groups: 2 (over x), rows: 8 (over z, y), cols: 2 (over core).
Axes of the slice: x: 2, y: 2, z: 4, core: 2. Of those that a mesh axis runs over, the one named last changes fastest.
Arguments:
- radiance: float32 [224, 512, 256], P(None, ('groups', 'rows'), 'cols'), parts along dimension 1, may hold values from -6 to 6
- decorrelation: float32 [224, 224], replicated, may hold values from -0.375 to 0.375
Outputs:
- coefficients: float32 [224, 512, 256], P(None, ('groups', 'rows'), 'cols'), parts along dimension 1
The draws below stay inside these ranges and needn't reach their ends.
There are 2 independent parts, one for each index of `groups`. The reference program is written for one: setup_inputs(seed, part) draws one part's arguments, and reference() takes and returns one part's arrays. A program takes and returns all parts, laid end to end along the dimension named above; an argument that names none is the same for every part. Nothing has to cross between parts.
All inputs are finite; a program needn't handle non-finite values.
Results may differ from the reference program's by a relative error of at most 0.00005.
Values sent between devices are 32-bit elements; how exact they have to be, the bound alone decides.
No kernel may reach another device: no remote copies, remote signals or barrier semaphores. Data moves between devices by JAX's collectives and lax.ppermute only.
A program may use at most 128 MiB of HBM per device.

```python
import jax
import jax.numpy as jnp
from jax import lax

BANDS = 224
LEVELS = 3
HEIGHT = 256
WIDTH = 256


def block_scale(key, shape, pieces, smallest, top_value):
    def one(dim, blocks):
        draws = jax.random.uniform(jax.random.fold_in(jax.random.fold_in(key, 6), dim), (blocks,), jnp.float32, smallest / len(pieces), top_value / len(pieces))
        return jnp.repeat(jnp.exp(draws), shape[dim] // blocks).reshape((-1,) + (1,) * (len(shape) - dim - 1))

    gain = one(*pieces[0])
    for cut in pieces[1:]:
        gain = gain * one(*cut)
    return gain


def centred(stream_key, extent, width, limit, cuts=(), dtype=jnp.bfloat16):
    entries = jax.random.normal(stream_key, extent, jnp.float32) * width
    if len(cuts) > 0:
        entries = block_scale(stream_key, extent, cuts, -0.22, 0.18) * entries
    return jnp.clip(entries, min=-limit, max=limit).astype(dtype)


def setup_inputs(seed: int = 0, part: int = 0) -> dict:
    streams_of = jax.random.split(jax.random.key(seed), 3)
    part_keys = jax.random.split(jax.random.fold_in(streams_of[2], part), 3)
    return {
        "radiance": centred(part_keys[0], (BANDS, HEIGHT, WIDTH), 1.0, 6.0, ((1, 8), (2, 2)), jnp.float32),
        "decorrelation": centred(streams_of[1], (BANDS, BANDS), BANDS ** -0.5, 0.375, (), jnp.float32),
    }


alpha_one = -1.586134342059924
beta_one = -0.052980118572961
alpha_two = 0.882911075530934
beta_two = 0.443506852043971
scale_k = 1.230174104914001


def split_axis(x, dim):
    shape = x.shape[:dim] + (x.shape[dim] // 2, 2) + x.shape[dim + 1:]
    paired = x.reshape(shape)
    return lax.index_in_dim(paired, 0, dim + 1, keepdims=False), lax.index_in_dim(paired, 1, dim + 1, keepdims=False)


def join_axis(even_part, odd_part, dim):
    stacked = jnp.stack([even_part, odd_part], axis=dim + 1)
    shape = even_part.shape[:dim] + (even_part.shape[dim] * 2,) + even_part.shape[dim + 1:]
    return stacked.reshape(shape)


def mirror_next(values, dim):
    size_here = values.shape[dim]
    return jnp.concatenate([lax.slice_in_dim(values, 1, size_here, axis=dim), lax.slice_in_dim(values, size_here - 1, size_here, axis=dim)], axis=dim)


def mirror_prev(values, dim):
    size_here = values.shape[dim]
    return jnp.concatenate([lax.slice_in_dim(values, 0, 1, axis=dim), lax.slice_in_dim(values, 0, size_here - 1, axis=dim)], axis=dim)


def lift_axis(x, dim):
    even_part, odd_part = split_axis(x, dim)
    for coeff_pair in ((alpha_one, beta_one), (alpha_two, beta_two)):
        odd_part = odd_part + coeff_pair[0] * (even_part + mirror_next(even_part, dim))
        even_part = even_part + coeff_pair[1] * (mirror_prev(odd_part, dim) + odd_part)
    return join_axis(even_part / scale_k, odd_part * scale_k, dim)


def decompose(level_array, remaining):
    if remaining == 0:
        return level_array
    lifted = lift_axis(lift_axis(level_array, 1), 2)
    band_count, height_here, width_here = lifted.shape
    blocks = lifted.reshape(band_count, height_here // 2, 2, width_here // 2, 2)
    inner_part = decompose(blocks[:, :, 0, :, 0], remaining - 1)
    return blocks.at[:, :, 0, :, 0].set(inner_part).reshape(band_count, height_here, width_here)


def reference(radiance, decorrelation):
    band_count = radiance.shape[0]
    flattened = radiance.reshape(band_count, -1)
    mixed = jnp.dot(decorrelation, flattened, precision=lax.Precision.HIGHEST, preferred_element_type=jnp.float32).reshape(radiance.shape)
    return decompose(mixed, LEVELS)
```

```python
import jax
import jax.numpy as jnp
from jax import lax
from jax.sharding import PartitionSpec as P

LEVELS = 3


alpha_one = -1.586134342059924
beta_one = -0.052980118572961
alpha_two = 0.882911075530934
beta_two = 0.443506852043971
scale_k = 1.230174104914001


def shifted(x, axis, by):
    size = lax.axis_size(axis)
    pairs = [(i, i + by) for i in range(size) if 0 <= i + by < size]
    return lax.ppermute(x, axis, pairs)


def split_axis(x, dim):
    shape = x.shape[:dim] + (x.shape[dim] // 2, 2) + x.shape[dim + 1 :]
    paired = x.reshape(shape)
    return (
        lax.index_in_dim(paired, 0, dim + 1, keepdims=False),
        lax.index_in_dim(paired, 1, dim + 1, keepdims=False),
    )


def join_axis(even_part, odd_part, dim):
    stacked = jnp.stack([even_part, odd_part], axis=dim + 1)
    shape = even_part.shape[:dim] + (even_part.shape[dim] * 2,) + even_part.shape[dim + 1 :]
    return stacked.reshape(shape)


def lift_axis(x, dim, axis):
    a1, b1, a2, b2 = alpha_one, beta_one, alpha_two, beta_two
    even, odd = split_axis(x, dim)
    m = even.shape[dim]

    def sl(v, lo, hi):
        return lax.slice_in_dim(v, lo, hi, axis=dim)

    def cat(parts):
        return jnp.concatenate(parts, axis=dim)

    s_first, s_second, d_first = sl(even, 0, 1), sl(even, 1, 2), sl(odd, 0, 1)
    s_pen, s_last = sl(even, m - 2, m - 1), sl(even, m - 1, m)
    d_pen, d_last = sl(odd, m - 2, m - 1), sl(odd, m - 1, m)

    to_next = cat([d_last + a1 * s_last, s_last + b1 * (d_pen + a1 * (s_pen + s_last))])
    to_prev = cat([s_first, s_first + b1 * (d_first + a1 * (s_first + s_second))])
    from_prev = shifted(to_next, axis, 1)
    from_next = shifted(to_prev, axis, -1)
    a_in, b_in = sl(from_prev, 0, 1), sl(from_prev, 1, 2)
    s_in, c_in = sl(from_next, 0, 1), sl(from_next, 1, 2)

    at_first = lax.axis_index(axis) == 0
    at_last = lax.axis_index(axis) == lax.axis_size(axis) - 1

    s_after = jnp.where(at_last, s_last, s_in)
    d1 = odd + a1 * (even + cat([sl(even, 1, m), s_after]))
    d1_before = jnp.where(at_first, sl(d1, 0, 1), a_in + a1 * s_first)
    s1 = even + b1 * (cat([d1_before, sl(d1, 0, m - 1)]) + d1)
    s1_after = jnp.where(at_last, sl(s1, m - 1, m), c_in + b1 * sl(d1, m - 1, m))
    d2 = d1 + a2 * (s1 + cat([sl(s1, 1, m), s1_after]))
    s1_before = b_in + b1 * d1_before
    d2_before = jnp.where(
        at_first, sl(d2, 0, 1), d1_before + a2 * (s1_before + sl(s1, 0, 1))
    )
    s2 = s1 + b2 * (cat([d2_before, sl(d2, 0, m - 1)]) + d2)
    return join_axis(s2 / scale_k, d2 * scale_k, dim)


def decompose(level_array, remaining):
    if remaining == 0:
        return level_array
    lifted = lift_axis(lift_axis(level_array, 1, "rows"), 2, "cols")
    band_count, height_here, width_here = lifted.shape
    blocks = lifted.reshape(band_count, height_here // 2, 2, width_here // 2, 2)
    inner_part = decompose(blocks[:, :, 0, :, 0], remaining - 1)
    return blocks.at[:, :, 0, :, 0].set(inner_part).reshape(band_count, height_here, width_here)


def on_device(radiance, decorrelation):
    band_count = radiance.shape[0]
    flattened = radiance.reshape(band_count, -1)
    mixed = jnp.dot(
        decorrelation,
        flattened,
        precision=lax.Precision.HIGHEST,
        preferred_element_type=jnp.float32,
    ).reshape(radiance.shape)
    return decompose(mixed, LEVELS)


def solution(mesh):
    placed = (P(None, ("groups", "rows"), "cols"), P())
    return jax.shard_map(
        on_device,
        mesh=mesh,
        in_specs=placed,
        out_specs=P(None, ("groups", "rows"), "cols"),
        check_vma=False,
    )
```

```python
import jax
import jax.numpy as jnp
from jax import lax
from jax.sharding import PartitionSpec as P

LEVELS = 3


alpha_one = -1.586134342059924
beta_one = -0.052980118572961
alpha_two = 0.882911075530934
beta_two = 0.443506852043971
scale_k = 1.230174104914001


def shifted(x, axis, by):
    size = lax.axis_size(axis)
    pairs = [(i, i + by) for i in range(size) if 0 <= i + by < size]
    return lax.ppermute(x, axis, pairs)


def split_axis(x, dim):
    shape = x.shape[:dim] + (x.shape[dim] // 2, 2) + x.shape[dim + 1 :]
    paired = x.reshape(shape)
    return (
        lax.index_in_dim(paired, 0, dim + 1, keepdims=False),
        lax.index_in_dim(paired, 1, dim + 1, keepdims=False),
    )


def join_axis(even_part, odd_part, dim):
    stacked = jnp.stack([even_part, odd_part], axis=dim + 1)
    shape = even_part.shape[:dim] + (even_part.shape[dim] * 2,) + even_part.shape[dim + 1 :]
    return stacked.reshape(shape)


def lift_axis(x, dim, axis):
    a1, b1, a2, b2 = alpha_one, beta_one, alpha_two, beta_two
    even, odd = split_axis(x, dim)
    m = even.shape[dim]

    def sl(v, lo, hi):
        return lax.slice_in_dim(v, lo, hi, axis=dim)

    def cat(parts):
        return jnp.concatenate(parts, axis=dim)

    s_first, s_second, d_first = sl(even, 0, 1), sl(even, 1, 2), sl(odd, 0, 1)
    s_pen, s_last = sl(even, m - 2, m - 1), sl(even, m - 1, m)
    d_pen, d_last = sl(odd, m - 2, m - 1), sl(odd, m - 1, m)

    to_next = cat([d_last + a1 * s_last, s_last + b1 * (d_pen + a1 * (s_pen + s_last))])
    to_prev = cat([s_first, s_first + b1 * (d_first + a1 * (s_first + s_second))])
    from_prev = shifted(to_next, axis, 1)
    from_next = shifted(to_prev, axis, -1)
    a_in, b_in = sl(from_prev, 0, 1), sl(from_prev, 1, 2)
    s_in, c_in = sl(from_next, 0, 1), sl(from_next, 1, 2)

    at_first = lax.axis_index(axis) == 0
    at_last = lax.axis_index(axis) == lax.axis_size(axis) - 1

    s_after = jnp.where(at_last, s_last, s_in)
    d1 = odd + a1 * (even + cat([sl(even, 1, m), s_after]))
    d1_before = jnp.where(at_first, sl(d1, 0, 1), a_in + a1 * s_first)
    s1 = even + b1 * (cat([d1_before, sl(d1, 0, m - 1)]) + d1)
    s1_after = jnp.where(at_last, sl(s1, m - 1, m), c_in + b1 * sl(d1, m - 1, m))
    d2 = d1 + a2 * (s1 + cat([sl(s1, 1, m), s1_after]))
    s1_before = b_in + b1 * d1_before
    d2_before = jnp.where(
        at_first, sl(d2, 0, 1), d1_before + a2 * (s1_before + sl(s1, 0, 1))
    )
    s2 = s1 + b2 * (cat([d2_before, sl(d2, 0, m - 1)]) + d2)
    return join_axis(s2 / scale_k, d2 * scale_k, dim)


def decompose(level_array, remaining):
    if remaining == 0:
        return level_array
    lifted = lift_axis(lift_axis(level_array, 0, "rows"), 1, "cols")
    height_here, width_here, band_count = lifted.shape
    blocks = lifted.reshape(height_here // 2, 2, width_here // 2, 2, band_count)
    inner_part = decompose(blocks[:, 0, :, 0], remaining - 1)
    return blocks.at[:, 0, :, 0].set(inner_part).reshape(height_here, width_here, band_count)


def on_device(radiance, decorrelation):
    mixed = jnp.einsum(
        "crw,bc->rwb",
        radiance,
        decorrelation,
        precision=lax.Precision.HIGHEST,
        preferred_element_type=jnp.float32,
    )
    return jnp.transpose(decompose(mixed, LEVELS), (2, 0, 1))


def solution(mesh):
    placed = (P(None, ("groups", "rows"), "cols"), P())
    return jax.shard_map(
        on_device,
        mesh=mesh,
        in_specs=placed,
        out_specs=P(None, ("groups", "rows"), "cols"),
        check_vma=False,
    )
```

```python
import jax
import jax.numpy as jnp
from jax import lax
from jax.sharding import PartitionSpec as P

LEVELS = 3


alpha_one = -1.586134342059924
beta_one = -0.052980118572961
alpha_two = 0.882911075530934
beta_two = 0.443506852043971
scale_k = 1.230174104914001


def shifted(x, axis, by):
    size = lax.axis_size(axis)
    pairs = [(i, i + by) for i in range(size) if 0 <= i + by < size]
    return lax.ppermute(x, axis, pairs)


def split_axis(x, dim):
    shape = x.shape[:dim] + (x.shape[dim] // 2, 2) + x.shape[dim + 1 :]
    paired = x.reshape(shape)
    return (
        lax.index_in_dim(paired, 0, dim + 1, keepdims=False),
        lax.index_in_dim(paired, 1, dim + 1, keepdims=False),
    )


def join_axis(even_part, odd_part, dim):
    stacked = jnp.stack([even_part, odd_part], axis=dim + 1)
    shape = even_part.shape[:dim] + (even_part.shape[dim] * 2,) + even_part.shape[dim + 1 :]
    return stacked.reshape(shape)


def lift_axis(x, dim, axis):
    a1, b1, a2, b2 = alpha_one, beta_one, alpha_two, beta_two
    even, odd = split_axis(x, dim)
    m = even.shape[dim]

    def sl(v, lo, hi):
        return lax.slice_in_dim(v, lo, hi, axis=dim)

    def cat(parts):
        return jnp.concatenate(parts, axis=dim)

    s_first, s_second, d_first = sl(even, 0, 1), sl(even, 1, 2), sl(odd, 0, 1)
    s_pen, s_last = sl(even, m - 2, m - 1), sl(even, m - 1, m)
    d_pen, d_last = sl(odd, m - 2, m - 1), sl(odd, m - 1, m)

    to_next = cat([d_last + a1 * s_last, s_last + b1 * (d_pen + a1 * (s_pen + s_last))])
    to_prev = cat([s_first, s_first + b1 * (d_first + a1 * (s_first + s_second))])
    from_prev = shifted(to_next, axis, 1)
    from_next = shifted(to_prev, axis, -1)
    a_in, b_in = sl(from_prev, 0, 1), sl(from_prev, 1, 2)
    s_in, c_in = sl(from_next, 0, 1), sl(from_next, 1, 2)

    at_first = lax.axis_index(axis) == 0
    at_last = lax.axis_index(axis) == lax.axis_size(axis) - 1

    s_after = jnp.where(at_last, s_last, s_in)
    d1 = odd + a1 * (even + cat([sl(even, 1, m), s_after]))
    d1_before = jnp.where(at_first, sl(d1, 0, 1), a_in + a1 * s_first)
    s1 = even + b1 * (cat([d1_before, sl(d1, 0, m - 1)]) + d1)
    s1_after = jnp.where(at_last, sl(s1, m - 1, m), c_in + b1 * sl(d1, m - 1, m))
    d2 = d1 + a2 * (s1 + cat([sl(s1, 1, m), s1_after]))
    s1_before = b_in + b1 * d1_before
    d2_before = jnp.where(
        at_first, sl(d2, 0, 1), d1_before + a2 * (s1_before + sl(s1, 0, 1))
    )
    s2 = s1 + b2 * (cat([d2_before, sl(d2, 0, m - 1)]) + d2)
    return join_axis(s2 / scale_k, d2 * scale_k, dim)


def lift_local(x, dim):
    even, odd = split_axis(x, dim)
    m = even.shape[dim]

    def sl(v, lo, hi):
        return lax.slice_in_dim(v, lo, hi, axis=dim)

    def cat(parts):
        return jnp.concatenate(parts, axis=dim)

    for a, b in ((alpha_one, beta_one), (alpha_two, beta_two)):
        odd = odd + a * (even + cat([sl(even, 1, m), sl(even, m - 1, m)]))
        even = even + b * (cat([sl(odd, 0, 1), sl(odd, 0, m - 1)]) + odd)
    return join_axis(even / scale_k, odd * scale_k, dim)


def decompose(level_array, remaining):
    if remaining == 0:
        return level_array
    lifted = lift_local(lift_axis(level_array, 0, "rows"), 1)
    height_here, width_here, band_count = lifted.shape
    blocks = lifted.reshape(height_here // 2, 2, width_here // 2, 2, band_count)
    inner_part = decompose(blocks[:, 0, :, 0], remaining - 1)
    return blocks.at[:, 0, :, 0].set(inner_part).reshape(height_here, width_here, band_count)


HALO = 32


def with_column_halo(radiance):
    width = radiance.shape[2]
    right_of_left = shifted(radiance[:, :, :HALO], "cols", -1)
    left_of_right = shifted(radiance[:, :, width - HALO :], "cols", 1)
    on_left = lax.axis_index("cols") == 0
    return jnp.where(
        on_left,
        jnp.concatenate([radiance, right_of_left], axis=2),
        jnp.concatenate([left_of_right, radiance], axis=2),
    )


def on_device(radiance, decorrelation):
    width = radiance.shape[2]
    extended = with_column_halo(radiance)
    mixed = jnp.einsum(
        "crw,bc->rwb",
        extended,
        decorrelation,
        precision=lax.Precision.HIGHEST,
        preferred_element_type=jnp.float32,
    )
    coeffs = decompose(mixed, LEVELS)
    own = jnp.where(
        lax.axis_index("cols") == 0, coeffs[:, :width], coeffs[:, HALO : HALO + width]
    )
    return jnp.transpose(own, (2, 0, 1))


def solution(mesh):
    assert mesh.shape["cols"] == 2
    placed = (P(None, ("groups", "rows"), "cols"), P())
    return jax.shard_map(
        on_device,
        mesh=mesh,
        in_specs=placed,
        out_specs=P(None, ("groups", "rows"), "cols"),
        check_vma=False,
    )
```

```python
import functools

import jax
import jax.numpy as jnp
from jax import lax
from jax.experimental import pallas as pl
from jax.experimental.pallas import tpu as pltpu
from jax.sharding import PartitionSpec as P

LEVELS = 3
HALO = 32
EDGE = 4


alpha_one = -1.586134342059924
beta_one = -0.052980118572961
alpha_two = 0.882911075530934
beta_two = 0.443506852043971
scale_k = 1.230174104914001


def shifted(x, axis, by):
    size = lax.axis_size(axis)
    pairs = [(i, i + by) for i in range(size) if 0 <= i + by < size]
    return lax.ppermute(x, axis, pairs)


def level_kernel(x_ref, top_ref, bot_ref, *rest, stride):
    if stride == 1:
        out_ref, ll_ref, ext, half = rest
    else:
        prev_ref, out_ref, ll_ref, ext, half = rest
        out_ref[...] = prev_ref[...]
    rows, width, bands = x_ref.shape
    hr, hw = rows // 2, width // 2
    a1, b1, a2, b2 = alpha_one, beta_one, alpha_two, beta_two

    ext[0:EDGE] = top_ref[...]
    ext[EDGE : EDGE + rows] = x_ref[...]
    ext[EDGE + rows : 2 * EDGE + rows] = bot_ref[...]
    n = hr + EDGE
    pairs = ext[...].reshape(n, 2, width, bands)
    s = pairs[:, 0]
    d = pairs[:, 1]

    def nxt0(v):
        return jnp.concatenate([v[1:], v[-1:]], axis=0)

    def prv0(v):
        return jnp.concatenate([v[:1], v[:-1]], axis=0)

    d = d + a1 * (s + nxt0(s))
    s = s + b1 * (prv0(d) + d)
    d = d + a2 * (s + nxt0(s))
    s = s + b2 * (prv0(d) + d)
    lo = EDGE // 2
    half[0] = s[lo : lo + hr] / scale_k
    half[1] = d[lo : lo + hr] * scale_k

    col = lax.broadcasted_iota(jnp.int32, (hr, hw, bands), 1)

    def nxt1(v):
        return jnp.where(col == hw - 1, v, pltpu.roll(v, hw - 1, 1))

    def prv1(v):
        return jnp.where(col == 0, v, pltpu.roll(v, 1, 1))

    for pr in range(2):
        e = half[pr, :, pl.ds(0, hw, stride=2), :]
        o = half[pr, :, pl.ds(1, hw, stride=2), :]
        o = o + a1 * (e + nxt1(e))
        e = e + b1 * (prv1(o) + o)
        o = o + a2 * (e + nxt1(e))
        e = e + b2 * (prv1(o) + o)
        e = e / scale_k
        o = o * scale_k
        step = 2 * stride
        out_ref[pl.ds(pr * stride, hr, stride=step), pl.ds(0, hw, stride=step), :] = e
        out_ref[pl.ds(pr * stride, hr, stride=step), pl.ds(stride, hw, stride=step), :] = o
        if pr == 0:
            ll_ref[...] = e


def run_level(x, top, bot, out, stride):
    rows, width, bands = x.shape
    vm = pl.BlockSpec(memory_space=pltpu.VMEM)
    ins = [x, top, bot]
    aliases = {}
    if out is not None:
        ins.append(out)
        aliases = {3: 0}
        out_shape = out.shape
    else:
        out_shape = x.shape
    return pl.pallas_call(
        functools.partial(level_kernel, stride=stride),
        out_shape=(
            jax.ShapeDtypeStruct(out_shape, jnp.float32),
            jax.ShapeDtypeStruct((rows // 2, width // 2, bands), jnp.float32),
        ),
        in_specs=[vm] * len(ins),
        out_specs=(vm, vm),
        scratch_shapes=[
            pltpu.VMEM((rows + 2 * EDGE, width, bands), jnp.float32),
            pltpu.VMEM((2, rows // 2, width, bands), jnp.float32),
        ],
        input_output_aliases=aliases,
        compiler_params=pltpu.CompilerParams(vmem_limit_bytes=100 * 1024 * 1024),
    )(*ins)


def row_halos(x):
    rows = x.shape[0]
    from_prev = shifted(x[rows - EDGE :], "rows", 1)
    from_next = shifted(x[:EDGE], "rows", -1)
    at_first = lax.axis_index("rows") == 0
    at_last = lax.axis_index("rows") == lax.axis_size("rows") - 1
    top = jnp.where(at_first, x[EDGE:0:-1], from_prev)
    bot = jnp.where(at_last, x[rows - 2 : rows - 2 - EDGE : -1], from_next)
    return top, bot


LANES = 128


def band_blocks(decorrelation):
    bands = decorrelation.shape[0]
    count = -(-bands // LANES)
    padded = jnp.pad(decorrelation, ((0, count * LANES - bands), (0, 0)))
    return [padded[i * LANES : (i + 1) * LANES] for i in range(count)]


def mix(radiance, decorrelation):
    return jnp.einsum(
        "crw,bc->rwb",
        radiance,
        decorrelation,
        precision=lax.Precision.HIGHEST,
        preferred_element_type=jnp.float32,
    )


def on_device(radiance, decorrelation):
    width = radiance.shape[2]
    on_left = lax.axis_index("cols") == 0
    right_of_left = shifted(radiance[:, :, :HALO], "cols", -1)
    left_of_right = shifted(radiance[:, :, width - HALO :], "cols", 1)
    halo_in = jnp.where(on_left, right_of_left, left_of_right)
    parts = []
    for block in band_blocks(decorrelation):
        own = mix(radiance, block)
        halo = mix(halo_in, block)
        level = jnp.where(
            on_left,
            jnp.concatenate([own, halo], axis=1),
            jnp.concatenate([halo, own], axis=1),
        )
        out = None
        for lvl in range(LEVELS):
            top, bot = row_halos(level)
            out, level = run_level(level, top, bot, out, 2**lvl)
        coeffs = jnp.where(on_left, out[:, :width], out[:, HALO : HALO + width])
        parts.append(jnp.transpose(coeffs, (2, 0, 1)))
    return jnp.concatenate(parts, axis=0)[: radiance.shape[0]]


def solution(mesh):
    assert mesh.shape["cols"] == 2
    placed = (P(None, ("groups", "rows"), "cols"), P())
    return jax.shard_map(
        on_device,
        mesh=mesh,
        in_specs=placed,
        out_specs=P(None, ("groups", "rows"), "cols"),
        check_vma=False,
    )
```

```python
import functools

import jax
import jax.numpy as jnp
from jax import lax
from jax.experimental import pallas as pl
from jax.experimental.pallas import tpu as pltpu
from jax.sharding import PartitionSpec as P

LEVELS = 3
HALO = 32
EDGE = 4
LANES = 128


alpha_one = -1.586134342059924
beta_one = -0.052980118572961
alpha_two = 0.882911075530934
beta_two = 0.443506852043971
scale_k = 1.230174104914001


def shifted(x, axis, by):
    size = lax.axis_size(axis)
    pairs = [(i, i + by) for i in range(size) if 0 <= i + by < size]
    return lax.ppermute(x, axis, pairs)


def fill_rows(ext, flags, top, bot, rows):
    first = flags[1] == 1
    last = flags[2] == 1

    @pl.when(first)
    def _():
        ext[0:EDGE] = jnp.concatenate(
            [ext[2 * EDGE - k : 2 * EDGE - k + 1] for k in range(EDGE)], axis=0
        )

    @pl.when(jnp.logical_not(first))
    def _():
        ext[0:EDGE] = top

    base = EDGE + rows

    @pl.when(last)
    def _():
        ext[base : base + EDGE] = jnp.concatenate(
            [ext[base - 2 - k : base - 1 - k] for k in range(EDGE)], axis=0
        )

    @pl.when(jnp.logical_not(last))
    def _():
        ext[base : base + EDGE] = bot


def lift_block(ext, half, out_ref, ll_ref, rows, width, stride):
    hr, hw = rows // 2, width // 2
    a1, b1, a2, b2 = alpha_one, beta_one, alpha_two, beta_two
    n = hr + EDGE
    pairs = ext[...].reshape(n, 2, width, LANES)
    s = pairs[:, 0]
    d = pairs[:, 1]

    def nxt0(v):
        return jnp.concatenate([v[1:], v[-1:]], axis=0)

    def prv0(v):
        return jnp.concatenate([v[:1], v[:-1]], axis=0)

    d = d + a1 * (s + nxt0(s))
    s = s + b1 * (prv0(d) + d)
    d = d + a2 * (s + nxt0(s))
    s = s + b2 * (prv0(d) + d)
    lo = EDGE // 2
    half[0] = s[lo : lo + hr] / scale_k
    half[1] = d[lo : lo + hr] * scale_k

    col = lax.broadcasted_iota(jnp.int32, (hr, hw, LANES), 1)

    def nxt1(v):
        return jnp.where(col == hw - 1, v, pltpu.roll(v, hw - 1, 1))

    def prv1(v):
        return jnp.where(col == 0, v, pltpu.roll(v, 1, 1))

    step = 2 * stride
    for pr in range(2):
        e = half[pr, :, pl.ds(0, hw, stride=2), :]
        o = half[pr, :, pl.ds(1, hw, stride=2), :]
        o = o + a1 * (e + nxt1(e))
        e = e + b1 * (prv1(o) + o)
        o = o + a2 * (e + nxt1(e))
        e = e + b2 * (prv1(o) + o)
        e = e / scale_k
        o = o * scale_k
        out_ref[pl.ds(pr * stride, hr, stride=step), pl.ds(0, hw, stride=step), :] = e
        out_ref[pl.ds(pr * stride, hr, stride=step), pl.ds(stride, hw, stride=step), :] = o
        if pr == 0:
            ll_ref[...] = e


def first_kernel(flags, own, halo, top_own, top_halo, bot_own, bot_halo, out_ref, ll_ref, ext, half):
    rows, width = own.shape[0], own.shape[1] + halo.shape[1]
    h = halo.shape[1]
    on_left = flags[0] == 1

    @pl.when(on_left)
    def _():
        ext[EDGE : EDGE + rows, 0 : width - h] = own[...]
        ext[EDGE : EDGE + rows, width - h : width] = halo[...]

    @pl.when(jnp.logical_not(on_left))
    def _():
        ext[EDGE : EDGE + rows, 0:h] = halo[...]
        ext[EDGE : EDGE + rows, h:width] = own[...]

    top = jnp.where(on_left, jnp.concatenate([top_own[...], top_halo[...]], axis=1),
                    jnp.concatenate([top_halo[...], top_own[...]], axis=1))
    bot = jnp.where(on_left, jnp.concatenate([bot_own[...], bot_halo[...]], axis=1),
                    jnp.concatenate([bot_halo[...], bot_own[...]], axis=1))
    fill_rows(ext, flags, top, bot, rows)
    lift_block(ext, half, out_ref, ll_ref, rows, width, 1)


def next_kernel(flags, x_ref, top_ref, bot_ref, prev_ref, out_ref, ll_ref, ext, half, *, stride):
    rows, width = x_ref.shape[0], x_ref.shape[1]
    out_ref[...] = prev_ref[...]
    ext[EDGE : EDGE + rows] = x_ref[...]
    fill_rows(ext, flags, top_ref[...], bot_ref[...], rows)
    lift_block(ext, half, out_ref, ll_ref, rows, width, stride)


def spec(shape):
    return pl.BlockSpec(shape[:-1] + (LANES,), lambda h, f: (0,) * (len(shape) - 1) + (h,))


def level_call(kernel, flags, arrays, out_shape, rows, width, aliases):
    bands = arrays[0].shape[-1]
    ll_shape = (rows // 2, width // 2, bands)
    grid_spec = pltpu.PrefetchScalarGridSpec(
        num_scalar_prefetch=1,
        grid=(bands // LANES,),
        in_specs=[spec(a.shape) for a in arrays],
        out_specs=(spec(out_shape), spec(ll_shape)),
        scratch_shapes=[
            pltpu.VMEM((rows + 2 * EDGE, width, LANES), jnp.float32),
            pltpu.VMEM((2, rows // 2, width, LANES), jnp.float32),
        ],
    )
    return pl.pallas_call(
        kernel,
        grid_spec=grid_spec,
        out_shape=(
            jax.ShapeDtypeStruct(out_shape, jnp.float32),
            jax.ShapeDtypeStruct(ll_shape, jnp.float32),
        ),
        input_output_aliases=aliases,
        compiler_params=pltpu.CompilerParams(vmem_limit_bytes=100 * 1024 * 1024),
    )(flags, *arrays)


def edge_rows(x):
    rows = x.shape[0]
    return shifted(x[rows - EDGE :], "rows", 1), shifted(x[:EDGE], "rows", -1)


def on_device(radiance, decorrelation):
    bands, rows, width = radiance.shape
    padded_bands = -(-bands // LANES) * LANES
    on_left = lax.axis_index("cols") == 0
    flags = jnp.stack(
        [
            on_left,
            lax.axis_index("rows") == 0,
            lax.axis_index("rows") == lax.axis_size("rows") - 1,
        ]
    ).astype(jnp.int32)
    right_of_left = shifted(radiance[:, :, :HALO], "cols", -1)
    left_of_right = shifted(radiance[:, :, width - HALO :], "cols", 1)
    halo_in = jnp.where(on_left, right_of_left, left_of_right)
    weights = jnp.pad(decorrelation, ((0, padded_bands - bands), (0, 0)))

    def mix(x):
        return jnp.einsum("crw,bc->rwb", x, weights, precision=lax.Precision.HIGHEST,
                          preferred_element_type=jnp.float32)

    own = mix(radiance)
    halo = mix(halo_in)
    top_own, bot_own = edge_rows(own)
    top_halo, bot_halo = edge_rows(halo)
    ext_width = width + HALO
    out_shape = (rows, ext_width, padded_bands)
    out, level = level_call(
        first_kernel, flags, [own, halo, top_own, top_halo, bot_own, bot_halo],
        out_shape, rows, ext_width, {})
    for lvl in range(1, LEVELS):
        top, bot = edge_rows(level)
        r, w = level.shape[0], level.shape[1]
        out, level = level_call(
            functools.partial(next_kernel, stride=2**lvl), flags,
            [level, top, bot, out], out_shape, r, w, {4: 0})
    coeffs = jnp.where(on_left, out[:, :width], out[:, HALO : HALO + width])
    return jnp.transpose(coeffs, (2, 0, 1))[:bands]


def solution(mesh):
    assert mesh.shape["cols"] == 2
    placed = (P(None, ("groups", "rows"), "cols"), P())
    return jax.shard_map(
        on_device,
        mesh=mesh,
        in_specs=placed,
        out_specs=P(None, ("groups", "rows"), "cols"),
        check_vma=False,
    )
```

```python
import functools

import jax
import jax.numpy as jnp
from jax import lax
from jax.experimental import pallas as pl
from jax.experimental.pallas import tpu as pltpu
from jax.sharding import PartitionSpec as P

LEVELS = 3
HALO = 32
EDGE = 4
LANES = 128


alpha_one = -1.586134342059924
beta_one = -0.052980118572961
alpha_two = 0.882911075530934
beta_two = 0.443506852043971
scale_k = 1.230174104914001


def shifted(x, axis, by):
    size = lax.axis_size(axis)
    pairs = [(i, i + by) for i in range(size) if 0 <= i + by < size]
    return lax.ppermute(x, axis, pairs)


def partials(x, axis):
    a1, b1 = alpha_one, beta_one
    n = x.shape[axis]

    def row(i):
        return lax.slice_in_dim(x, i, i + 1, axis=axis)

    s_pen, d_pen, s_last, d_last = row(n - 4), row(n - 3), row(n - 2), row(n - 1)
    s0, d0, s1 = row(0), row(1), row(2)
    to_next = jnp.concatenate(
        [s_last + b1 * (d_pen + a1 * (s_pen + s_last)), d_last + a1 * s_last], axis=axis
    )
    to_prev = jnp.concatenate([s0, d0 + a1 * (s0 + s1)], axis=axis)
    return to_next, to_prev


def fill_rows(ext, flags, from_prev, from_next, rows):
    a1 = alpha_one
    first = flags[1] == 1
    last = flags[2] == 1
    base = EDGE + rows

    @pl.when(first)
    def _():
        ext[0:EDGE] = jnp.concatenate(
            [ext[2 * EDGE - k : 2 * EDGE - k + 1] for k in range(EDGE)], axis=0
        )

    @pl.when(jnp.logical_not(first))
    def _():
        b, a = from_prev[0:1], from_prev[1:2]
        ext[0:EDGE] = jnp.concatenate([jnp.zeros_like(b), -a1 * b, b, a - a1 * b], axis=0)

    @pl.when(last)
    def _():
        ext[base : base + EDGE] = jnp.concatenate(
            [ext[base - 2 - k : base - 1 - k] for k in range(EDGE)], axis=0
        )

    @pl.when(jnp.logical_not(last))
    def _():
        s, dp = from_next[0:1], from_next[1:2]
        z = jnp.zeros_like(s)
        ext[base : base + EDGE] = jnp.concatenate([s, dp - a1 * s, z, z], axis=0)


def lift_block(ext, half, out_ref, ll_ref, tn_ref, tp_ref, rows, width, stride):
    hr, hw = rows // 2, width // 2
    a1, b1, a2, b2 = alpha_one, beta_one, alpha_two, beta_two
    n = hr + EDGE
    pairs = ext[...].reshape(n, 2, width, LANES)
    s = pairs[:, 0]
    d = pairs[:, 1]

    def nxt0(v):
        return jnp.concatenate([v[1:], v[-1:]], axis=0)

    def prv0(v):
        return jnp.concatenate([v[:1], v[:-1]], axis=0)

    d = d + a1 * (s + nxt0(s))
    s = s + b1 * (prv0(d) + d)
    d = d + a2 * (s + nxt0(s))
    s = s + b2 * (prv0(d) + d)
    lo = EDGE // 2
    half[0] = s[lo : lo + hr] / scale_k
    half[1] = d[lo : lo + hr] * scale_k

    col = lax.broadcasted_iota(jnp.int32, (hr, hw, LANES), 1)

    def nxt1(v):
        return jnp.where(col == hw - 1, v, pltpu.roll(v, hw - 1, 1))

    def prv1(v):
        return jnp.where(col == 0, v, pltpu.roll(v, 1, 1))

    step = 2 * stride
    for pr in range(2):
        e = half[pr, :, pl.ds(0, hw, stride=2), :]
        o = half[pr, :, pl.ds(1, hw, stride=2), :]
        o = o + a1 * (e + nxt1(e))
        e = e + b1 * (prv1(o) + o)
        o = o + a2 * (e + nxt1(e))
        e = e + b2 * (prv1(o) + o)
        e = e / scale_k
        o = o * scale_k
        out_ref[pl.ds(pr * stride, hr, stride=step), pl.ds(0, hw, stride=step), :] = e
        out_ref[pl.ds(pr * stride, hr, stride=step), pl.ds(stride, hw, stride=step), :] = o
        if pr == 0:
            ll_ref[...] = e
            to_next, to_prev = partials(e, 0)
            tn_ref[...] = to_next
            tp_ref[...] = to_prev


def first_kernel(flags, own, halo, prev_own, prev_halo, next_own, next_halo,
                 out_ref, ll_ref, tn_ref, tp_ref, ext, half):
    rows, h = own.shape[0], halo.shape[1]
    width = own.shape[1] + h
    on_left = flags[0] == 1

    @pl.when(on_left)
    def _():
        ext[EDGE : EDGE + rows, 0 : width - h] = own[...]
        ext[EDGE : EDGE + rows, width - h : width] = halo[...]

    @pl.when(jnp.logical_not(on_left))
    def _():
        ext[EDGE : EDGE + rows, 0:h] = halo[...]
        ext[EDGE : EDGE + rows, h:width] = own[...]

    def joined(o, hh):
        return jnp.where(on_left, jnp.concatenate([o[...], hh[...]], axis=1),
                         jnp.concatenate([hh[...], o[...]], axis=1))

    fill_rows(ext, flags, joined(prev_own, prev_halo), joined(next_own, next_halo), rows)
    lift_block(ext, half, out_ref, ll_ref, tn_ref, tp_ref, rows, width, 1)


def next_kernel(flags, x_ref, from_prev, from_next, prev_out,
                out_ref, ll_ref, tn_ref, tp_ref, ext, half, *, stride):
    rows, width = x_ref.shape[0], x_ref.shape[1]
    out_ref[...] = prev_out[...]
    ext[EDGE : EDGE + rows] = x_ref[...]
    fill_rows(ext, flags, from_prev[...], from_next[...], rows)
    lift_block(ext, half, out_ref, ll_ref, tn_ref, tp_ref, rows, width, stride)


def spec(shape):
    return pl.BlockSpec(shape[:-1] + (LANES,), lambda h, f: (0,) * (len(shape) - 1) + (h,))


def level_call(kernel, flags, arrays, out_shape, rows, width, aliases):
    bands = arrays[0].shape[-1]
    ll_shape = (rows // 2, width // 2, bands)
    edge_shape = (2, width // 2, bands)
    outs = (out_shape, ll_shape, edge_shape, edge_shape)
    grid_spec = pltpu.PrefetchScalarGridSpec(
        num_scalar_prefetch=1,
        grid=(bands // LANES,),
        in_specs=[spec(a.shape) for a in arrays],
        out_specs=tuple(spec(o) for o in outs),
        scratch_shapes=[
            pltpu.VMEM((rows + 2 * EDGE, width, LANES), jnp.float32),
            pltpu.VMEM((2, rows // 2, width, LANES), jnp.float32),
        ],
    )
    return pl.pallas_call(
        kernel,
        grid_spec=grid_spec,
        out_shape=tuple(jax.ShapeDtypeStruct(o, jnp.float32) for o in outs),
        input_output_aliases=aliases,
        compiler_params=pltpu.CompilerParams(vmem_limit_bytes=100 * 1024 * 1024),
    )(flags, *arrays)


def to_core_mate(x):
    return lax.ppermute(x, "cols", [(0, 1), (1, 0)])


def diagonal(x, by):
    rows = lax.axis_size("rows")
    pairs = [
        (r * 2 + c, (r + by) * 2 + 1 - c)
        for r in range(rows)
        for c in range(2)
        if 0 <= r + by < rows
    ]
    return lax.ppermute(x, ("rows", "cols"), pairs)


def on_device(radiance, decorrelation):
    bands, rows, width = radiance.shape
    padded_bands = -(-bands // LANES) * LANES
    on_left = lax.axis_index("cols") == 0
    flags = jnp.stack(
        [
            on_left,
            lax.axis_index("rows") == 0,
            lax.axis_index("rows") == lax.axis_size("rows") - 1,
        ]
    ).astype(jnp.int32)
    weights = jnp.pad(decorrelation, ((0, padded_bands - bands), (0, 0)))

    def facing(x):
        return jnp.where(on_left, x[..., width - HALO :], x[..., :HALO])

    rad_next, rad_prev = partials(radiance, 1)
    p_own = shifted(rad_next, "rows", 1)
    n_own = shifted(rad_prev, "rows", -1)
    p_halo = diagonal(facing(rad_next), 1)
    n_halo = diagonal(facing(rad_prev), -1)

    def mix(x):
        return jnp.einsum("crw,bc->rwb", x, weights, precision=lax.Precision.HIGHEST,
                          preferred_element_type=jnp.float32)

    own = mix(radiance)
    halo = to_core_mate(jnp.where(on_left, own[:, width - HALO :], own[:, :HALO]))
    ext_width = width + HALO
    out_shape = (rows, ext_width, padded_bands)
    out, level, tn, tp = level_call(
        first_kernel, flags,
        [own, halo, mix(p_own), mix(p_halo), mix(n_own), mix(n_halo)],
        out_shape, rows, ext_width, {})
    for lvl in range(1, LEVELS):
        from_prev = shifted(tn, "rows", 1)
        from_next = shifted(tp, "rows", -1)
        r, w = level.shape[0], level.shape[1]
        out, level, tn, tp = level_call(
            functools.partial(next_kernel, stride=2**lvl), flags,
            [level, from_prev, from_next, out], out_shape, r, w, {4: 0})
    coeffs = jnp.where(on_left, out[:, :width], out[:, HALO : HALO + width])
    return jnp.transpose(coeffs, (2, 0, 1))[:bands]


def solution(mesh):
    assert mesh.shape["cols"] == 2
    placed = (P(None, ("groups", "rows"), "cols"), P())
    return jax.shard_map(
        on_device,
        mesh=mesh,
        in_specs=placed,
        out_specs=P(None, ("groups", "rows"), "cols"),
        check_vma=False,
    )
```

```python
import functools

import jax
import jax.numpy as jnp
from jax import lax
from jax.experimental import pallas as pl
from jax.experimental.pallas import tpu as pltpu
from jax.sharding import PartitionSpec as P

LEVELS = 3
HALO = 32
EDGE = 4
LANES = 128


alpha_one = -1.586134342059924
beta_one = -0.052980118572961
alpha_two = 0.882911075530934
beta_two = 0.443506852043971
scale_k = 1.230174104914001


def shifted(x, axis, by):
    size = lax.axis_size(axis)
    pairs = [(i, i + by) for i in range(size) if 0 <= i + by < size]
    return lax.ppermute(x, axis, pairs)


def partials(x, axis):
    a1, b1 = alpha_one, beta_one
    n = x.shape[axis]

    def row(i):
        return lax.slice_in_dim(x, i, i + 1, axis=axis)

    s_pen, d_pen, s_last, d_last = row(n - 4), row(n - 3), row(n - 2), row(n - 1)
    s0, d0, s1 = row(0), row(1), row(2)
    to_next = jnp.concatenate(
        [s_last + b1 * (d_pen + a1 * (s_pen + s_last)), d_last + a1 * s_last], axis=axis
    )
    to_prev = jnp.concatenate([s0, d0 + a1 * (s0 + s1)], axis=axis)
    return to_next, to_prev


def fill_rows(ext, flags, from_prev, from_next, rows):
    a1 = alpha_one
    first = flags[1] == 1
    last = flags[2] == 1
    base = EDGE + rows

    @pl.when(first)
    def _():
        ext[0:EDGE] = jnp.concatenate(
            [ext[2 * EDGE - k : 2 * EDGE - k + 1] for k in range(EDGE)], axis=0
        )

    @pl.when(jnp.logical_not(first))
    def _():
        b, a = from_prev[0:1], from_prev[1:2]
        ext[0:EDGE] = jnp.concatenate([jnp.zeros_like(b), -a1 * b, b, a - a1 * b], axis=0)

    @pl.when(last)
    def _():
        ext[base : base + EDGE] = jnp.concatenate(
            [ext[base - 2 - k : base - 1 - k] for k in range(EDGE)], axis=0
        )

    @pl.when(jnp.logical_not(last))
    def _():
        s, dp = from_next[0:1], from_next[1:2]
        z = jnp.zeros_like(s)
        ext[base : base + EDGE] = jnp.concatenate([s, dp - a1 * s, z, z], axis=0)


def lift_block(flags, ext, half, out_ref, ll_ref, tn_ref, tp_ref, rows, width, stride):
    hr, hw = rows // 2, width // 2
    a1, b1, a2, b2 = alpha_one, beta_one, alpha_two, beta_two
    n = hr + EDGE
    pairs = ext[...].reshape(n, 2, width, LANES)
    s = pairs[:, 0]
    d = pairs[:, 1]

    def nxt0(v):
        return jnp.concatenate([v[1:], v[-1:]], axis=0)

    def prv0(v):
        return jnp.concatenate([v[:1], v[:-1]], axis=0)

    d = d + a1 * (s + nxt0(s))
    s = s + b1 * (prv0(d) + d)
    d = d + a2 * (s + nxt0(s))
    s = s + b2 * (prv0(d) + d)
    lo = EDGE // 2
    half[0] = s[lo : lo + hr] / scale_k
    half[1] = d[lo : lo + hr] * scale_k

    col = lax.broadcasted_iota(jnp.int32, (hr, hw, LANES), 1)

    def nxt1(v):
        return jnp.where(col == hw - 1, v, pltpu.roll(v, hw - 1, 1))

    def prv1(v):
        return jnp.where(col == 0, v, pltpu.roll(v, 1, 1))

    step = 2 * stride
    own_hw = out_ref.shape[1] // step
    on_left = flags[0] == 1

    def store(pr, e, o):
        rows_at = pl.ds(pr * stride, hr, stride=step)

        @pl.when(on_left)
        def _():
            out_ref[rows_at, pl.ds(0, own_hw, stride=step), :] = e[:, :own_hw]
            out_ref[rows_at, pl.ds(stride, own_hw, stride=step), :] = o[:, :own_hw]

        @pl.when(jnp.logical_not(on_left))
        def _():
            out_ref[rows_at, pl.ds(0, own_hw, stride=step), :] = e[:, hw - own_hw :]
            out_ref[rows_at, pl.ds(stride, own_hw, stride=step), :] = o[:, hw - own_hw :]

    for pr in range(2):
        e = half[pr, :, pl.ds(0, hw, stride=2), :]
        o = half[pr, :, pl.ds(1, hw, stride=2), :]
        o = o + a1 * (e + nxt1(e))
        e = e + b1 * (prv1(o) + o)
        o = o + a2 * (e + nxt1(e))
        e = e + b2 * (prv1(o) + o)
        e = e / scale_k
        o = o * scale_k
        store(pr, e, o)
        if pr == 0:
            ll_ref[...] = e
            to_next, to_prev = partials(e, 0)
            tn_ref[...] = to_next
            tp_ref[...] = to_prev


def first_kernel(flags, own, halo, prev_own, prev_halo, next_own, next_halo,
                 out_ref, ll_ref, tn_ref, tp_ref, ext, half):
    rows, h = own.shape[0], halo.shape[1]
    width = own.shape[1] + h
    on_left = flags[0] == 1

    @pl.when(on_left)
    def _():
        ext[EDGE : EDGE + rows, 0 : width - h] = own[...]
        ext[EDGE : EDGE + rows, width - h : width] = halo[...]

    @pl.when(jnp.logical_not(on_left))
    def _():
        ext[EDGE : EDGE + rows, 0:h] = halo[...]
        ext[EDGE : EDGE + rows, h:width] = own[...]

    def joined(o, hh):
        return jnp.where(on_left, jnp.concatenate([o[...], hh[...]], axis=1),
                         jnp.concatenate([hh[...], o[...]], axis=1))

    fill_rows(ext, flags, joined(prev_own, prev_halo), joined(next_own, next_halo), rows)
    lift_block(flags, ext, half, out_ref, ll_ref, tn_ref, tp_ref, rows, width, 1)


def next_kernel(flags, x_ref, from_prev, from_next, prev_out,
                out_ref, ll_ref, tn_ref, tp_ref, ext, half, *, stride):
    rows, width = x_ref.shape[0], x_ref.shape[1]
    out_ref[...] = prev_out[...]
    ext[EDGE : EDGE + rows] = x_ref[...]
    fill_rows(ext, flags, from_prev[...], from_next[...], rows)
    lift_block(flags, ext, half, out_ref, ll_ref, tn_ref, tp_ref, rows, width, stride)


def spec(shape):
    return pl.BlockSpec(shape[:-1] + (LANES,), lambda h, f: (0,) * (len(shape) - 1) + (h,))


def level_call(kernel, flags, arrays, out_shape, rows, width, aliases):
    bands = arrays[0].shape[-1]
    ll_shape = (rows // 2, width // 2, bands)
    edge_shape = (2, width // 2, bands)
    outs = (out_shape, ll_shape, edge_shape, edge_shape)
    grid_spec = pltpu.PrefetchScalarGridSpec(
        num_scalar_prefetch=1,
        grid=(bands // LANES,),
        in_specs=[spec(a.shape) for a in arrays],
        out_specs=tuple(spec(o) for o in outs),
        scratch_shapes=[
            pltpu.VMEM((rows + 2 * EDGE, width, LANES), jnp.float32),
            pltpu.VMEM((2, rows // 2, width, LANES), jnp.float32),
        ],
    )
    return pl.pallas_call(
        kernel,
        grid_spec=grid_spec,
        out_shape=tuple(jax.ShapeDtypeStruct(o, jnp.float32) for o in outs),
        input_output_aliases=aliases,
        compiler_params=pltpu.CompilerParams(vmem_limit_bytes=100 * 1024 * 1024),
    )(flags, *arrays)


def to_core_mate(x):
    return lax.ppermute(x, "cols", [(0, 1), (1, 0)])


def diagonal(x, by):
    rows = lax.axis_size("rows")
    pairs = [
        (r * 2 + c, (r + by) * 2 + 1 - c)
        for r in range(rows)
        for c in range(2)
        if 0 <= r + by < rows
    ]
    return lax.ppermute(x, ("rows", "cols"), pairs)


def on_device(radiance, decorrelation):
    bands, rows, width = radiance.shape
    padded_bands = -(-bands // LANES) * LANES
    on_left = lax.axis_index("cols") == 0
    flags = jnp.stack(
        [
            on_left,
            lax.axis_index("rows") == 0,
            lax.axis_index("rows") == lax.axis_size("rows") - 1,
        ]
    ).astype(jnp.int32)
    weights = jnp.pad(decorrelation, ((0, padded_bands - bands), (0, 0)))

    def facing(x):
        return jnp.where(on_left, x[:, width - HALO :], x[:, :HALO])

    def mix(x):
        return jnp.einsum("crw,bc->rwb", x, weights, precision=lax.Precision.HIGHEST,
                          preferred_element_type=jnp.float32)

    rad_next, rad_prev = partials(radiance, 1)
    mixed_parts = mix(jnp.concatenate([rad_next, rad_prev], axis=1))
    mixed_next, mixed_prev = mixed_parts[:2], mixed_parts[2:]
    p_own = shifted(mixed_next, "rows", 1)
    n_own = shifted(mixed_prev, "rows", -1)
    p_halo = diagonal(facing(mixed_next), 1)
    n_halo = diagonal(facing(mixed_prev), -1)

    own = mix(radiance)
    halo = to_core_mate(facing(own))
    ext_width = width + HALO
    out_shape = (rows, width, padded_bands)
    out, level, tn, tp = level_call(
        first_kernel, flags,
        [own, halo, p_own, p_halo, n_own, n_halo],
        out_shape, rows, ext_width, {})
    for lvl in range(1, LEVELS):
        from_prev = shifted(tn, "rows", 1)
        from_next = shifted(tp, "rows", -1)
        r, w = level.shape[0], level.shape[1]
        out, level, tn, tp = level_call(
            functools.partial(next_kernel, stride=2**lvl), flags,
            [level, from_prev, from_next, out], out_shape, r, w, {4: 0})
    return jnp.transpose(out, (2, 0, 1))[:bands]


def solution(mesh):
    assert mesh.shape["cols"] == 2
    placed = (P(None, ("groups", "rows"), "cols"), P())
    return jax.shard_map(
        on_device,
        mesh=mesh,
        in_specs=placed,
        out_specs=P(None, ("groups", "rows"), "cols"),
        check_vma=False,
    )
```

```python
import functools

import jax
import jax.numpy as jnp
from jax import lax
from jax.experimental import pallas as pl
from jax.experimental.pallas import tpu as pltpu
from jax.sharding import PartitionSpec as P

LEVELS = 3
HALO = 32
EDGE = 4
LANES = 128


alpha_one = -1.586134342059924
beta_one = -0.052980118572961
alpha_two = 0.882911075530934
beta_two = 0.443506852043971
scale_k = 1.230174104914001


def shifted(x, axis, by):
    size = lax.axis_size(axis)
    pairs = [(i, i + by) for i in range(size) if 0 <= i + by < size]
    return lax.ppermute(x, axis, pairs)


def partials(x, axis):
    a1, b1 = alpha_one, beta_one
    n = x.shape[axis]

    def row(i):
        return lax.slice_in_dim(x, i, i + 1, axis=axis)

    s_pen, d_pen, s_last, d_last = row(n - 4), row(n - 3), row(n - 2), row(n - 1)
    s0, d0, s1 = row(0), row(1), row(2)
    to_next = jnp.concatenate(
        [s_last + b1 * (d_pen + a1 * (s_pen + s_last)), d_last + a1 * s_last], axis=axis
    )
    to_prev = jnp.concatenate([s0, d0 + a1 * (s0 + s1)], axis=axis)
    return to_next, to_prev


def fill_rows(ext, flags, from_prev, from_next, rows):
    a1 = alpha_one
    first = flags[1] == 1
    last = flags[2] == 1
    base = EDGE + rows

    @pl.when(first)
    def _():
        ext[0:EDGE] = jnp.concatenate(
            [ext[2 * EDGE - k : 2 * EDGE - k + 1] for k in range(EDGE)], axis=0
        )

    @pl.when(jnp.logical_not(first))
    def _():
        b, a = from_prev[0:1], from_prev[1:2]
        ext[0:EDGE] = jnp.concatenate([jnp.zeros_like(b), -a1 * b, b, a - a1 * b], axis=0)

    @pl.when(last)
    def _():
        ext[base : base + EDGE] = jnp.concatenate(
            [ext[base - 2 - k : base - 1 - k] for k in range(EDGE)], axis=0
        )

    @pl.when(jnp.logical_not(last))
    def _():
        s, dp = from_next[0:1], from_next[1:2]
        z = jnp.zeros_like(s)
        ext[base : base + EDGE] = jnp.concatenate([s, dp - a1 * s, z, z], axis=0)


def lift_block(flags, ext, half, out_ref, ll_ref, tn_ref, tp_ref, rows, width, stride):
    hr, hw = rows // 2, width // 2
    a1, b1, a2, b2 = alpha_one, beta_one, alpha_two, beta_two
    n = hr + EDGE
    pairs = ext[...].reshape(n, 2, width, LANES)
    s = pairs[:, 0]
    d = pairs[:, 1]

    def nxt0(v):
        return jnp.concatenate([v[1:], v[-1:]], axis=0)

    def prv0(v):
        return jnp.concatenate([v[:1], v[:-1]], axis=0)

    d = d + a1 * (s + nxt0(s))
    s = s + b1 * (prv0(d) + d)
    d = d + a2 * (s + nxt0(s))
    s = s + b2 * (prv0(d) + d)
    lo = EDGE // 2
    half[0] = s[lo : lo + hr] / scale_k
    half[1] = d[lo : lo + hr] * scale_k

    col = lax.broadcasted_iota(jnp.int32, (hr, hw, LANES), 1)

    def nxt1(v):
        return jnp.where(col == hw - 1, v, pltpu.roll(v, hw - 1, 1))

    def prv1(v):
        return jnp.where(col == 0, v, pltpu.roll(v, 1, 1))

    step = 2 * stride
    own_hw = out_ref.shape[1] // step
    on_left = flags[0] == 1

    def store(pr, e, o):
        rows_at = pl.ds(pr * stride, hr, stride=step)

        @pl.when(on_left)
        def _():
            out_ref[rows_at, pl.ds(0, own_hw, stride=step), :] = e[:, :own_hw]
            out_ref[rows_at, pl.ds(stride, own_hw, stride=step), :] = o[:, :own_hw]

        @pl.when(jnp.logical_not(on_left))
        def _():
            out_ref[rows_at, pl.ds(0, own_hw, stride=step), :] = e[:, hw - own_hw :]
            out_ref[rows_at, pl.ds(stride, own_hw, stride=step), :] = o[:, hw - own_hw :]

    for pr in range(2):
        e = half[pr, :, pl.ds(0, hw, stride=2), :]
        o = half[pr, :, pl.ds(1, hw, stride=2), :]
        o = o + a1 * (e + nxt1(e))
        e = e + b1 * (prv1(o) + o)
        o = o + a2 * (e + nxt1(e))
        e = e + b2 * (prv1(o) + o)
        e = e / scale_k
        o = o * scale_k
        store(pr, e, o)
        if pr == 0:
            ll_ref[...] = e
            to_next, to_prev = partials(e, 0)
            tn_ref[...] = to_next
            tp_ref[...] = to_prev


def first_kernel(flags, own, halo, prev_own, prev_halo, next_own, next_halo,
                 out_ref, ll_ref, tn_ref, tp_ref, ext, half):
    rows, h = own.shape[0], halo.shape[1]
    width = own.shape[1] + h
    on_left = flags[0] == 1

    @pl.when(on_left)
    def _():
        ext[EDGE : EDGE + rows, 0 : width - h] = own[...]
        ext[EDGE : EDGE + rows, width - h : width] = halo[...]

    @pl.when(jnp.logical_not(on_left))
    def _():
        ext[EDGE : EDGE + rows, 0:h] = halo[...]
        ext[EDGE : EDGE + rows, h:width] = own[...]

    def joined(o, hh):
        return jnp.where(on_left, jnp.concatenate([o[...], hh[...]], axis=1),
                         jnp.concatenate([hh[...], o[...]], axis=1))

    fill_rows(ext, flags, joined(prev_own, prev_halo), joined(next_own, next_halo), rows)
    lift_block(flags, ext, half, out_ref, ll_ref, tn_ref, tp_ref, rows, width, 1)


def next_kernel(flags, x_ref, from_prev, from_next, prev_out,
                out_ref, ll_ref, tn_ref, tp_ref, ext, half, *, stride):
    rows, width = x_ref.shape[0], x_ref.shape[1]
    out_ref[...] = prev_out[...]
    ext[EDGE : EDGE + rows] = x_ref[...]
    fill_rows(ext, flags, from_prev[...], from_next[...], rows)
    lift_block(flags, ext, half, out_ref, ll_ref, tn_ref, tp_ref, rows, width, stride)


def spec(shape):
    return pl.BlockSpec(shape[:-1] + (LANES,), lambda h, f: (0,) * (len(shape) - 1) + (h,))


def level_call(kernel, flags, arrays, out_shape, rows, width, aliases):
    bands = arrays[0].shape[-1]
    ll_shape = (rows // 2, width // 2, bands)
    edge_shape = (2, width // 2, bands)
    outs = (out_shape, ll_shape, edge_shape, edge_shape)
    grid_spec = pltpu.PrefetchScalarGridSpec(
        num_scalar_prefetch=1,
        grid=(bands // LANES,),
        in_specs=[spec(a.shape) for a in arrays],
        out_specs=tuple(spec(o) for o in outs),
        scratch_shapes=[
            pltpu.VMEM((rows + 2 * EDGE, width, LANES), jnp.float32),
            pltpu.VMEM((2, rows // 2, width, LANES), jnp.float32),
        ],
    )
    return pl.pallas_call(
        kernel,
        grid_spec=grid_spec,
        out_shape=tuple(jax.ShapeDtypeStruct(o, jnp.float32) for o in outs),
        input_output_aliases=aliases,
        compiler_params=pltpu.CompilerParams(vmem_limit_bytes=100 * 1024 * 1024),
    )(flags, *arrays)


def to_core_mate(x):
    return lax.ppermute(x, "cols", [(0, 1), (1, 0)])


def diagonal(x, by):
    rows = lax.axis_size("rows")
    pairs = [
        (r * 2 + c, (r + by) * 2 + 1 - c)
        for r in range(rows)
        for c in range(2)
        if 0 <= r + by < rows
    ]
    return lax.ppermute(x, ("rows", "cols"), pairs)


def on_device(radiance, decorrelation):
    bands, rows, width = radiance.shape
    padded_bands = -(-bands // LANES) * LANES
    on_left = lax.axis_index("cols") == 0
    flags = jnp.stack(
        [
            on_left,
            lax.axis_index("rows") == 0,
            lax.axis_index("rows") == lax.axis_size("rows") - 1,
        ]
    ).astype(jnp.int32)
    weights = jnp.pad(decorrelation, ((0, padded_bands - bands), (0, 0)))

    def facing(x):
        return jnp.where(on_left, x[..., width - HALO :], x[..., :HALO])

    def mix(x):
        return jnp.einsum("crw,bc->rwb", x, weights, precision=lax.Precision.HIGHEST,
                          preferred_element_type=jnp.float32)

    rad_next, rad_prev = partials(radiance, 1)
    got_own = jnp.concatenate(
        [shifted(rad_next, "rows", 1), shifted(rad_prev, "rows", -1)], axis=1
    )
    got_halo = jnp.concatenate(
        [diagonal(facing(rad_next), 1), diagonal(facing(rad_prev), -1)], axis=1
    )
    mixed_own = mix(got_own)
    mixed_halo = mix(got_halo)
    p_own, n_own = mixed_own[:2], mixed_own[2:]
    p_halo, n_halo = mixed_halo[:2], mixed_halo[2:]

    own = mix(radiance)
    halo = to_core_mate(jnp.where(on_left, own[:, width - HALO :], own[:, :HALO]))
    ext_width = width + HALO
    out_shape = (rows, width, padded_bands)
    out, level, tn, tp = level_call(
        first_kernel, flags,
        [own, halo, p_own, p_halo, n_own, n_halo],
        out_shape, rows, ext_width, {})
    for lvl in range(1, LEVELS):
        from_prev = shifted(tn, "rows", 1)
        from_next = shifted(tp, "rows", -1)
        r, w = level.shape[0], level.shape[1]
        out, level, tn, tp = level_call(
            functools.partial(next_kernel, stride=2**lvl), flags,
            [level, from_prev, from_next, out], out_shape, r, w, {4: 0})
    return jnp.transpose(out, (2, 0, 1))[:bands]


def solution(mesh):
    assert mesh.shape["cols"] == 2
    placed = (P(None, ("groups", "rows"), "cols"), P())
    return jax.shard_map(
        on_device,
        mesh=mesh,
        in_specs=placed,
        out_specs=P(None, ("groups", "rows"), "cols"),
        check_vma=False,
    )
```

```python
import functools

import jax
import jax.numpy as jnp
from jax import lax
from jax.experimental import pallas as pl
from jax.experimental.pallas import tpu as pltpu
from jax.sharding import PartitionSpec as P

LEVELS = 3
HALO = 32
EDGE = 4
LANES = 128


alpha_one = -1.586134342059924
beta_one = -0.052980118572961
alpha_two = 0.882911075530934
beta_two = 0.443506852043971
scale_k = 1.230174104914001


def shifted(x, axis, by):
    size = lax.axis_size(axis)
    pairs = [(i, i + by) for i in range(size) if 0 <= i + by < size]
    return lax.ppermute(x, axis, pairs)


def partials(x, axis):
    a1, b1 = alpha_one, beta_one
    n = x.shape[axis]

    def row(i):
        return lax.slice_in_dim(x, i, i + 1, axis=axis)

    s_pen, d_pen, s_last, d_last = row(n - 4), row(n - 3), row(n - 2), row(n - 1)
    s0, d0, s1 = row(0), row(1), row(2)
    to_next = jnp.concatenate(
        [s_last + b1 * (d_pen + a1 * (s_pen + s_last)), d_last + a1 * s_last], axis=axis
    )
    to_prev = jnp.concatenate([s0, d0 + a1 * (s0 + s1)], axis=axis)
    return to_next, to_prev


def fill_rows(ext, flags, from_prev, from_next, rows):
    a1 = alpha_one
    first = flags[1] == 1
    last = flags[2] == 1
    base = EDGE + rows

    @pl.when(first)
    def _():
        ext[0:EDGE] = jnp.concatenate(
            [ext[2 * EDGE - k : 2 * EDGE - k + 1] for k in range(EDGE)], axis=0
        )

    @pl.when(jnp.logical_not(first))
    def _():
        b, a = from_prev[0:1], from_prev[1:2]
        ext[0:EDGE] = jnp.concatenate([jnp.zeros_like(b), -a1 * b, b, a - a1 * b], axis=0)

    @pl.when(last)
    def _():
        ext[base : base + EDGE] = jnp.concatenate(
            [ext[base - 2 - k : base - 1 - k] for k in range(EDGE)], axis=0
        )

    @pl.when(jnp.logical_not(last))
    def _():
        s, dp = from_next[0:1], from_next[1:2]
        z = jnp.zeros_like(s)
        ext[base : base + EDGE] = jnp.concatenate([s, dp - a1 * s, z, z], axis=0)


def lift_block(flags, ext, half, out_ref, ll_ref, tn_ref, tp_ref, rows, width, stride):
    hr, hw = rows // 2, width // 2
    a1, b1, a2, b2 = alpha_one, beta_one, alpha_two, beta_two
    n = hr + EDGE
    pairs = ext[...].reshape(n, 2, width, LANES)
    s = pairs[:, 0]
    d = pairs[:, 1]

    def nxt0(v):
        return jnp.concatenate([v[1:], v[-1:]], axis=0)

    def prv0(v):
        return jnp.concatenate([v[:1], v[:-1]], axis=0)

    d = d + a1 * (s + nxt0(s))
    s = s + b1 * (prv0(d) + d)
    d = d + a2 * (s + nxt0(s))
    s = s + b2 * (prv0(d) + d)
    lo = EDGE // 2
    half[0] = s[lo : lo + hr] / scale_k
    half[1] = d[lo : lo + hr] * scale_k

    col = lax.broadcasted_iota(jnp.int32, (hr, hw, LANES), 1)

    def nxt1(v):
        return jnp.where(col == hw - 1, v, pltpu.roll(v, hw - 1, 1))

    def prv1(v):
        return jnp.where(col == 0, v, pltpu.roll(v, 1, 1))

    step = 2 * stride
    own_hw = out_ref.shape[1] // step
    on_left = flags[0] == 1

    def store(pr, e, o):
        rows_at = pl.ds(pr * stride, hr, stride=step)

        @pl.when(on_left)
        def _():
            out_ref[rows_at, pl.ds(0, own_hw, stride=step), :] = e[:, :own_hw]
            out_ref[rows_at, pl.ds(stride, own_hw, stride=step), :] = o[:, :own_hw]

        @pl.when(jnp.logical_not(on_left))
        def _():
            out_ref[rows_at, pl.ds(0, own_hw, stride=step), :] = e[:, hw - own_hw :]
            out_ref[rows_at, pl.ds(stride, own_hw, stride=step), :] = o[:, hw - own_hw :]

    for pr in range(2):
        e = half[pr, :, pl.ds(0, hw, stride=2), :]
        o = half[pr, :, pl.ds(1, hw, stride=2), :]
        o = o + a1 * (e + nxt1(e))
        e = e + b1 * (prv1(o) + o)
        o = o + a2 * (e + nxt1(e))
        e = e + b2 * (prv1(o) + o)
        e = e / scale_k
        o = o * scale_k
        store(pr, e, o)
        if pr == 0:
            ll_ref[...] = e
            to_next, to_prev = partials(e, 0)
            tn_ref[...] = to_next
            tp_ref[...] = to_prev


def first_kernel(flags, own, halo, prev_own, prev_halo, next_own, next_halo,
                 out_ref, ll_ref, tn_ref, tp_ref, ext, half):
    rows, h = own.shape[0], halo.shape[1]
    width = own.shape[1] + h
    on_left = flags[0] == 1

    @pl.when(on_left)
    def _():
        ext[EDGE : EDGE + rows, 0 : width - h] = own[...]
        ext[EDGE : EDGE + rows, width - h : width] = halo[...]

    @pl.when(jnp.logical_not(on_left))
    def _():
        ext[EDGE : EDGE + rows, 0:h] = halo[...]
        ext[EDGE : EDGE + rows, h:width] = own[...]

    def joined(o, hh):
        return jnp.where(on_left, jnp.concatenate([o[...], hh[...]], axis=1),
                         jnp.concatenate([hh[...], o[...]], axis=1))

    fill_rows(ext, flags, joined(prev_own, prev_halo), joined(next_own, next_halo), rows)
    lift_block(flags, ext, half, out_ref, ll_ref, tn_ref, tp_ref, rows, width, 1)


def next_kernel(flags, x_ref, from_prev, from_next, prev_out,
                out_ref, ll_ref, tn_ref, tp_ref, ext, half, *, stride):
    rows, width = x_ref.shape[0], x_ref.shape[1]
    out_ref[...] = prev_out[...]
    ext[EDGE : EDGE + rows] = x_ref[...]
    fill_rows(ext, flags, from_prev[...], from_next[...], rows)
    lift_block(flags, ext, half, out_ref, ll_ref, tn_ref, tp_ref, rows, width, stride)


def spec(shape):
    return pl.BlockSpec(shape[:-1] + (LANES,), lambda h, f: (0,) * (len(shape) - 1) + (h,))


def level_call(kernel, flags, arrays, out_shape, rows, width, aliases):
    bands = arrays[0].shape[-1]
    ll_shape = (rows // 2, width // 2, bands)
    edge_shape = (2, width // 2, bands)
    outs = (out_shape, ll_shape, edge_shape, edge_shape)
    grid_spec = pltpu.PrefetchScalarGridSpec(
        num_scalar_prefetch=1,
        grid=(bands // LANES,),
        in_specs=[spec(a.shape) for a in arrays],
        out_specs=tuple(spec(o) for o in outs),
        scratch_shapes=[
            pltpu.VMEM((rows + 2 * EDGE, width, LANES), jnp.float32),
            pltpu.VMEM((2, rows // 2, width, LANES), jnp.float32),
        ],
    )
    return pl.pallas_call(
        kernel,
        grid_spec=grid_spec,
        out_shape=tuple(jax.ShapeDtypeStruct(o, jnp.float32) for o in outs),
        input_output_aliases=aliases,
        compiler_params=pltpu.CompilerParams(vmem_limit_bytes=100 * 1024 * 1024),
    )(flags, *arrays)


def to_core_mate(x):
    return lax.ppermute(x, "cols", [(0, 1), (1, 0)])


def diagonal(x, by):
    rows = lax.axis_size("rows")
    pairs = [
        (r * 2 + c, (r + by) * 2 + 1 - c)
        for r in range(rows)
        for c in range(2)
        if 0 <= r + by < rows
    ]
    return lax.ppermute(x, ("rows", "cols"), pairs)


def on_device(radiance, decorrelation):
    bands, rows, width = radiance.shape
    padded_bands = -(-bands // LANES) * LANES
    on_left = lax.axis_index("cols") == 0
    flags = jnp.stack(
        [
            on_left,
            lax.axis_index("rows") == 0,
            lax.axis_index("rows") == lax.axis_size("rows") - 1,
        ]
    ).astype(jnp.int32)
    weights = jnp.pad(decorrelation, ((0, padded_bands - bands), (0, 0)))

    def facing(x):
        return jnp.where(on_left, x[:, width - HALO :], x[:, :HALO])

    def mix(x):
        return jnp.einsum("crw,bc->rwb", x, weights, precision=lax.Precision.HIGH,
                          preferred_element_type=jnp.float32)

    rad_next, rad_prev = partials(radiance, 1)
    mixed_parts = mix(jnp.concatenate([rad_next, rad_prev], axis=1))
    mixed_next, mixed_prev = mixed_parts[:2], mixed_parts[2:]
    p_own = shifted(mixed_next, "rows", 1)
    n_own = shifted(mixed_prev, "rows", -1)
    p_halo = diagonal(facing(mixed_next), 1)
    n_halo = diagonal(facing(mixed_prev), -1)

    own = mix(radiance)
    halo = to_core_mate(facing(own))
    ext_width = width + HALO
    out_shape = (rows, width, padded_bands)
    out, level, tn, tp = level_call(
        first_kernel, flags,
        [own, halo, p_own, p_halo, n_own, n_halo],
        out_shape, rows, ext_width, {})
    for lvl in range(1, LEVELS):
        from_prev = shifted(tn, "rows", 1)
        from_next = shifted(tp, "rows", -1)
        r, w = level.shape[0], level.shape[1]
        out, level, tn, tp = level_call(
            functools.partial(next_kernel, stride=2**lvl), flags,
            [level, from_prev, from_next, out], out_shape, r, w, {4: 0})
    return jnp.transpose(out, (2, 0, 1))[:bands]


def solution(mesh):
    assert mesh.shape["cols"] == 2
    placed = (P(None, ("groups", "rows"), "cols"), P())
    return jax.shard_map(
        on_device,
        mesh=mesh,
        in_specs=placed,
        out_specs=P(None, ("groups", "rows"), "cols"),
        check_vma=False,
    )
```

```python
import functools

import jax
import jax.numpy as jnp
from jax import lax
from jax.experimental import pallas as pl
from jax.experimental.pallas import tpu as pltpu
from jax.sharding import PartitionSpec as P

LEVELS = 3
HALO = 32
EDGE = 4
LANES = 128


alpha_one = -1.586134342059924
beta_one = -0.052980118572961
alpha_two = 0.882911075530934
beta_two = 0.443506852043971
scale_k = 1.230174104914001


def shifted(x, axis, by):
    size = lax.axis_size(axis)
    pairs = [(i, i + by) for i in range(size) if 0 <= i + by < size]
    return lax.ppermute(x, axis, pairs)


def partials(x, axis):
    a1, b1 = alpha_one, beta_one
    n = x.shape[axis]

    def row(i):
        return lax.slice_in_dim(x, i, i + 1, axis=axis)

    s_pen, d_pen, s_last, d_last = row(n - 4), row(n - 3), row(n - 2), row(n - 1)
    s0, d0, s1 = row(0), row(1), row(2)
    to_next = jnp.concatenate(
        [s_last + b1 * (d_pen + a1 * (s_pen + s_last)), d_last + a1 * s_last], axis=axis
    )
    to_prev = jnp.concatenate([s0, d0 + a1 * (s0 + s1)], axis=axis)
    return to_next, to_prev


def fill_rows(ext, flags, from_prev, from_next, rows):
    a1 = alpha_one
    first = flags[1] == 1
    last = flags[2] == 1
    base = EDGE + rows

    @pl.when(first)
    def _():
        ext[0:EDGE] = jnp.concatenate(
            [ext[2 * EDGE - k : 2 * EDGE - k + 1] for k in range(EDGE)], axis=0
        )

    @pl.when(jnp.logical_not(first))
    def _():
        b, a = from_prev[0:1], from_prev[1:2]
        ext[0:EDGE] = jnp.concatenate([jnp.zeros_like(b), -a1 * b, b, a - a1 * b], axis=0)

    @pl.when(last)
    def _():
        ext[base : base + EDGE] = jnp.concatenate(
            [ext[base - 2 - k : base - 1 - k] for k in range(EDGE)], axis=0
        )

    @pl.when(jnp.logical_not(last))
    def _():
        s, dp = from_next[0:1], from_next[1:2]
        z = jnp.zeros_like(s)
        ext[base : base + EDGE] = jnp.concatenate([s, dp - a1 * s, z, z], axis=0)


def lift_block(flags, ext, half, out_ref, ll_ref, tn_ref, tp_ref, rows, width, stride):
    hr, hw = rows // 2, width // 2
    a1, b1, a2, b2 = alpha_one, beta_one, alpha_two, beta_two
    n = hr + EDGE
    pairs = ext[...].reshape(n, 2, width, LANES)
    s = pairs[:, 0]
    d = pairs[:, 1]

    def nxt0(v):
        return jnp.concatenate([v[1:], v[-1:]], axis=0)

    def prv0(v):
        return jnp.concatenate([v[:1], v[:-1]], axis=0)

    d = d + a1 * (s + nxt0(s))
    s = s + b1 * (prv0(d) + d)
    d = d + a2 * (s + nxt0(s))
    s = s + b2 * (prv0(d) + d)
    lo = EDGE // 2
    half[0] = s[lo : lo + hr] / scale_k
    half[1] = d[lo : lo + hr] * scale_k

    col = lax.broadcasted_iota(jnp.int32, (hr, hw, LANES), 1)

    def nxt1(v):
        return jnp.where(col == hw - 1, v, pltpu.roll(v, hw - 1, 1))

    def prv1(v):
        return jnp.where(col == 0, v, pltpu.roll(v, 1, 1))

    step = 2 * stride
    own_hw = out_ref.shape[1] // step
    on_left = flags[0] == 1

    def store(pr, e, o):
        rows_at = pl.ds(pr * stride, hr, stride=step)

        @pl.when(on_left)
        def _():
            out_ref[rows_at, pl.ds(0, own_hw, stride=step), :] = e[:, :own_hw]
            out_ref[rows_at, pl.ds(stride, own_hw, stride=step), :] = o[:, :own_hw]

        @pl.when(jnp.logical_not(on_left))
        def _():
            out_ref[rows_at, pl.ds(0, own_hw, stride=step), :] = e[:, hw - own_hw :]
            out_ref[rows_at, pl.ds(stride, own_hw, stride=step), :] = o[:, hw - own_hw :]

    for pr in range(2):
        e = half[pr, :, pl.ds(0, hw, stride=2), :]
        o = half[pr, :, pl.ds(1, hw, stride=2), :]
        o = o + a1 * (e + nxt1(e))
        e = e + b1 * (prv1(o) + o)
        o = o + a2 * (e + nxt1(e))
        e = e + b2 * (prv1(o) + o)
        e = e / scale_k
        o = o * scale_k
        store(pr, e, o)
        if pr == 0:
            ll_ref[...] = e
            to_next, to_prev = partials(e, 0)
            tn_ref[...] = to_next
            tp_ref[...] = to_prev


def first_kernel(flags, own, halo, prev_own, prev_halo, next_own, next_halo,
                 out_ref, ll_ref, tn_ref, tp_ref, ext, half):
    rows, h = own.shape[0], halo.shape[1]
    width = own.shape[1] + h
    on_left = flags[0] == 1

    @pl.when(on_left)
    def _():
        ext[EDGE : EDGE + rows, 0 : width - h] = own[...]
        ext[EDGE : EDGE + rows, width - h : width] = halo[...]

    @pl.when(jnp.logical_not(on_left))
    def _():
        ext[EDGE : EDGE + rows, 0:h] = halo[...]
        ext[EDGE : EDGE + rows, h:width] = own[...]

    def joined(o, hh):
        return jnp.where(on_left, jnp.concatenate([o[...], hh[...]], axis=1),
                         jnp.concatenate([hh[...], o[...]], axis=1))

    fill_rows(ext, flags, joined(prev_own, prev_halo), joined(next_own, next_halo), rows)
    lift_block(flags, ext, half, out_ref, ll_ref, tn_ref, tp_ref, rows, width, 1)


def next_kernel(flags, x_ref, from_prev, from_next, prev_out,
                out_ref, ll_ref, tn_ref, tp_ref, ext, half, *, stride):
    rows, width = x_ref.shape[0], x_ref.shape[1]
    out_ref[...] = prev_out[...]
    ext[EDGE : EDGE + rows] = x_ref[...]
    fill_rows(ext, flags, from_prev[...], from_next[...], rows)
    lift_block(flags, ext, half, out_ref, ll_ref, tn_ref, tp_ref, rows, width, stride)


def last_kernel(flags, x_ref, from_prev, from_next, prev_out,
                final_ref, ext, half, full, ll, tn, tp, *, stride):
    rows, width = x_ref.shape[0], x_ref.shape[1]
    full[...] = prev_out[...]
    ext[EDGE : EDGE + rows] = x_ref[...]
    fill_rows(ext, flags, from_prev[...], from_next[...], rows)
    lift_block(flags, ext, half, full, ll, tn, tp, rows, width, stride)
    for r in range(full.shape[0]):
        final_ref[:, r, :] = full[r].T


def spec(shape):
    return pl.BlockSpec(shape[:-1] + (LANES,), lambda h, f: (0,) * (len(shape) - 1) + (h,))


def level_call(kernel, flags, arrays, out_shape, rows, width, aliases):
    bands = arrays[0].shape[-1]
    ll_shape = (rows // 2, width // 2, bands)
    edge_shape = (2, width // 2, bands)
    outs = (out_shape, ll_shape, edge_shape, edge_shape)
    grid_spec = pltpu.PrefetchScalarGridSpec(
        num_scalar_prefetch=1,
        grid=(bands // LANES,),
        in_specs=[spec(a.shape) for a in arrays],
        out_specs=tuple(spec(o) for o in outs),
        scratch_shapes=[
            pltpu.VMEM((rows + 2 * EDGE, width, LANES), jnp.float32),
            pltpu.VMEM((2, rows // 2, width, LANES), jnp.float32),
        ],
    )
    return pl.pallas_call(
        kernel,
        grid_spec=grid_spec,
        out_shape=tuple(jax.ShapeDtypeStruct(o, jnp.float32) for o in outs),
        input_output_aliases=aliases,
        compiler_params=pltpu.CompilerParams(vmem_limit_bytes=100 * 1024 * 1024),
    )(flags, *arrays)


def to_core_mate(x):
    return lax.ppermute(x, "cols", [(0, 1), (1, 0)])


def diagonal(x, by):
    rows = lax.axis_size("rows")
    pairs = [
        (r * 2 + c, (r + by) * 2 + 1 - c)
        for r in range(rows)
        for c in range(2)
        if 0 <= r + by < rows
    ]
    return lax.ppermute(x, ("rows", "cols"), pairs)


def on_device(radiance, decorrelation):
    bands, rows, width = radiance.shape
    padded_bands = -(-bands // LANES) * LANES
    on_left = lax.axis_index("cols") == 0
    flags = jnp.stack(
        [
            on_left,
            lax.axis_index("rows") == 0,
            lax.axis_index("rows") == lax.axis_size("rows") - 1,
        ]
    ).astype(jnp.int32)
    weights = jnp.pad(decorrelation, ((0, padded_bands - bands), (0, 0)))

    def facing(x):
        return jnp.where(on_left, x[:, width - HALO :], x[:, :HALO])

    def mix(x):
        return jnp.einsum("crw,bc->rwb", x, weights, precision=lax.Precision.HIGHEST,
                          preferred_element_type=jnp.float32)

    rad_next, rad_prev = partials(radiance, 1)
    mixed_parts = mix(jnp.concatenate([rad_next, rad_prev], axis=1))
    mixed_next, mixed_prev = mixed_parts[:2], mixed_parts[2:]
    p_own = shifted(mixed_next, "rows", 1)
    n_own = shifted(mixed_prev, "rows", -1)
    p_halo = diagonal(facing(mixed_next), 1)
    n_halo = diagonal(facing(mixed_prev), -1)

    own = mix(radiance)
    halo = to_core_mate(facing(own))
    ext_width = width + HALO
    out_shape = (rows, width, padded_bands)
    out, level, tn, tp = level_call(
        first_kernel, flags,
        [own, halo, p_own, p_halo, n_own, n_halo],
        out_shape, rows, ext_width, {})
    for lvl in range(1, LEVELS - 1):
        from_prev = shifted(tn, "rows", 1)
        from_next = shifted(tp, "rows", -1)
        r, w = level.shape[0], level.shape[1]
        out, level, tn, tp = level_call(
            functools.partial(next_kernel, stride=2**lvl), flags,
            [level, from_prev, from_next, out], out_shape, r, w, {4: 0})
    from_prev = shifted(tn, "rows", 1)
    from_next = shifted(tp, "rows", -1)
    return last_call(flags, [level, from_prev, from_next, out], bands, 2 ** (LEVELS - 1))


def last_call(flags, arrays, bands, stride):
    level, out = arrays[0], arrays[3]
    rows, width = level.shape[0], level.shape[1]
    final_shape = (bands, out.shape[0], out.shape[1])
    grid_spec = pltpu.PrefetchScalarGridSpec(
        num_scalar_prefetch=1,
        grid=(out.shape[-1] // LANES,),
        in_specs=[spec(a.shape) for a in arrays],
        out_specs=pl.BlockSpec((LANES,) + final_shape[1:], lambda h, f: (h, 0, 0)),
        scratch_shapes=[
            pltpu.VMEM((rows + 2 * EDGE, width, LANES), jnp.float32),
            pltpu.VMEM((2, rows // 2, width, LANES), jnp.float32),
            pltpu.VMEM(out.shape[:-1] + (LANES,), jnp.float32),
            pltpu.VMEM((rows // 2, width // 2, LANES), jnp.float32),
            pltpu.VMEM((2, width // 2, LANES), jnp.float32),
            pltpu.VMEM((2, width // 2, LANES), jnp.float32),
        ],
    )
    return pl.pallas_call(
        functools.partial(last_kernel, stride=stride),
        grid_spec=grid_spec,
        out_shape=jax.ShapeDtypeStruct(final_shape, jnp.float32),
        compiler_params=pltpu.CompilerParams(vmem_limit_bytes=100 * 1024 * 1024),
    )(flags, *arrays)


def solution(mesh):
    assert mesh.shape["cols"] == 2
    placed = (P(None, ("groups", "rows"), "cols"), P())
    return jax.shard_map(
        on_device,
        mesh=mesh,
        in_specs=placed,
        out_specs=P(None, ("groups", "rows"), "cols"),
        check_vma=False,
    )
```

```python
import functools

import jax
import jax.numpy as jnp
from jax import lax
from jax.experimental import pallas as pl
from jax.experimental.pallas import tpu as pltpu
from jax.sharding import PartitionSpec as P

LEVELS = 3
HALO = 32
EDGE = 4
LANES = 128


alpha_one = -1.586134342059924
beta_one = -0.052980118572961
alpha_two = 0.882911075530934
beta_two = 0.443506852043971
scale_k = 1.230174104914001


def shifted(x, axis, by):
    size = lax.axis_size(axis)
    pairs = [(i, i + by) for i in range(size) if 0 <= i + by < size]
    return lax.ppermute(x, axis, pairs)


def partials(x, axis):
    a1, b1 = alpha_one, beta_one
    n = x.shape[axis]

    def row(i):
        return lax.slice_in_dim(x, i, i + 1, axis=axis)

    s_pen, d_pen, s_last, d_last = row(n - 4), row(n - 3), row(n - 2), row(n - 1)
    s0, d0, s1 = row(0), row(1), row(2)
    to_next = jnp.concatenate(
        [s_last + b1 * (d_pen + a1 * (s_pen + s_last)), d_last + a1 * s_last], axis=axis
    )
    to_prev = jnp.concatenate([s0, d0 + a1 * (s0 + s1)], axis=axis)
    return to_next, to_prev


def fill_rows(ext, flags, from_prev, from_next, rows):
    a1 = alpha_one
    first = flags[1] == 1
    last = flags[2] == 1
    base = EDGE + rows

    @pl.when(first)
    def _():
        ext[0:EDGE] = jnp.concatenate(
            [ext[2 * EDGE - k : 2 * EDGE - k + 1] for k in range(EDGE)], axis=0
        )

    @pl.when(jnp.logical_not(first))
    def _():
        b, a = from_prev[0:1], from_prev[1:2]
        ext[0:EDGE] = jnp.concatenate([jnp.zeros_like(b), -a1 * b, b, a - a1 * b], axis=0)

    @pl.when(last)
    def _():
        ext[base : base + EDGE] = jnp.concatenate(
            [ext[base - 2 - k : base - 1 - k] for k in range(EDGE)], axis=0
        )

    @pl.when(jnp.logical_not(last))
    def _():
        s, dp = from_next[0:1], from_next[1:2]
        z = jnp.zeros_like(s)
        ext[base : base + EDGE] = jnp.concatenate([s, dp - a1 * s, z, z], axis=0)


def lift_block(flags, ext, half, out_ref, ll_ref, tn_ref, tp_ref, rows, width, stride):
    hr, hw = rows // 2, width // 2
    a1, b1, a2, b2 = alpha_one, beta_one, alpha_two, beta_two
    n = hr + EDGE
    pairs = ext[...].reshape(n, 2, width, LANES)
    s = pairs[:, 0]
    d = pairs[:, 1]

    def nxt0(v):
        return jnp.concatenate([v[1:], v[-1:]], axis=0)

    def prv0(v):
        return jnp.concatenate([v[:1], v[:-1]], axis=0)

    d = d + a1 * (s + nxt0(s))
    s = s + b1 * (prv0(d) + d)
    d = d + a2 * (s + nxt0(s))
    s = s + b2 * (prv0(d) + d)
    lo = EDGE // 2
    half[0] = s[lo : lo + hr] / scale_k
    half[1] = d[lo : lo + hr] * scale_k

    col = lax.broadcasted_iota(jnp.int32, (hr, hw, LANES), 1)

    def nxt1(v):
        return jnp.where(col == hw - 1, v, pltpu.roll(v, hw - 1, 1))

    def prv1(v):
        return jnp.where(col == 0, v, pltpu.roll(v, 1, 1))

    step = 2 * stride
    own_hw = out_ref.shape[1] // step
    on_left = flags[0] == 1

    def store(pr, e, o):
        rows_at = pl.ds(pr * stride, hr, stride=step)

        @pl.when(on_left)
        def _():
            out_ref[rows_at, pl.ds(0, own_hw, stride=step), :] = e[:, :own_hw]
            out_ref[rows_at, pl.ds(stride, own_hw, stride=step), :] = o[:, :own_hw]

        @pl.when(jnp.logical_not(on_left))
        def _():
            out_ref[rows_at, pl.ds(0, own_hw, stride=step), :] = e[:, hw - own_hw :]
            out_ref[rows_at, pl.ds(stride, own_hw, stride=step), :] = o[:, hw - own_hw :]

    for pr in range(2):
        e = half[pr, :, pl.ds(0, hw, stride=2), :]
        o = half[pr, :, pl.ds(1, hw, stride=2), :]
        o = o + a1 * (e + nxt1(e))
        e = e + b1 * (prv1(o) + o)
        o = o + a2 * (e + nxt1(e))
        e = e + b2 * (prv1(o) + o)
        e = e / scale_k
        o = o * scale_k
        store(pr, e, o)
        if pr == 0:
            ll_ref[...] = e
            to_next, to_prev = partials(e, 0)
            tn_ref[...] = to_next
            tp_ref[...] = to_prev


def first_kernel(flags, own, halo, prev_own, prev_halo, next_own, next_halo,
                 out_ref, ll_ref, tn_ref, tp_ref, ext, half):
    rows, h = own.shape[0], halo.shape[1]
    width = own.shape[1] + h
    on_left = flags[0] == 1

    @pl.when(on_left)
    def _():
        ext[EDGE : EDGE + rows, 0 : width - h] = own[...]
        ext[EDGE : EDGE + rows, width - h : width] = halo[...]

    @pl.when(jnp.logical_not(on_left))
    def _():
        ext[EDGE : EDGE + rows, 0:h] = halo[...]
        ext[EDGE : EDGE + rows, h:width] = own[...]

    def joined(o, hh):
        return jnp.where(on_left, jnp.concatenate([o[...], hh[...]], axis=1),
                         jnp.concatenate([hh[...], o[...]], axis=1))

    fill_rows(ext, flags, joined(prev_own, prev_halo), joined(next_own, next_halo), rows)
    lift_block(flags, ext, half, out_ref, ll_ref, tn_ref, tp_ref, rows, width, 1)


def next_kernel(flags, x_ref, from_prev, from_next, prev_out,
                out_ref, ll_ref, tn_ref, tp_ref, ext, half, *, stride):
    rows, width = x_ref.shape[0], x_ref.shape[1]
    out_ref[...] = prev_out[...]
    ext[EDGE : EDGE + rows] = x_ref[...]
    fill_rows(ext, flags, from_prev[...], from_next[...], rows)
    lift_block(flags, ext, half, out_ref, ll_ref, tn_ref, tp_ref, rows, width, stride)


def last_kernel(flags, x_ref, from_prev, from_next, prev_out,
                final_ref, ext, half, full, ll, tn, tp, *, stride):
    rows, width = x_ref.shape[0], x_ref.shape[1]
    full[...] = prev_out[...]
    ext[EDGE : EDGE + rows] = x_ref[...]
    fill_rows(ext, flags, from_prev[...], from_next[...], rows)
    lift_block(flags, ext, half, full, ll, tn, tp, rows, width, stride)
    for r in range(full.shape[0]):
        final_ref[:, r, :] = full[r].T


def spec(shape):
    return pl.BlockSpec(shape[:-1] + (LANES,), lambda h, f: (0,) * (len(shape) - 1) + (h,))


def level_call(kernel, flags, arrays, out_shape, rows, width, aliases):
    bands = arrays[0].shape[-1]
    ll_shape = (rows // 2, width // 2, bands)
    edge_shape = (2, width // 2, bands)
    outs = (out_shape, ll_shape, edge_shape, edge_shape)
    grid_spec = pltpu.PrefetchScalarGridSpec(
        num_scalar_prefetch=1,
        grid=(bands // LANES,),
        in_specs=[spec(a.shape) for a in arrays],
        out_specs=tuple(spec(o) for o in outs),
        scratch_shapes=[
            pltpu.VMEM((rows + 2 * EDGE, width, LANES), jnp.float32),
            pltpu.VMEM((2, rows // 2, width, LANES), jnp.float32),
        ],
    )
    return pl.pallas_call(
        kernel,
        grid_spec=grid_spec,
        out_shape=tuple(jax.ShapeDtypeStruct(o, jnp.float32) for o in outs),
        input_output_aliases=aliases,
        compiler_params=pltpu.CompilerParams(vmem_limit_bytes=100 * 1024 * 1024),
    )(flags, *arrays)


def mix_kernel(w_ref, x_ref, o_ref):
    w = w_ref[...]
    for j in range(x_ref.shape[1]):
        y = jnp.dot(w, x_ref[:, j, :], precision=lax.Precision.HIGHEST,
                    preferred_element_type=jnp.float32)
        o_ref[j] = y.T


def mix_block(weights, x):
    c, rows, width = x.shape
    b = weights.shape[0]
    vm = pl.BlockSpec(memory_space=pltpu.VMEM)
    return pl.pallas_call(
        mix_kernel,
        out_shape=jax.ShapeDtypeStruct((rows, width, b), jnp.float32),
        in_specs=[vm, vm],
        out_specs=vm,
        cost_estimate=pl.CostEstimate(
            flops=12 * b * c * rows * width,
            transcendentals=0,
            bytes_accessed=4 * (c * rows * width + b * c + b * rows * width),
        ),
        compiler_params=pltpu.CompilerParams(vmem_limit_bytes=100 * 1024 * 1024),
    )(weights, x)


def to_core_mate(x):
    return lax.ppermute(x, "cols", [(0, 1), (1, 0)])


def diagonal(x, by):
    rows = lax.axis_size("rows")
    pairs = [
        (r * 2 + c, (r + by) * 2 + 1 - c)
        for r in range(rows)
        for c in range(2)
        if 0 <= r + by < rows
    ]
    return lax.ppermute(x, ("rows", "cols"), pairs)


def on_device(radiance, decorrelation):
    bands, rows, width = radiance.shape
    padded_bands = -(-bands // LANES) * LANES
    on_left = lax.axis_index("cols") == 0
    flags = jnp.stack(
        [
            on_left,
            lax.axis_index("rows") == 0,
            lax.axis_index("rows") == lax.axis_size("rows") - 1,
        ]
    ).astype(jnp.int32)
    weights = jnp.pad(decorrelation, ((0, padded_bands - bands), (0, 0)))

    def facing(x):
        return jnp.where(on_left, x[:, width - HALO :], x[:, :HALO])

    def mix(x):
        return jnp.einsum("crw,bc->rwb", x, weights, precision=lax.Precision.HIGHEST,
                          preferred_element_type=jnp.float32)

    rad_next, rad_prev = partials(radiance, 1)
    mixed_parts = mix(jnp.concatenate([rad_next, rad_prev], axis=1))
    mixed_next, mixed_prev = mixed_parts[:2], mixed_parts[2:]
    p_own = shifted(mixed_next, "rows", 1)
    n_own = shifted(mixed_prev, "rows", -1)
    p_halo = diagonal(facing(mixed_next), 1)
    n_halo = diagonal(facing(mixed_prev), -1)

    own = mix_block(weights, radiance)
    halo = to_core_mate(facing(own))
    ext_width = width + HALO
    out_shape = (rows, width, padded_bands)
    out, level, tn, tp = level_call(
        first_kernel, flags,
        [own, halo, p_own, p_halo, n_own, n_halo],
        out_shape, rows, ext_width, {})
    for lvl in range(1, LEVELS - 1):
        from_prev = shifted(tn, "rows", 1)
        from_next = shifted(tp, "rows", -1)
        r, w = level.shape[0], level.shape[1]
        out, level, tn, tp = level_call(
            functools.partial(next_kernel, stride=2**lvl), flags,
            [level, from_prev, from_next, out], out_shape, r, w, {4: 0})
    from_prev = shifted(tn, "rows", 1)
    from_next = shifted(tp, "rows", -1)
    return last_call(flags, [level, from_prev, from_next, out], bands, 2 ** (LEVELS - 1))


def last_call(flags, arrays, bands, stride):
    level, out = arrays[0], arrays[3]
    rows, width = level.shape[0], level.shape[1]
    final_shape = (bands, out.shape[0], out.shape[1])
    grid_spec = pltpu.PrefetchScalarGridSpec(
        num_scalar_prefetch=1,
        grid=(out.shape[-1] // LANES,),
        in_specs=[spec(a.shape) for a in arrays],
        out_specs=pl.BlockSpec((LANES,) + final_shape[1:], lambda h, f: (h, 0, 0)),
        scratch_shapes=[
            pltpu.VMEM((rows + 2 * EDGE, width, LANES), jnp.float32),
            pltpu.VMEM((2, rows // 2, width, LANES), jnp.float32),
            pltpu.VMEM(out.shape[:-1] + (LANES,), jnp.float32),
            pltpu.VMEM((rows // 2, width // 2, LANES), jnp.float32),
            pltpu.VMEM((2, width // 2, LANES), jnp.float32),
            pltpu.VMEM((2, width // 2, LANES), jnp.float32),
        ],
    )
    return pl.pallas_call(
        functools.partial(last_kernel, stride=stride),
        grid_spec=grid_spec,
        out_shape=jax.ShapeDtypeStruct(final_shape, jnp.float32),
        compiler_params=pltpu.CompilerParams(vmem_limit_bytes=100 * 1024 * 1024),
    )(flags, *arrays)


def solution(mesh):
    assert mesh.shape["cols"] == 2
    placed = (P(None, ("groups", "rows"), "cols"), P())
    return jax.shard_map(
        on_device,
        mesh=mesh,
        in_specs=placed,
        out_specs=P(None, ("groups", "rows"), "cols"),
        check_vma=False,
    )
```

```python
import functools

import numpy as np
import jax
import jax.numpy as jnp
from jax import lax
from jax.experimental import pallas as pl
from jax.experimental.pallas import tpu as pltpu
from jax.sharding import PartitionSpec as P

LEVELS = 3
HALO = 32
EDGE = 4
LANES = 128


alpha_one = -1.586134342059924
beta_one = -0.052980118572961
alpha_two = 0.882911075530934
beta_two = 0.443506852043971
scale_k = 1.230174104914001


def shifted(x, axis, by):
    size = lax.axis_size(axis)
    pairs = [(i, i + by) for i in range(size) if 0 <= i + by < size]
    return lax.ppermute(x, axis, pairs)


def partials(x, axis):
    a1, b1 = alpha_one, beta_one
    n = x.shape[axis]

    def row(i):
        return lax.slice_in_dim(x, i, i + 1, axis=axis)

    s_pen, d_pen, s_last, d_last = row(n - 4), row(n - 3), row(n - 2), row(n - 1)
    s0, d0, s1 = row(0), row(1), row(2)
    to_next = jnp.concatenate(
        [s_last + b1 * (d_pen + a1 * (s_pen + s_last)), d_last + a1 * s_last], axis=axis
    )
    to_prev = jnp.concatenate([s0, d0 + a1 * (s0 + s1)], axis=axis)
    return to_next, to_prev


def fill_rows(ext, flags, from_prev, from_next, rows):
    a1 = alpha_one
    first = flags[1] == 1
    last = flags[2] == 1
    base = EDGE + rows

    @pl.when(first)
    def _():
        ext[0:EDGE] = jnp.concatenate(
            [ext[2 * EDGE - k : 2 * EDGE - k + 1] for k in range(EDGE)], axis=0
        )

    @pl.when(jnp.logical_not(first))
    def _():
        b, a = from_prev[0:1], from_prev[1:2]
        ext[0:EDGE] = jnp.concatenate([jnp.zeros_like(b), -a1 * b, b, a - a1 * b], axis=0)

    @pl.when(last)
    def _():
        ext[base : base + EDGE] = jnp.concatenate(
            [ext[base - 2 - k : base - 1 - k] for k in range(EDGE)], axis=0
        )

    @pl.when(jnp.logical_not(last))
    def _():
        s, dp = from_next[0:1], from_next[1:2]
        z = jnp.zeros_like(s)
        ext[base : base + EDGE] = jnp.concatenate([s, dp - a1 * s, z, z], axis=0)


def lift_block(flags, ext, half, out_ref, ll_ref, tn_ref, tp_ref, rows, width, stride):
    hr, hw = rows // 2, width // 2
    a1, b1, a2, b2 = alpha_one, beta_one, alpha_two, beta_two
    n = hr + EDGE
    pairs = ext[...].reshape(n, 2, width, LANES)
    s = pairs[:, 0]
    d = pairs[:, 1]

    def nxt0(v):
        return jnp.concatenate([v[1:], v[-1:]], axis=0)

    def prv0(v):
        return jnp.concatenate([v[:1], v[:-1]], axis=0)

    d = d + a1 * (s + nxt0(s))
    s = s + b1 * (prv0(d) + d)
    d = d + a2 * (s + nxt0(s))
    s = s + b2 * (prv0(d) + d)
    lo = EDGE // 2
    half[0] = s[lo : lo + hr] / scale_k
    half[1] = d[lo : lo + hr] * scale_k

    col = lax.broadcasted_iota(jnp.int32, (hr, hw, LANES), 1)

    def nxt1(v):
        return jnp.where(col == hw - 1, v, pltpu.roll(v, hw - 1, 1))

    def prv1(v):
        return jnp.where(col == 0, v, pltpu.roll(v, 1, 1))

    step = 2 * stride
    own_hw = out_ref.shape[1] // step
    on_left = flags[0] == 1

    def store(pr, e, o):
        rows_at = pl.ds(pr * stride, hr, stride=step)

        @pl.when(on_left)
        def _():
            out_ref[rows_at, pl.ds(0, own_hw, stride=step), :] = e[:, :own_hw]
            out_ref[rows_at, pl.ds(stride, own_hw, stride=step), :] = o[:, :own_hw]

        @pl.when(jnp.logical_not(on_left))
        def _():
            out_ref[rows_at, pl.ds(0, own_hw, stride=step), :] = e[:, hw - own_hw :]
            out_ref[rows_at, pl.ds(stride, own_hw, stride=step), :] = o[:, hw - own_hw :]

    for pr in range(2):
        e = half[pr, :, pl.ds(0, hw, stride=2), :]
        o = half[pr, :, pl.ds(1, hw, stride=2), :]
        o = o + a1 * (e + nxt1(e))
        e = e + b1 * (prv1(o) + o)
        o = o + a2 * (e + nxt1(e))
        e = e + b2 * (prv1(o) + o)
        e = e / scale_k
        o = o * scale_k
        store(pr, e, o)
        if pr == 0:
            ll_ref[...] = e
            to_next, to_prev = partials(e, 0)
            tn_ref[...] = to_next
            tp_ref[...] = to_prev


def first_kernel(flags, own, halo, prev_own, prev_halo, next_own, next_halo,
                 out_ref, ll_ref, tn_ref, tp_ref, ext, half):
    rows, h = own.shape[0], halo.shape[1]
    width = own.shape[1] + h
    on_left = flags[0] == 1

    @pl.when(on_left)
    def _():
        ext[EDGE : EDGE + rows, 0 : width - h] = own[...]
        ext[EDGE : EDGE + rows, width - h : width] = halo[...]

    @pl.when(jnp.logical_not(on_left))
    def _():
        ext[EDGE : EDGE + rows, 0:h] = halo[...]
        ext[EDGE : EDGE + rows, h:width] = own[...]

    def joined(o, hh):
        return jnp.where(on_left, jnp.concatenate([o[...], hh[...]], axis=1),
                         jnp.concatenate([hh[...], o[...]], axis=1))

    fill_rows(ext, flags, joined(prev_own, prev_halo), joined(next_own, next_halo), rows)
    lift_block(flags, ext, half, out_ref, ll_ref, tn_ref, tp_ref, rows, width, 1)


def next_kernel(flags, x_ref, from_prev, from_next, prev_out,
                out_ref, ll_ref, tn_ref, tp_ref, ext, half, *, stride):
    rows, width = x_ref.shape[0], x_ref.shape[1]
    out_ref[...] = prev_out[...]
    ext[EDGE : EDGE + rows] = x_ref[...]
    fill_rows(ext, flags, from_prev[...], from_next[...], rows)
    lift_block(flags, ext, half, out_ref, ll_ref, tn_ref, tp_ref, rows, width, stride)


def last_kernel(flags, x_ref, from_prev, from_next, prev_out,
                final_ref, ext, half, full, ll, tn, tp, *, stride):
    rows, width = x_ref.shape[0], x_ref.shape[1]
    full[...] = prev_out[...]
    ext[EDGE : EDGE + rows] = x_ref[...]
    fill_rows(ext, flags, from_prev[...], from_next[...], rows)
    lift_block(flags, ext, half, full, ll, tn, tp, rows, width, stride)
    for r in range(full.shape[0]):
        final_ref[:, r, :] = full[r].T


def spec(shape):
    return pl.BlockSpec(shape[:-1] + (LANES,), lambda h, f: (0,) * (len(shape) - 1) + (h,))


def level_call(kernel, flags, arrays, out_shape, rows, width, aliases):
    bands = arrays[0].shape[-1]
    ll_shape = (rows // 2, width // 2, bands)
    edge_shape = (2, width // 2, bands)
    outs = (out_shape, ll_shape, edge_shape, edge_shape)
    grid_spec = pltpu.PrefetchScalarGridSpec(
        num_scalar_prefetch=1,
        grid=(bands // LANES,),
        in_specs=[spec(a.shape) for a in arrays],
        out_specs=tuple(spec(o) for o in outs),
        scratch_shapes=[
            pltpu.VMEM((rows + 2 * EDGE, width, LANES), jnp.float32),
            pltpu.VMEM((2, rows // 2, width, LANES), jnp.float32),
        ],
    )
    return pl.pallas_call(
        kernel,
        grid_spec=grid_spec,
        out_shape=tuple(jax.ShapeDtypeStruct(o, jnp.float32) for o in outs),
        input_output_aliases=aliases,
        compiler_params=pltpu.CompilerParams(vmem_limit_bytes=100 * 1024 * 1024),
    )(flags, *arrays)


def np_partials(x):
    a1, b1 = alpha_one, beta_one
    n = x.shape[0]
    s_pen, d_pen, s_last, d_last = x[n - 4], x[n - 3], x[n - 2], x[n - 1]
    to_next = np.stack([s_last + b1 * (d_pen + a1 * (s_pen + s_last)), d_last + a1 * s_last])
    to_prev = np.stack([x[0], x[1] + a1 * (x[0] + x[2])])
    return to_next, to_prev


def np_lift(v, axis):
    a1, b1, a2, b2 = alpha_one, beta_one, alpha_two, beta_two
    v = np.moveaxis(v, axis, 0)
    s, d = v[0::2].copy(), v[1::2].copy()

    def nxt(u):
        return np.concatenate([u[1:], u[-1:]])

    def prv(u):
        return np.concatenate([u[:1], u[:-1]])

    d = d + a1 * (s + nxt(s))
    s = s + b1 * (prv(d) + d)
    d = d + a2 * (s + nxt(s))
    s = s + b2 * (prv(d) + d)
    return np.moveaxis(s / scale_k, 0, axis), np.moveaxis(d * scale_k, 0, axis)


def np_ll(level, from_prev, from_next):
    a1 = alpha_one
    b, a = from_prev
    s, dp = from_next
    z = np.zeros_like(b)
    ext = np.concatenate([np.stack([z, -a1 * b, b, a - a1 * b]), level,
                          np.stack([s, dp - a1 * s, z, z])])
    rows_s, _ = np_lift(ext, 0)
    lo = EDGE // 2
    rows_s = rows_s[lo : lo + level.shape[0] // 2]
    ll, _ = np_lift(rows_s, 1)
    return ll


@functools.lru_cache(maxsize=None)
def next_level_maps(rows, width):
    zero_edge = np.zeros((2, width))
    own = np.zeros((rows, width, 4, width // 2))
    for r in range(rows):
        for w in range(width):
            unit = np.zeros((rows, width))
            unit[r, w] = 1.0
            ll = np_ll(unit, zero_edge, zero_edge)
            tn, tp = np_partials(ll)
            own[r, w] = np.concatenate([tn, tp])
    from_below = np.zeros((2, width, 2, width // 2))
    from_above = np.zeros((2, width, 2, width // 2))
    zero = np.zeros((rows, width))
    for p in range(2):
        for w in range(width):
            unit = np.zeros((2, width))
            unit[p, w] = 1.0
            from_below[p, w] = np_partials(np_ll(zero, zero_edge, unit))[0]
            from_above[p, w] = np_partials(np_ll(zero, unit, zero_edge))[1]
    return tuple(m.astype(np.float32) for m in (own, from_below, from_above))


def to_core_mate(x):
    return lax.ppermute(x, "cols", [(0, 1), (1, 0)])


def diagonal(x, by):
    rows = lax.axis_size("rows")
    pairs = [
        (r * 2 + c, (r + by) * 2 + 1 - c)
        for r in range(rows)
        for c in range(2)
        if 0 <= r + by < rows
    ]
    return lax.ppermute(x, ("rows", "cols"), pairs)


def on_device(radiance, decorrelation):
    bands, rows, width = radiance.shape
    padded_bands = -(-bands // LANES) * LANES
    on_left = lax.axis_index("cols") == 0
    flags = jnp.stack(
        [
            on_left,
            lax.axis_index("rows") == 0,
            lax.axis_index("rows") == lax.axis_size("rows") - 1,
        ]
    ).astype(jnp.int32)
    weights = jnp.pad(decorrelation, ((0, padded_bands - bands), (0, 0)))

    def facing(x):
        return jnp.where(on_left, x[:, width - HALO :], x[:, :HALO])

    def mix(x):
        return jnp.einsum("crw,bc->rwb", x, weights, precision=lax.Precision.HIGHEST,
                          preferred_element_type=jnp.float32)

    rad_next, rad_prev = partials(radiance, 1)
    mixed_parts = mix(jnp.concatenate([rad_next, rad_prev], axis=1))
    mixed_next, mixed_prev = mixed_parts[:2], mixed_parts[2:]
    p_own = shifted(mixed_next, "rows", 1)
    n_own = shifted(mixed_prev, "rows", -1)
    p_halo = diagonal(facing(mixed_next), 1)
    n_halo = diagonal(facing(mixed_prev), -1)

    own = mix(radiance)
    halo = to_core_mate(facing(own))
    ext_width = width + HALO
    out_shape = (rows, width, padded_bands)
    out, level, tn, tp = level_call(
        first_kernel, flags,
        [own, halo, p_own, p_halo, n_own, n_halo],
        out_shape, rows, ext_width, {})
    assert LEVELS == 3
    r, w = level.shape[0], level.shape[1]
    own_map, below_map, above_map = next_level_maps(r, w)

    def apply(x, m):
        return jnp.einsum("rwb,rwqv->qvb", x, m, precision=lax.Precision.HIGHEST,
                          preferred_element_type=jnp.float32)

    ahead = apply(level, own_map)
    send_next = jnp.concatenate([tn, ahead[:2]], axis=1)
    send_prev = jnp.concatenate([tp, ahead[2:]], axis=1)
    got_prev = shifted(send_next, "rows", 1)
    got_next = shifted(send_prev, "rows", -1)
    from_prev3 = got_prev[:, w:] + apply(tp, below_map)
    from_next3 = got_next[:, w:] + apply(tn, above_map)
    out, level, tn, tp = level_call(
        functools.partial(next_kernel, stride=2), flags,
        [level, got_prev[:, :w], got_next[:, :w], out], out_shape, r, w, {4: 0})
    return last_call(flags, [level, from_prev3, from_next3, out], bands, 4)


def last_call(flags, arrays, bands, stride):
    level, out = arrays[0], arrays[3]
    rows, width = level.shape[0], level.shape[1]
    final_shape = (bands, out.shape[0], out.shape[1])
    grid_spec = pltpu.PrefetchScalarGridSpec(
        num_scalar_prefetch=1,
        grid=(out.shape[-1] // LANES,),
        in_specs=[spec(a.shape) for a in arrays],
        out_specs=pl.BlockSpec((LANES,) + final_shape[1:], lambda h, f: (h, 0, 0)),
        scratch_shapes=[
            pltpu.VMEM((rows + 2 * EDGE, width, LANES), jnp.float32),
            pltpu.VMEM((2, rows // 2, width, LANES), jnp.float32),
            pltpu.VMEM(out.shape[:-1] + (LANES,), jnp.float32),
            pltpu.VMEM((rows // 2, width // 2, LANES), jnp.float32),
            pltpu.VMEM((2, width // 2, LANES), jnp.float32),
            pltpu.VMEM((2, width // 2, LANES), jnp.float32),
        ],
    )
    return pl.pallas_call(
        functools.partial(last_kernel, stride=stride),
        grid_spec=grid_spec,
        out_shape=jax.ShapeDtypeStruct(final_shape, jnp.float32),
        compiler_params=pltpu.CompilerParams(vmem_limit_bytes=100 * 1024 * 1024),
    )(flags, *arrays)


def solution(mesh):
    assert mesh.shape["cols"] == 2
    placed = (P(None, ("groups", "rows"), "cols"), P())
    return jax.shard_map(
        on_device,
        mesh=mesh,
        in_specs=placed,
        out_specs=P(None, ("groups", "rows"), "cols"),
        check_vma=False,
    )
```

```python
import functools

import numpy as np
import jax
import jax.numpy as jnp
from jax import lax
from jax.experimental import pallas as pl
from jax.experimental.pallas import tpu as pltpu
from jax.sharding import PartitionSpec as P

LEVELS = 3
HALO = 32
EDGE = 4
LANES = 128


alpha_one = -1.586134342059924
beta_one = -0.052980118572961
alpha_two = 0.882911075530934
beta_two = 0.443506852043971
scale_k = 1.230174104914001


def shifted(x, axis, by):
    size = lax.axis_size(axis)
    pairs = [(i, i + by) for i in range(size) if 0 <= i + by < size]
    return lax.ppermute(x, axis, pairs)


def partials(x, axis):
    a1, b1 = alpha_one, beta_one
    n = x.shape[axis]

    def row(i):
        return lax.slice_in_dim(x, i, i + 1, axis=axis)

    s_pen, d_pen, s_last, d_last = row(n - 4), row(n - 3), row(n - 2), row(n - 1)
    s0, d0, s1 = row(0), row(1), row(2)
    to_next = jnp.concatenate(
        [s_last + b1 * (d_pen + a1 * (s_pen + s_last)), d_last + a1 * s_last], axis=axis
    )
    to_prev = jnp.concatenate([s0, d0 + a1 * (s0 + s1)], axis=axis)
    return to_next, to_prev


def fill_rows(ext, flags, from_prev, from_next, rows):
    a1 = alpha_one
    first = flags[1] == 1
    last = flags[2] == 1
    base = EDGE + rows

    @pl.when(first)
    def _():
        ext[0:EDGE] = jnp.concatenate(
            [ext[2 * EDGE - k : 2 * EDGE - k + 1] for k in range(EDGE)], axis=0
        )

    @pl.when(jnp.logical_not(first))
    def _():
        b, a = from_prev[0:1], from_prev[1:2]
        ext[0:EDGE] = jnp.concatenate([jnp.zeros_like(b), -a1 * b, b, a - a1 * b], axis=0)

    @pl.when(last)
    def _():
        ext[base : base + EDGE] = jnp.concatenate(
            [ext[base - 2 - k : base - 1 - k] for k in range(EDGE)], axis=0
        )

    @pl.when(jnp.logical_not(last))
    def _():
        s, dp = from_next[0:1], from_next[1:2]
        z = jnp.zeros_like(s)
        ext[base : base + EDGE] = jnp.concatenate([s, dp - a1 * s, z, z], axis=0)


def lift_block(flags, ext, half, out_ref, ll_ref, tn_ref, tp_ref, rows, width, stride,
               ahead_map=None):
    hr, hw = rows // 2, width // 2
    a1, b1, a2, b2 = alpha_one, beta_one, alpha_two, beta_two
    n = hr + EDGE
    pairs = ext[...].reshape(n, 2, width, LANES)
    s = pairs[:, 0]
    d = pairs[:, 1]

    def nxt0(v):
        return jnp.concatenate([v[1:], v[-1:]], axis=0)

    def prv0(v):
        return jnp.concatenate([v[:1], v[:-1]], axis=0)

    d = d + a1 * (s + nxt0(s))
    s = s + b1 * (prv0(d) + d)
    d = d + a2 * (s + nxt0(s))
    s = s + b2 * (prv0(d) + d)
    lo = EDGE // 2
    half[0] = s[lo : lo + hr] / scale_k
    half[1] = d[lo : lo + hr] * scale_k

    col = lax.broadcasted_iota(jnp.int32, (hr, hw, LANES), 1)

    def nxt1(v):
        return jnp.where(col == hw - 1, v, pltpu.roll(v, hw - 1, 1))

    def prv1(v):
        return jnp.where(col == 0, v, pltpu.roll(v, 1, 1))

    step = 2 * stride
    own_hw = out_ref.shape[1] // step
    on_left = flags[0] == 1

    def store(pr, e, o):
        rows_at = pl.ds(pr * stride, hr, stride=step)

        @pl.when(on_left)
        def _():
            out_ref[rows_at, pl.ds(0, own_hw, stride=step), :] = e[:, :own_hw]
            out_ref[rows_at, pl.ds(stride, own_hw, stride=step), :] = o[:, :own_hw]

        @pl.when(jnp.logical_not(on_left))
        def _():
            out_ref[rows_at, pl.ds(0, own_hw, stride=step), :] = e[:, hw - own_hw :]
            out_ref[rows_at, pl.ds(stride, own_hw, stride=step), :] = o[:, hw - own_hw :]

    for pr in range(2):
        e = half[pr, :, pl.ds(0, hw, stride=2), :]
        o = half[pr, :, pl.ds(1, hw, stride=2), :]
        o = o + a1 * (e + nxt1(e))
        e = e + b1 * (prv1(o) + o)
        o = o + a2 * (e + nxt1(e))
        e = e + b2 * (prv1(o) + o)
        e = e / scale_k
        o = o * scale_k
        store(pr, e, o)
        if pr == 0:
            ll_ref[...] = e
            to_next, to_prev = partials(e, 0)
            if ahead_map is None:
                tn_ref[...] = to_next
                tp_ref[...] = to_prev
            else:
                quarter = hw // 2
                ahead = jnp.dot(ahead_map[...], e.reshape(hr * hw, LANES),
                                precision=lax.Precision.HIGHEST,
                                preferred_element_type=jnp.float32)
                ahead = ahead.reshape(4, quarter, LANES)
                tn_ref[:, :hw] = to_next
                tn_ref[:, hw:] = ahead[:2]
                tp_ref[:, :hw] = to_prev
                tp_ref[:, hw:] = ahead[2:]


def first_kernel(flags, own, halo, prev_own, prev_halo, next_own, next_halo, ahead_map,
                 out_ref, ll_ref, tn_ref, tp_ref, ext, half):
    rows, h = own.shape[0], halo.shape[1]
    width = own.shape[1] + h
    on_left = flags[0] == 1

    @pl.when(on_left)
    def _():
        ext[EDGE : EDGE + rows, 0 : width - h] = own[...]
        ext[EDGE : EDGE + rows, width - h : width] = halo[...]

    @pl.when(jnp.logical_not(on_left))
    def _():
        ext[EDGE : EDGE + rows, 0:h] = halo[...]
        ext[EDGE : EDGE + rows, h:width] = own[...]

    def joined(o, hh):
        return jnp.where(on_left, jnp.concatenate([o[...], hh[...]], axis=1),
                         jnp.concatenate([hh[...], o[...]], axis=1))

    fill_rows(ext, flags, joined(prev_own, prev_halo), joined(next_own, next_halo), rows)
    lift_block(flags, ext, half, out_ref, ll_ref, tn_ref, tp_ref, rows, width, 1, ahead_map)


def next_kernel(flags, x_ref, from_prev, from_next, prev_out,
                out_ref, ll_ref, tn_ref, tp_ref, ext, half, *, stride):
    rows, width = x_ref.shape[0], x_ref.shape[1]
    out_ref[...] = prev_out[...]
    ext[EDGE : EDGE + rows] = x_ref[...]
    fill_rows(ext, flags, from_prev[:, :width], from_next[:, :width], rows)
    lift_block(flags, ext, half, out_ref, ll_ref, tn_ref, tp_ref, rows, width, stride)


def last_kernel(flags, x_ref, got_prev, got_next, sent_next, sent_prev, below_map, above_map,
                prev_out, final_ref, ext, half, full, ll, tn, tp, *, stride):
    rows, width = x_ref.shape[0], x_ref.shape[1]
    wide = 2 * width

    def share(m, sent):
        part = jnp.dot(m[...], sent[:, :wide].reshape(2 * wide, LANES),
                       precision=lax.Precision.HIGHEST, preferred_element_type=jnp.float32)
        return part.reshape(2, width, LANES)

    full[...] = prev_out[...]
    ext[EDGE : EDGE + rows] = x_ref[...]
    from_prev = got_prev[:, wide:] + share(below_map, sent_prev)
    from_next = got_next[:, wide:] + share(above_map, sent_next)
    fill_rows(ext, flags, from_prev, from_next, rows)
    lift_block(flags, ext, half, full, ll, tn, tp, rows, width, stride)
    for r in range(full.shape[0]):
        final_ref[:, r, :] = full[r].T


def spec(shape):
    return pl.BlockSpec(shape[:-1] + (LANES,), lambda h, f: (0,) * (len(shape) - 1) + (h,))


def whole(a):
    return pl.BlockSpec(a.shape, lambda h, f: (0,) * a.ndim)


def level_call(kernel, flags, arrays, out_shape, rows, width, aliases, consts=(), ahead=False):
    bands = arrays[0].shape[-1]
    ll_shape = (rows // 2, width // 2, bands)
    edge_shape = (2, width // 2 + (width // 4 if ahead else 0), bands)
    outs = (out_shape, ll_shape, edge_shape, edge_shape)
    grid_spec = pltpu.PrefetchScalarGridSpec(
        num_scalar_prefetch=1,
        grid=(bands // LANES,),
        in_specs=[spec(a.shape) for a in arrays] + [whole(c) for c in consts],
        out_specs=tuple(spec(o) for o in outs),
        scratch_shapes=[
            pltpu.VMEM((rows + 2 * EDGE, width, LANES), jnp.float32),
            pltpu.VMEM((2, rows // 2, width, LANES), jnp.float32),
        ],
    )
    return pl.pallas_call(
        kernel,
        grid_spec=grid_spec,
        out_shape=tuple(jax.ShapeDtypeStruct(o, jnp.float32) for o in outs),
        input_output_aliases=aliases,
        compiler_params=pltpu.CompilerParams(vmem_limit_bytes=100 * 1024 * 1024),
    )(flags, *arrays, *consts)


def np_partials(x):
    a1, b1 = alpha_one, beta_one
    n = x.shape[0]
    s_pen, d_pen, s_last, d_last = x[n - 4], x[n - 3], x[n - 2], x[n - 1]
    to_next = np.stack([s_last + b1 * (d_pen + a1 * (s_pen + s_last)), d_last + a1 * s_last])
    to_prev = np.stack([x[0], x[1] + a1 * (x[0] + x[2])])
    return to_next, to_prev


def np_lift(v, axis):
    a1, b1, a2, b2 = alpha_one, beta_one, alpha_two, beta_two
    v = np.moveaxis(v, axis, 0)
    s, d = v[0::2].copy(), v[1::2].copy()

    def nxt(u):
        return np.concatenate([u[1:], u[-1:]])

    def prv(u):
        return np.concatenate([u[:1], u[:-1]])

    d = d + a1 * (s + nxt(s))
    s = s + b1 * (prv(d) + d)
    d = d + a2 * (s + nxt(s))
    s = s + b2 * (prv(d) + d)
    return np.moveaxis(s / scale_k, 0, axis), np.moveaxis(d * scale_k, 0, axis)


def np_ll(level, from_prev, from_next):
    a1 = alpha_one
    b, a = from_prev
    s, dp = from_next
    z = np.zeros_like(b)
    ext = np.concatenate([np.stack([z, -a1 * b, b, a - a1 * b]), level,
                          np.stack([s, dp - a1 * s, z, z])])
    rows_s, _ = np_lift(ext, 0)
    lo = EDGE // 2
    rows_s = rows_s[lo : lo + level.shape[0] // 2]
    ll, _ = np_lift(rows_s, 1)
    return ll


@functools.lru_cache(maxsize=None)
def next_level_maps(rows, width):
    zero_edge = np.zeros((2, width))
    own = np.zeros((rows, width, 4, width // 2))
    for r in range(rows):
        for w in range(width):
            unit = np.zeros((rows, width))
            unit[r, w] = 1.0
            ll = np_ll(unit, zero_edge, zero_edge)
            tn, tp = np_partials(ll)
            own[r, w] = np.concatenate([tn, tp])
    from_below = np.zeros((2, width, 2, width // 2))
    from_above = np.zeros((2, width, 2, width // 2))
    zero = np.zeros((rows, width))
    for p in range(2):
        for w in range(width):
            unit = np.zeros((2, width))
            unit[p, w] = 1.0
            from_below[p, w] = np_partials(np_ll(zero, zero_edge, unit))[0]
            from_above[p, w] = np_partials(np_ll(zero, unit, zero_edge))[1]
    return tuple(m.astype(np.float32) for m in (own, from_below, from_above))


def to_core_mate(x):
    return lax.ppermute(x, "cols", [(0, 1), (1, 0)])


def diagonal(x, by):
    rows = lax.axis_size("rows")
    pairs = [
        (r * 2 + c, (r + by) * 2 + 1 - c)
        for r in range(rows)
        for c in range(2)
        if 0 <= r + by < rows
    ]
    return lax.ppermute(x, ("rows", "cols"), pairs)


def on_device(radiance, decorrelation):
    bands, rows, width = radiance.shape
    padded_bands = -(-bands // LANES) * LANES
    on_left = lax.axis_index("cols") == 0
    flags = jnp.stack(
        [
            on_left,
            lax.axis_index("rows") == 0,
            lax.axis_index("rows") == lax.axis_size("rows") - 1,
        ]
    ).astype(jnp.int32)
    weights = jnp.pad(decorrelation, ((0, padded_bands - bands), (0, 0)))

    def facing(x):
        return jnp.where(on_left, x[:, width - HALO :], x[:, :HALO])

    def mix(x):
        return jnp.einsum("crw,bc->rwb", x, weights, precision=lax.Precision.HIGHEST,
                          preferred_element_type=jnp.float32)

    rad_next, rad_prev = partials(radiance, 1)
    mixed_parts = mix(jnp.concatenate([rad_next, rad_prev], axis=1))
    mixed_next, mixed_prev = mixed_parts[:2], mixed_parts[2:]
    p_own = shifted(mixed_next, "rows", 1)
    n_own = shifted(mixed_prev, "rows", -1)
    p_halo = diagonal(facing(mixed_next), 1)
    n_halo = diagonal(facing(mixed_prev), -1)

    own = mix(radiance)
    halo = to_core_mate(facing(own))
    ext_width = width + HALO
    out_shape = (rows, width, padded_bands)
    assert LEVELS == 3
    own_map, below_map, above_map = next_level_maps(rows // 2, ext_width // 2)
    ahead_map = jnp.asarray(own_map.reshape(-1, own_map.shape[2] * own_map.shape[3]).T)
    out, level, tn, tp = level_call(
        first_kernel, flags,
        [own, halo, p_own, p_halo, n_own, n_halo],
        out_shape, rows, ext_width, {}, consts=(ahead_map,), ahead=True)
    r, w = level.shape[0], level.shape[1]
    got_prev = shifted(tn, "rows", 1)
    got_next = shifted(tp, "rows", -1)
    sent_next, sent_prev = tn, tp
    out, level, tn, tp = level_call(
        functools.partial(next_kernel, stride=2), flags,
        [level, got_prev, got_next, out], out_shape, r, w, {4: 0})
    below = jnp.asarray(below_map.reshape(-1, below_map.shape[2] * below_map.shape[3]).T)
    above = jnp.asarray(above_map.reshape(-1, above_map.shape[2] * above_map.shape[3]).T)
    return last_call(flags, [level, got_prev, got_next, sent_next, sent_prev, out],
                     (below, above), bands, 4)


def last_call(flags, arrays, consts, bands, stride):
    level, out = arrays[0], arrays[-1]
    arrays = arrays[:-1]
    rows, width = level.shape[0], level.shape[1]
    final_shape = (bands, out.shape[0], out.shape[1])
    grid_spec = pltpu.PrefetchScalarGridSpec(
        num_scalar_prefetch=1,
        grid=(out.shape[-1] // LANES,),
        in_specs=[spec(a.shape) for a in arrays] + [whole(c) for c in consts] + [spec(out.shape)],
        out_specs=pl.BlockSpec((LANES,) + final_shape[1:], lambda h, f: (h, 0, 0)),
        scratch_shapes=[
            pltpu.VMEM((rows + 2 * EDGE, width, LANES), jnp.float32),
            pltpu.VMEM((2, rows // 2, width, LANES), jnp.float32),
            pltpu.VMEM(out.shape[:-1] + (LANES,), jnp.float32),
            pltpu.VMEM((rows // 2, width // 2, LANES), jnp.float32),
            pltpu.VMEM((2, width // 2, LANES), jnp.float32),
            pltpu.VMEM((2, width // 2, LANES), jnp.float32),
        ],
    )
    return pl.pallas_call(
        functools.partial(last_kernel, stride=stride),
        grid_spec=grid_spec,
        out_shape=jax.ShapeDtypeStruct(final_shape, jnp.float32),
        compiler_params=pltpu.CompilerParams(vmem_limit_bytes=100 * 1024 * 1024),
    )(flags, *arrays, *consts, out)


def solution(mesh):
    assert mesh.shape["cols"] == 2
    placed = (P(None, ("groups", "rows"), "cols"), P())
    return jax.shard_map(
        on_device,
        mesh=mesh,
        in_specs=placed,
        out_specs=P(None, ("groups", "rows"), "cols"),
        check_vma=False,
    )
```

```python
import functools

import numpy as np
import jax
import jax.numpy as jnp
from jax import lax
from jax.experimental import pallas as pl
from jax.experimental.pallas import tpu as pltpu
from jax.sharding import PartitionSpec as P

LEVELS = 3
HALO = 32
EDGE = 4
LANES = 128


alpha_one = -1.586134342059924
beta_one = -0.052980118572961
alpha_two = 0.882911075530934
beta_two = 0.443506852043971
scale_k = 1.230174104914001


def shifted(x, axis, by):
    size = lax.axis_size(axis)
    pairs = [(i, i + by) for i in range(size) if 0 <= i + by < size]
    return lax.ppermute(x, axis, pairs)


def partials(x, axis):
    a1, b1 = alpha_one, beta_one
    n = x.shape[axis]

    def row(i):
        return lax.slice_in_dim(x, i, i + 1, axis=axis)

    s_pen, d_pen, s_last, d_last = row(n - 4), row(n - 3), row(n - 2), row(n - 1)
    s0, d0, s1 = row(0), row(1), row(2)
    to_next = jnp.concatenate(
        [s_last + b1 * (d_pen + a1 * (s_pen + s_last)), d_last + a1 * s_last], axis=axis
    )
    to_prev = jnp.concatenate([s0, d0 + a1 * (s0 + s1)], axis=axis)
    return to_next, to_prev


def fill_rows(ext, flags, from_prev, from_next, rows):
    a1 = alpha_one
    first = flags[1] == 1
    last = flags[2] == 1
    base = EDGE + rows

    @pl.when(first)
    def _():
        ext[0:EDGE] = jnp.concatenate(
            [ext[2 * EDGE - k : 2 * EDGE - k + 1] for k in range(EDGE)], axis=0
        )

    @pl.when(jnp.logical_not(first))
    def _():
        b, a = from_prev[0:1], from_prev[1:2]
        ext[0:EDGE] = jnp.concatenate([jnp.zeros_like(b), -a1 * b, b, a - a1 * b], axis=0)

    @pl.when(last)
    def _():
        ext[base : base + EDGE] = jnp.concatenate(
            [ext[base - 2 - k : base - 1 - k] for k in range(EDGE)], axis=0
        )

    @pl.when(jnp.logical_not(last))
    def _():
        s, dp = from_next[0:1], from_next[1:2]
        z = jnp.zeros_like(s)
        ext[base : base + EDGE] = jnp.concatenate([s, dp - a1 * s, z, z], axis=0)


def lift_block(flags, ext, half, out_ref, ll_ref, tn_ref, tp_ref, rows, width, stride,
               ahead_map=None):
    hr, hw = rows // 2, width // 2
    a1, b1, a2, b2 = alpha_one, beta_one, alpha_two, beta_two
    n = hr + EDGE
    pairs = ext[...].reshape(n, 2, width, LANES)
    s = pairs[:, 0]
    d = pairs[:, 1]

    def nxt0(v):
        return jnp.concatenate([v[1:], v[-1:]], axis=0)

    def prv0(v):
        return jnp.concatenate([v[:1], v[:-1]], axis=0)

    d = d + a1 * (s + nxt0(s))
    s = s + b1 * (prv0(d) + d)
    d = d + a2 * (s + nxt0(s))
    s = s + b2 * (prv0(d) + d)
    lo = EDGE // 2
    half[0] = s[lo : lo + hr] / scale_k
    half[1] = d[lo : lo + hr] * scale_k

    col = lax.broadcasted_iota(jnp.int32, (hr, hw, LANES), 1)

    def nxt1(v):
        return jnp.where(col == hw - 1, v, pltpu.roll(v, hw - 1, 1))

    def prv1(v):
        return jnp.where(col == 0, v, pltpu.roll(v, 1, 1))

    step = 2 * stride
    own_hw = out_ref.shape[1] // step
    on_left = flags[0] == 1

    def store(pr, e, o):
        rows_at = pl.ds(pr * stride, hr, stride=step)

        @pl.when(on_left)
        def _():
            out_ref[rows_at, pl.ds(0, own_hw, stride=step), :] = e[:, :own_hw]
            out_ref[rows_at, pl.ds(stride, own_hw, stride=step), :] = o[:, :own_hw]

        @pl.when(jnp.logical_not(on_left))
        def _():
            out_ref[rows_at, pl.ds(0, own_hw, stride=step), :] = e[:, hw - own_hw :]
            out_ref[rows_at, pl.ds(stride, own_hw, stride=step), :] = o[:, hw - own_hw :]

    for pr in range(2):
        e = half[pr, :, pl.ds(0, hw, stride=2), :]
        o = half[pr, :, pl.ds(1, hw, stride=2), :]
        o = o + a1 * (e + nxt1(e))
        e = e + b1 * (prv1(o) + o)
        o = o + a2 * (e + nxt1(e))
        e = e + b2 * (prv1(o) + o)
        e = e / scale_k
        o = o * scale_k
        store(pr, e, o)
        if pr == 0:
            ll_ref[...] = e
            to_next, to_prev = partials(e, 0)
            if ahead_map is None:
                tn_ref[...] = to_next
                tp_ref[...] = to_prev
            else:
                quarter = hw // 2
                ahead = jnp.dot(ahead_map[...], e.reshape(hr * hw, LANES),
                                precision=lax.Precision.HIGHEST,
                                preferred_element_type=jnp.float32)
                ahead = ahead.reshape(4, quarter, LANES)
                tn_ref[:, :hw] = to_next
                tn_ref[:, hw:] = ahead[:2]
                tp_ref[:, :hw] = to_prev
                tp_ref[:, hw:] = ahead[2:]


def first_kernel(flags, own, halo, prev_own, prev_halo, next_own, next_halo, ahead_map,
                 out_ref, ll_ref, tn_ref, tp_ref, ext, half):
    rows, h = own.shape[0], halo.shape[1]
    width = own.shape[1] + h
    on_left = flags[0] == 1

    @pl.when(on_left)
    def _():
        ext[EDGE : EDGE + rows, 0 : width - h] = own[...]
        ext[EDGE : EDGE + rows, width - h : width] = halo[...]

    @pl.when(jnp.logical_not(on_left))
    def _():
        ext[EDGE : EDGE + rows, 0:h] = halo[...]
        ext[EDGE : EDGE + rows, h:width] = own[...]

    def joined(o, hh):
        return jnp.where(on_left, jnp.concatenate([o[...], hh[...]], axis=1),
                         jnp.concatenate([hh[...], o[...]], axis=1))

    fill_rows(ext, flags, joined(prev_own, prev_halo), joined(next_own, next_halo), rows)
    lift_block(flags, ext, half, out_ref, ll_ref, tn_ref, tp_ref, rows, width, 1, ahead_map)


def next_kernel(flags, x_ref, from_prev, from_next,
                out_ref, ll_ref, tn_ref, tp_ref, ext, half, *, stride):
    rows, width = x_ref.shape[0], x_ref.shape[1]
    ext[EDGE : EDGE + rows] = x_ref[...]
    fill_rows(ext, flags, from_prev[:, :width], from_next[:, :width], rows)
    lift_block(flags, ext, half, out_ref, ll_ref, tn_ref, tp_ref, rows, width, stride)


def last_kernel(flags, x_ref, got_prev, got_next, sent_next, sent_prev, below_map, above_map,
                prev_out, middle, final_ref, ext, half, full, ll, tn, tp, *, stride):
    rows, width = x_ref.shape[0], x_ref.shape[1]
    wide = 2 * width

    def share(m, sent):
        part = jnp.dot(m[...], sent[:, :wide].reshape(2 * wide, LANES),
                       precision=lax.Precision.HIGHEST, preferred_element_type=jnp.float32)
        return part.reshape(2, width, LANES)

    full[...] = prev_out[...]
    mr, mw = middle.shape[0], middle.shape[1]
    full[pl.ds(0, mr, stride=2), pl.ds(0, mw, stride=2), :] = middle[...]
    ext[EDGE : EDGE + rows] = x_ref[...]
    from_prev = got_prev[:, wide:] + share(below_map, sent_prev)
    from_next = got_next[:, wide:] + share(above_map, sent_next)
    fill_rows(ext, flags, from_prev, from_next, rows)
    lift_block(flags, ext, half, full, ll, tn, tp, rows, width, stride)
    for r in range(full.shape[0]):
        final_ref[:, r, :] = full[r].T


def spec(shape):
    return pl.BlockSpec(shape[:-1] + (LANES,), lambda h, f: (0,) * (len(shape) - 1) + (h,))


def whole(a):
    return pl.BlockSpec(a.shape, lambda h, f: (0,) * a.ndim)


def level_call(kernel, flags, arrays, out_shape, rows, width, aliases, consts=(), ahead=False):
    bands = arrays[0].shape[-1]
    ll_shape = (rows // 2, width // 2, bands)
    edge_shape = (2, width // 2 + (width // 4 if ahead else 0), bands)
    outs = (out_shape, ll_shape, edge_shape, edge_shape)
    grid_spec = pltpu.PrefetchScalarGridSpec(
        num_scalar_prefetch=1,
        grid=(bands // LANES,),
        in_specs=[spec(a.shape) for a in arrays] + [whole(c) for c in consts],
        out_specs=tuple(spec(o) for o in outs),
        scratch_shapes=[
            pltpu.VMEM((rows + 2 * EDGE, width, LANES), jnp.float32),
            pltpu.VMEM((2, rows // 2, width, LANES), jnp.float32),
        ],
    )
    return pl.pallas_call(
        kernel,
        grid_spec=grid_spec,
        out_shape=tuple(jax.ShapeDtypeStruct(o, jnp.float32) for o in outs),
        input_output_aliases=aliases,
        compiler_params=pltpu.CompilerParams(vmem_limit_bytes=100 * 1024 * 1024),
    )(flags, *arrays, *consts)


def np_partials(x):
    a1, b1 = alpha_one, beta_one
    n = x.shape[0]
    s_pen, d_pen, s_last, d_last = x[n - 4], x[n - 3], x[n - 2], x[n - 1]
    to_next = np.stack([s_last + b1 * (d_pen + a1 * (s_pen + s_last)), d_last + a1 * s_last])
    to_prev = np.stack([x[0], x[1] + a1 * (x[0] + x[2])])
    return to_next, to_prev


def np_lift(v, axis):
    a1, b1, a2, b2 = alpha_one, beta_one, alpha_two, beta_two
    v = np.moveaxis(v, axis, 0)
    s, d = v[0::2].copy(), v[1::2].copy()

    def nxt(u):
        return np.concatenate([u[1:], u[-1:]])

    def prv(u):
        return np.concatenate([u[:1], u[:-1]])

    d = d + a1 * (s + nxt(s))
    s = s + b1 * (prv(d) + d)
    d = d + a2 * (s + nxt(s))
    s = s + b2 * (prv(d) + d)
    return np.moveaxis(s / scale_k, 0, axis), np.moveaxis(d * scale_k, 0, axis)


def np_ll(level, from_prev, from_next):
    a1 = alpha_one
    b, a = from_prev
    s, dp = from_next
    z = np.zeros_like(b)
    ext = np.concatenate([np.stack([z, -a1 * b, b, a - a1 * b]), level,
                          np.stack([s, dp - a1 * s, z, z])])
    rows_s, _ = np_lift(ext, 0)
    lo = EDGE // 2
    rows_s = rows_s[lo : lo + level.shape[0] // 2]
    ll, _ = np_lift(rows_s, 1)
    return ll


@functools.lru_cache(maxsize=None)
def next_level_maps(rows, width):
    zero_edge = np.zeros((2, width))
    own = np.zeros((rows, width, 4, width // 2))
    for r in range(rows):
        for w in range(width):
            unit = np.zeros((rows, width))
            unit[r, w] = 1.0
            ll = np_ll(unit, zero_edge, zero_edge)
            tn, tp = np_partials(ll)
            own[r, w] = np.concatenate([tn, tp])
    from_below = np.zeros((2, width, 2, width // 2))
    from_above = np.zeros((2, width, 2, width // 2))
    zero = np.zeros((rows, width))
    for p in range(2):
        for w in range(width):
            unit = np.zeros((2, width))
            unit[p, w] = 1.0
            from_below[p, w] = np_partials(np_ll(zero, zero_edge, unit))[0]
            from_above[p, w] = np_partials(np_ll(zero, unit, zero_edge))[1]
    return tuple(m.astype(np.float32) for m in (own, from_below, from_above))


def to_core_mate(x):
    return lax.ppermute(x, "cols", [(0, 1), (1, 0)])


def diagonal(x, by):
    rows = lax.axis_size("rows")
    pairs = [
        (r * 2 + c, (r + by) * 2 + 1 - c)
        for r in range(rows)
        for c in range(2)
        if 0 <= r + by < rows
    ]
    return lax.ppermute(x, ("rows", "cols"), pairs)


def on_device(radiance, decorrelation):
    bands, rows, width = radiance.shape
    padded_bands = -(-bands // LANES) * LANES
    on_left = lax.axis_index("cols") == 0
    flags = jnp.stack(
        [
            on_left,
            lax.axis_index("rows") == 0,
            lax.axis_index("rows") == lax.axis_size("rows") - 1,
        ]
    ).astype(jnp.int32)
    weights = jnp.pad(decorrelation, ((0, padded_bands - bands), (0, 0)))

    def facing(x):
        return jnp.where(on_left, x[:, width - HALO :], x[:, :HALO])

    def mix(x):
        return jnp.einsum("crw,bc->rwb", x, weights, precision=lax.Precision.HIGHEST,
                          preferred_element_type=jnp.float32)

    rad_next, rad_prev = partials(radiance, 1)
    mixed_parts = mix(jnp.concatenate([rad_next, rad_prev], axis=1))
    mixed_next, mixed_prev = mixed_parts[:2], mixed_parts[2:]
    p_own = shifted(mixed_next, "rows", 1)
    n_own = shifted(mixed_prev, "rows", -1)
    p_halo = diagonal(facing(mixed_next), 1)
    n_halo = diagonal(facing(mixed_prev), -1)

    own = mix(radiance)
    halo = to_core_mate(facing(own))
    ext_width = width + HALO
    out_shape = (rows, width, padded_bands)
    assert LEVELS == 3
    own_map, below_map, above_map = next_level_maps(rows // 2, ext_width // 2)
    ahead_map = jnp.asarray(own_map.reshape(-1, own_map.shape[2] * own_map.shape[3]).T)
    out, level, tn, tp = level_call(
        first_kernel, flags,
        [own, halo, p_own, p_halo, n_own, n_halo],
        out_shape, rows, ext_width, {}, consts=(ahead_map,), ahead=True)
    r, w = level.shape[0], level.shape[1]
    got_prev = shifted(tn, "rows", 1)
    got_next = shifted(tp, "rows", -1)
    sent_next, sent_prev = tn, tp
    middle, level, tn, tp = level_call(
        functools.partial(next_kernel, stride=1), flags,
        [level, got_prev, got_next], (rows // 2, width // 2, padded_bands), r, w, {})
    below = jnp.asarray(below_map.reshape(-1, below_map.shape[2] * below_map.shape[3]).T)
    above = jnp.asarray(above_map.reshape(-1, above_map.shape[2] * above_map.shape[3]).T)
    return last_call(flags, [level, got_prev, got_next, sent_next, sent_prev, out, middle],
                     (below, above), bands, 4)


def last_call(flags, arrays, consts, bands, stride):
    level, out, middle = arrays[0], arrays[-2], arrays[-1]
    arrays = arrays[:-2]
    rows, width = level.shape[0], level.shape[1]
    final_shape = (bands, out.shape[0], out.shape[1])
    grid_spec = pltpu.PrefetchScalarGridSpec(
        num_scalar_prefetch=1,
        grid=(out.shape[-1] // LANES,),
        in_specs=[spec(a.shape) for a in arrays] + [whole(c) for c in consts]
        + [spec(out.shape), spec(middle.shape)],
        out_specs=pl.BlockSpec((LANES,) + final_shape[1:], lambda h, f: (h, 0, 0)),
        scratch_shapes=[
            pltpu.VMEM((rows + 2 * EDGE, width, LANES), jnp.float32),
            pltpu.VMEM((2, rows // 2, width, LANES), jnp.float32),
            pltpu.VMEM(out.shape[:-1] + (LANES,), jnp.float32),
            pltpu.VMEM((rows // 2, width // 2, LANES), jnp.float32),
            pltpu.VMEM((2, width // 2, LANES), jnp.float32),
            pltpu.VMEM((2, width // 2, LANES), jnp.float32),
        ],
    )
    return pl.pallas_call(
        functools.partial(last_kernel, stride=stride),
        grid_spec=grid_spec,
        out_shape=jax.ShapeDtypeStruct(final_shape, jnp.float32),
        compiler_params=pltpu.CompilerParams(vmem_limit_bytes=100 * 1024 * 1024),
    )(flags, *arrays, *consts, out, middle)


def solution(mesh):
    assert mesh.shape["cols"] == 2
    placed = (P(None, ("groups", "rows"), "cols"), P())
    return jax.shard_map(
        on_device,
        mesh=mesh,
        in_specs=placed,
        out_specs=P(None, ("groups", "rows"), "cols"),
        check_vma=False,
    )
```

```python
import functools

import numpy as np
import jax
import jax.numpy as jnp
from jax import lax
from jax.experimental import pallas as pl
from jax.experimental.pallas import tpu as pltpu
from jax.sharding import PartitionSpec as P

LEVELS = 3
HALO = 32
EDGE = 4
LANES = 128


alpha_one = -1.586134342059924
beta_one = -0.052980118572961
alpha_two = 0.882911075530934
beta_two = 0.443506852043971
scale_k = 1.230174104914001


def shifted(x, axis, by):
    size = lax.axis_size(axis)
    pairs = [(i, i + by) for i in range(size) if 0 <= i + by < size]
    return lax.ppermute(x, axis, pairs)


def partials(x, axis):
    a1, b1 = alpha_one, beta_one
    n = x.shape[axis]

    def row(i):
        return lax.slice_in_dim(x, i, i + 1, axis=axis)

    s_pen, d_pen, s_last, d_last = row(n - 4), row(n - 3), row(n - 2), row(n - 1)
    s0, d0, s1 = row(0), row(1), row(2)
    to_next = jnp.concatenate(
        [s_last + b1 * (d_pen + a1 * (s_pen + s_last)), d_last + a1 * s_last], axis=axis
    )
    to_prev = jnp.concatenate([s0, d0 + a1 * (s0 + s1)], axis=axis)
    return to_next, to_prev


def fill_rows(ext, flags, from_prev, from_next, rows):
    a1 = alpha_one
    first = flags[1] == 1
    last = flags[2] == 1
    base = EDGE + rows

    @pl.when(first)
    def _():
        ext[0:EDGE] = jnp.concatenate(
            [ext[2 * EDGE - k : 2 * EDGE - k + 1] for k in range(EDGE)], axis=0
        )

    @pl.when(jnp.logical_not(first))
    def _():
        b, a = from_prev[0:1], from_prev[1:2]
        ext[0:EDGE] = jnp.concatenate([jnp.zeros_like(b), -a1 * b, b, a - a1 * b], axis=0)

    @pl.when(last)
    def _():
        ext[base : base + EDGE] = jnp.concatenate(
            [ext[base - 2 - k : base - 1 - k] for k in range(EDGE)], axis=0
        )

    @pl.when(jnp.logical_not(last))
    def _():
        s, dp = from_next[0:1], from_next[1:2]
        z = jnp.zeros_like(s)
        ext[base : base + EDGE] = jnp.concatenate([s, dp - a1 * s, z, z], axis=0)


def lift_block(flags, ext, half, out_ref, ll_ref, tn_ref, tp_ref, rows, width, stride,
               ahead_map=None):
    hr, hw = rows // 2, width // 2
    a1, b1, a2, b2 = alpha_one, beta_one, alpha_two, beta_two
    n = hr + EDGE
    pairs = ext[...].reshape(n, 2, width, LANES)
    s = pairs[:, 0]
    d = pairs[:, 1]

    def nxt0(v):
        return jnp.concatenate([v[1:], v[-1:]], axis=0)

    def prv0(v):
        return jnp.concatenate([v[:1], v[:-1]], axis=0)

    d = d + a1 * (s + nxt0(s))
    s = s + b1 * (prv0(d) + d)
    d = d + a2 * (s + nxt0(s))
    s = s + b2 * (prv0(d) + d)
    lo = EDGE // 2
    half[0] = s[lo : lo + hr] / scale_k
    half[1] = d[lo : lo + hr] * scale_k

    col = lax.broadcasted_iota(jnp.int32, (hr, hw, LANES), 1)

    def nxt1(v):
        return jnp.where(col == hw - 1, v, pltpu.roll(v, hw - 1, 1))

    def prv1(v):
        return jnp.where(col == 0, v, pltpu.roll(v, 1, 1))

    step = 2 * stride
    own_hw = out_ref.shape[1] // step
    on_left = flags[0] == 1

    def store(pr, e, o):
        rows_at = pl.ds(pr * stride, hr, stride=step)

        @pl.when(on_left)
        def _():
            out_ref[rows_at, pl.ds(0, own_hw, stride=step), :] = e[:, :own_hw]
            out_ref[rows_at, pl.ds(stride, own_hw, stride=step), :] = o[:, :own_hw]

        @pl.when(jnp.logical_not(on_left))
        def _():
            out_ref[rows_at, pl.ds(0, own_hw, stride=step), :] = e[:, hw - own_hw :]
            out_ref[rows_at, pl.ds(stride, own_hw, stride=step), :] = o[:, hw - own_hw :]

    for pr in range(2):
        e = half[pr, :, pl.ds(0, hw, stride=2), :]
        o = half[pr, :, pl.ds(1, hw, stride=2), :]
        o = o + a1 * (e + nxt1(e))
        e = e + b1 * (prv1(o) + o)
        o = o + a2 * (e + nxt1(e))
        e = e + b2 * (prv1(o) + o)
        e = e / scale_k
        o = o * scale_k
        store(pr, e, o)
        if pr == 0:
            ll_ref[...] = e
            to_next, to_prev = partials(e, 0)
            if ahead_map is None:
                tn_ref[...] = to_next
                tp_ref[...] = to_prev
            else:
                quarter = hw // 2
                ahead = jnp.dot(ahead_map[...], e.reshape(hr * hw, LANES),
                                precision=lax.Precision.HIGHEST,
                                preferred_element_type=jnp.float32)
                ahead = ahead.reshape(4, quarter, LANES)
                tn_ref[:, :hw] = to_next
                tn_ref[:, hw:] = ahead[:2]
                tp_ref[:, :hw] = to_prev
                tp_ref[:, hw:] = ahead[2:]


def first_kernel(flags, own, halo, prev_own, prev_halo, next_own, next_halo, ahead_map,
                 out_ref, ll_ref, tn_ref, tp_ref, ext, half):
    rows, h = own.shape[0], halo.shape[1]
    width = own.shape[1] + h
    on_left = flags[0] == 1

    @pl.when(on_left)
    def _():
        ext[EDGE : EDGE + rows, 0 : width - h] = own[...]
        ext[EDGE : EDGE + rows, width - h : width] = halo[...]

    @pl.when(jnp.logical_not(on_left))
    def _():
        ext[EDGE : EDGE + rows, 0:h] = halo[...]
        ext[EDGE : EDGE + rows, h:width] = own[...]

    def joined(o, hh):
        return jnp.where(on_left, jnp.concatenate([o[...], hh[...]], axis=1),
                         jnp.concatenate([hh[...], o[...]], axis=1))

    fill_rows(ext, flags, joined(prev_own, prev_halo), joined(next_own, next_halo), rows)
    lift_block(flags, ext, half, out_ref, ll_ref, tn_ref, tp_ref, rows, width, 1, ahead_map)


def next_kernel(flags, x_ref, from_prev, from_next,
                out_ref, ll_ref, tn_ref, tp_ref, ext, half, *, stride):
    rows, width = x_ref.shape[0], x_ref.shape[1]
    ext[EDGE : EDGE + rows] = x_ref[...]
    fill_rows(ext, flags, from_prev[:, :width], from_next[:, :width], rows)
    lift_block(flags, ext, half, out_ref, ll_ref, tn_ref, tp_ref, rows, width, stride)


def last_kernel(flags, x_ref, got_prev, got_next, sent_next, sent_prev, below_map, above_map,
                prev_out, middle, final_ref, ext, half, full, ll, tn, tp, *, stride):
    rows, width = x_ref.shape[0], x_ref.shape[1]
    wide = 2 * width

    def share(m, sent):
        part = jnp.dot(m[...], sent[:, :wide].reshape(2 * wide, LANES),
                       precision=lax.Precision.HIGHEST, preferred_element_type=jnp.float32)
        return part.reshape(2, width, LANES)

    full[...] = prev_out[...]
    mr, mw = middle.shape[0], middle.shape[1]
    full[pl.ds(0, mr, stride=2), pl.ds(0, mw, stride=2), :] = middle[...]
    ext[EDGE : EDGE + rows] = x_ref[...]
    from_prev = got_prev[:, wide:] + share(below_map, sent_prev)
    from_next = got_next[:, wide:] + share(above_map, sent_next)
    fill_rows(ext, flags, from_prev, from_next, rows)
    lift_block(flags, ext, half, full, ll, tn, tp, rows, width, stride)
    for r in range(full.shape[0]):
        final_ref[:, r, :] = full[r].T


def spec(shape):
    return pl.BlockSpec(shape[:-1] + (LANES,), lambda h, f: (0,) * (len(shape) - 1) + (h,))


def whole(a):
    return pl.BlockSpec(a.shape, lambda h, f: (0,) * a.ndim)


def level_call(kernel, flags, arrays, out_shape, rows, width, aliases, consts=(), ahead=False):
    bands = arrays[0].shape[-1]
    ll_shape = (rows // 2, width // 2, bands)
    edge_shape = (2, width // 2 + (width // 4 if ahead else 0), bands)
    outs = (out_shape, ll_shape, edge_shape, edge_shape)
    grid_spec = pltpu.PrefetchScalarGridSpec(
        num_scalar_prefetch=1,
        grid=(bands // LANES,),
        in_specs=[spec(a.shape) for a in arrays] + [whole(c) for c in consts],
        out_specs=tuple(spec(o) for o in outs),
        scratch_shapes=[
            pltpu.VMEM((rows + 2 * EDGE, width, LANES), jnp.float32),
            pltpu.VMEM((2, rows // 2, width, LANES), jnp.float32),
        ],
    )
    return pl.pallas_call(
        kernel,
        grid_spec=grid_spec,
        out_shape=tuple(jax.ShapeDtypeStruct(o, jnp.float32) for o in outs),
        input_output_aliases=aliases,
        compiler_params=pltpu.CompilerParams(vmem_limit_bytes=100 * 1024 * 1024),
    )(flags, *arrays, *consts)


def np_partials(x):
    a1, b1 = alpha_one, beta_one
    n = x.shape[0]
    s_pen, d_pen, s_last, d_last = x[n - 4], x[n - 3], x[n - 2], x[n - 1]
    to_next = np.stack([s_last + b1 * (d_pen + a1 * (s_pen + s_last)), d_last + a1 * s_last])
    to_prev = np.stack([x[0], x[1] + a1 * (x[0] + x[2])])
    return to_next, to_prev


def np_lift(v, axis):
    a1, b1, a2, b2 = alpha_one, beta_one, alpha_two, beta_two
    v = np.moveaxis(v, axis, 0)
    s, d = v[0::2].copy(), v[1::2].copy()

    def nxt(u):
        return np.concatenate([u[1:], u[-1:]])

    def prv(u):
        return np.concatenate([u[:1], u[:-1]])

    d = d + a1 * (s + nxt(s))
    s = s + b1 * (prv(d) + d)
    d = d + a2 * (s + nxt(s))
    s = s + b2 * (prv(d) + d)
    return np.moveaxis(s / scale_k, 0, axis), np.moveaxis(d * scale_k, 0, axis)


def np_ll(level, from_prev, from_next):
    a1 = alpha_one
    b, a = from_prev
    s, dp = from_next
    z = np.zeros_like(b)
    ext = np.concatenate([np.stack([z, -a1 * b, b, a - a1 * b]), level,
                          np.stack([s, dp - a1 * s, z, z])])
    rows_s, _ = np_lift(ext, 0)
    lo = EDGE // 2
    rows_s = rows_s[lo : lo + level.shape[0] // 2]
    ll, _ = np_lift(rows_s, 1)
    return ll


@functools.lru_cache(maxsize=None)
def next_level_maps(rows, width):
    zero_edge = np.zeros((2, width))
    own = np.zeros((rows, width, 4, width // 2))
    for r in range(rows):
        for w in range(width):
            unit = np.zeros((rows, width))
            unit[r, w] = 1.0
            ll = np_ll(unit, zero_edge, zero_edge)
            tn, tp = np_partials(ll)
            own[r, w] = np.concatenate([tn, tp])
    from_below = np.zeros((2, width, 2, width // 2))
    from_above = np.zeros((2, width, 2, width // 2))
    zero = np.zeros((rows, width))
    for p in range(2):
        for w in range(width):
            unit = np.zeros((2, width))
            unit[p, w] = 1.0
            from_below[p, w] = np_partials(np_ll(zero, zero_edge, unit))[0]
            from_above[p, w] = np_partials(np_ll(zero, unit, zero_edge))[1]
    return tuple(m.astype(np.float32) for m in (own, from_below, from_above))


def to_core_mate(x):
    return lax.ppermute(x, "cols", [(0, 1), (1, 0)])


def diagonal(x, by):
    rows = lax.axis_size("rows")
    pairs = [
        (r * 2 + c, (r + by) * 2 + 1 - c)
        for r in range(rows)
        for c in range(2)
        if 0 <= r + by < rows
    ]
    return lax.ppermute(x, ("rows", "cols"), pairs)


def on_device(radiance, decorrelation):
    bands, rows, width = radiance.shape
    padded_bands = -(-bands // LANES) * LANES
    on_left = lax.axis_index("cols") == 0
    flags = jnp.stack(
        [
            on_left,
            lax.axis_index("rows") == 0,
            lax.axis_index("rows") == lax.axis_size("rows") - 1,
        ]
    ).astype(jnp.int32)
    weights = jnp.pad(decorrelation, ((0, padded_bands - bands), (0, 0)))

    def facing(x):
        return jnp.where(on_left, x[:, width - HALO :], x[:, :HALO])

    def mix(x):
        return jnp.einsum("crw,bc->rwb", x, weights, precision=lax.Precision.HIGHEST,
                          preferred_element_type=jnp.float32)

    own = mix(radiance)
    mixed_next, mixed_prev = partials(own, 0)
    p_own = shifted(mixed_next, "rows", 1)
    n_own = shifted(mixed_prev, "rows", -1)
    p_halo = diagonal(facing(mixed_next), 1)
    n_halo = diagonal(facing(mixed_prev), -1)
    halo = to_core_mate(facing(own))
    ext_width = width + HALO
    out_shape = (rows, width, padded_bands)
    assert LEVELS == 3
    own_map, below_map, above_map = next_level_maps(rows // 2, ext_width // 2)
    ahead_map = jnp.asarray(own_map.reshape(-1, own_map.shape[2] * own_map.shape[3]).T)
    out, level, tn, tp = level_call(
        first_kernel, flags,
        [own, halo, p_own, p_halo, n_own, n_halo],
        out_shape, rows, ext_width, {}, consts=(ahead_map,), ahead=True)
    r, w = level.shape[0], level.shape[1]
    got_prev = shifted(tn, "rows", 1)
    got_next = shifted(tp, "rows", -1)
    sent_next, sent_prev = tn, tp
    middle, level, tn, tp = level_call(
        functools.partial(next_kernel, stride=1), flags,
        [level, got_prev, got_next], (rows // 2, width // 2, padded_bands), r, w, {})
    below = jnp.asarray(below_map.reshape(-1, below_map.shape[2] * below_map.shape[3]).T)
    above = jnp.asarray(above_map.reshape(-1, above_map.shape[2] * above_map.shape[3]).T)
    return last_call(flags, [level, got_prev, got_next, sent_next, sent_prev, out, middle],
                     (below, above), bands, 4)


def last_call(flags, arrays, consts, bands, stride):
    level, out, middle = arrays[0], arrays[-2], arrays[-1]
    arrays = arrays[:-2]
    rows, width = level.shape[0], level.shape[1]
    final_shape = (bands, out.shape[0], out.shape[1])
    grid_spec = pltpu.PrefetchScalarGridSpec(
        num_scalar_prefetch=1,
        grid=(out.shape[-1] // LANES,),
        in_specs=[spec(a.shape) for a in arrays] + [whole(c) for c in consts]
        + [spec(out.shape), spec(middle.shape)],
        out_specs=pl.BlockSpec((LANES,) + final_shape[1:], lambda h, f: (h, 0, 0)),
        scratch_shapes=[
            pltpu.VMEM((rows + 2 * EDGE, width, LANES), jnp.float32),
            pltpu.VMEM((2, rows // 2, width, LANES), jnp.float32),
            pltpu.VMEM(out.shape[:-1] + (LANES,), jnp.float32),
            pltpu.VMEM((rows // 2, width // 2, LANES), jnp.float32),
            pltpu.VMEM((2, width // 2, LANES), jnp.float32),
            pltpu.VMEM((2, width // 2, LANES), jnp.float32),
        ],
    )
    return pl.pallas_call(
        functools.partial(last_kernel, stride=stride),
        grid_spec=grid_spec,
        out_shape=jax.ShapeDtypeStruct(final_shape, jnp.float32),
        compiler_params=pltpu.CompilerParams(vmem_limit_bytes=100 * 1024 * 1024),
    )(flags, *arrays, *consts, out, middle)


def solution(mesh):
    assert mesh.shape["cols"] == 2
    placed = (P(None, ("groups", "rows"), "cols"), P())
    return jax.shard_map(
        on_device,
        mesh=mesh,
        in_specs=placed,
        out_specs=P(None, ("groups", "rows"), "cols"),
        check_vma=False,
    )
```

```python
import functools

import numpy as np
import jax
import jax.numpy as jnp
from jax import lax
from jax.experimental import pallas as pl
from jax.experimental.pallas import tpu as pltpu
from jax.sharding import PartitionSpec as P

LEVELS = 3
HALO = 32
EDGE = 4
LANES = 128


alpha_one = -1.586134342059924
beta_one = -0.052980118572961
alpha_two = 0.882911075530934
beta_two = 0.443506852043971
scale_k = 1.230174104914001


def shifted(x, axis, by):
    size = lax.axis_size(axis)
    pairs = [(i, i + by) for i in range(size) if 0 <= i + by < size]
    return lax.ppermute(x, axis, pairs)


def partials(x, axis):
    a1, b1 = alpha_one, beta_one
    n = x.shape[axis]

    def row(i):
        return lax.slice_in_dim(x, i, i + 1, axis=axis)

    s_pen, d_pen, s_last, d_last = row(n - 4), row(n - 3), row(n - 2), row(n - 1)
    s0, d0, s1 = row(0), row(1), row(2)
    to_next = jnp.concatenate(
        [s_last + b1 * (d_pen + a1 * (s_pen + s_last)), d_last + a1 * s_last], axis=axis
    )
    to_prev = jnp.concatenate([s0, d0 + a1 * (s0 + s1)], axis=axis)
    return to_next, to_prev


def fill_rows(ext, flags, from_prev, from_next, rows):
    a1 = alpha_one
    first = flags[1] == 1
    last = flags[2] == 1
    base = EDGE + rows

    @pl.when(first)
    def _():
        ext[0:EDGE] = jnp.concatenate(
            [ext[2 * EDGE - k : 2 * EDGE - k + 1] for k in range(EDGE)], axis=0
        )

    @pl.when(jnp.logical_not(first))
    def _():
        b, a = from_prev[0:1], from_prev[1:2]
        ext[0:EDGE] = jnp.concatenate([jnp.zeros_like(b), -a1 * b, b, a - a1 * b], axis=0)

    @pl.when(last)
    def _():
        ext[base : base + EDGE] = jnp.concatenate(
            [ext[base - 2 - k : base - 1 - k] for k in range(EDGE)], axis=0
        )

    @pl.when(jnp.logical_not(last))
    def _():
        s, dp = from_next[0:1], from_next[1:2]
        z = jnp.zeros_like(s)
        ext[base : base + EDGE] = jnp.concatenate([s, dp - a1 * s, z, z], axis=0)


def lift_block(flags, ext, half, out_ref, ll_ref, tn_ref, tp_ref, rows, width, stride,
               ahead_map=None):
    hr, hw = rows // 2, width // 2
    a1, b1, a2, b2 = alpha_one, beta_one, alpha_two, beta_two
    n = hr + EDGE
    pairs = ext[...].reshape(n, 2, width, LANES)
    s = pairs[:, 0]
    d = pairs[:, 1]

    def nxt0(v):
        return jnp.concatenate([v[1:], v[-1:]], axis=0)

    def prv0(v):
        return jnp.concatenate([v[:1], v[:-1]], axis=0)

    d = d + a1 * (s + nxt0(s))
    s = s + b1 * (prv0(d) + d)
    d = d + a2 * (s + nxt0(s))
    s = s + b2 * (prv0(d) + d)
    lo = EDGE // 2
    half[0] = s[lo : lo + hr] / scale_k
    half[1] = d[lo : lo + hr] * scale_k

    col = lax.broadcasted_iota(jnp.int32, (hr, hw, LANES), 1)

    def nxt1(v):
        return jnp.where(col == hw - 1, v, pltpu.roll(v, hw - 1, 1))

    def prv1(v):
        return jnp.where(col == 0, v, pltpu.roll(v, 1, 1))

    step = 2 * stride
    own_hw = out_ref.shape[1] // step
    on_left = flags[0] == 1

    def store(pr, e, o):
        rows_at = pl.ds(pr * stride, hr, stride=step)

        @pl.when(on_left)
        def _():
            out_ref[rows_at, pl.ds(0, own_hw, stride=step), :] = e[:, :own_hw]
            out_ref[rows_at, pl.ds(stride, own_hw, stride=step), :] = o[:, :own_hw]

        @pl.when(jnp.logical_not(on_left))
        def _():
            out_ref[rows_at, pl.ds(0, own_hw, stride=step), :] = e[:, hw - own_hw :]
            out_ref[rows_at, pl.ds(stride, own_hw, stride=step), :] = o[:, hw - own_hw :]

    for pr in range(2):
        e = half[pr, :, pl.ds(0, hw, stride=2), :]
        o = half[pr, :, pl.ds(1, hw, stride=2), :]
        o = o + a1 * (e + nxt1(e))
        e = e + b1 * (prv1(o) + o)
        o = o + a2 * (e + nxt1(e))
        e = e + b2 * (prv1(o) + o)
        e = e / scale_k
        o = o * scale_k
        store(pr, e, o)
        if pr == 0:
            ll_ref[...] = e
            to_next, to_prev = partials(e, 0)
            if ahead_map is None:
                tn_ref[...] = to_next
                tp_ref[...] = to_prev
            else:
                quarter = hw // 2
                ahead = jnp.dot(ahead_map[...], e.reshape(hr * hw, LANES),
                                precision=lax.Precision.HIGHEST,
                                preferred_element_type=jnp.float32)
                ahead = ahead.reshape(4, quarter, LANES)
                tn_ref[:, :hw] = to_next
                tn_ref[:, hw:] = ahead[:2]
                tp_ref[:, :hw] = to_prev
                tp_ref[:, hw:] = ahead[2:]


def first_kernel(flags, own, halo, prev_own, prev_halo, next_own, next_halo, ahead_map,
                 out_ref, ll_ref, tn_ref, tp_ref, ext, half):
    rows, h = own.shape[0], halo.shape[1]
    width = own.shape[1] + h
    on_left = flags[0] == 1

    @pl.when(on_left)
    def _():
        ext[EDGE : EDGE + rows, 0 : width - h] = own[...]
        ext[EDGE : EDGE + rows, width - h : width] = halo[...]

    @pl.when(jnp.logical_not(on_left))
    def _():
        ext[EDGE : EDGE + rows, 0:h] = halo[...]
        ext[EDGE : EDGE + rows, h:width] = own[...]

    def joined(o, hh):
        return jnp.where(on_left, jnp.concatenate([o[...], hh[...]], axis=1),
                         jnp.concatenate([hh[...], o[...]], axis=1))

    fill_rows(ext, flags, joined(prev_own, prev_halo), joined(next_own, next_halo), rows)
    lift_block(flags, ext, half, out_ref, ll_ref, tn_ref, tp_ref, rows, width, 1, ahead_map)


def next_kernel(flags, x_ref, from_prev, from_next,
                out_ref, ll_ref, tn_ref, tp_ref, ext, half, *, stride):
    rows, width = x_ref.shape[0], x_ref.shape[1]
    ext[EDGE : EDGE + rows] = x_ref[...]
    fill_rows(ext, flags, from_prev[:, :width], from_next[:, :width], rows)
    lift_block(flags, ext, half, out_ref, ll_ref, tn_ref, tp_ref, rows, width, stride)


def last_kernel(flags, x_ref, got_prev, got_next, sent_next, sent_prev, below_map, above_map,
                prev_out, middle, final_ref, ext, half, full, ll, tn, tp, *, stride):
    rows, width = x_ref.shape[0], x_ref.shape[1]
    wide = 2 * width

    def share(m, sent):
        part = jnp.dot(m[...], sent[:, :wide].reshape(2 * wide, LANES),
                       precision=lax.Precision.HIGHEST, preferred_element_type=jnp.float32)
        return part.reshape(2, width, LANES)

    full[...] = prev_out[...]
    mr, mw = middle.shape[0], middle.shape[1]
    full[pl.ds(0, mr, stride=2), pl.ds(0, mw, stride=2), :] = middle[...]
    ext[EDGE : EDGE + rows] = x_ref[...]
    from_prev = got_prev[:, wide:] + share(below_map, sent_prev)
    from_next = got_next[:, wide:] + share(above_map, sent_next)
    fill_rows(ext, flags, from_prev, from_next, rows)
    lift_block(flags, ext, half, full, ll, tn, tp, rows, width, stride)
    for r in range(full.shape[0]):
        final_ref[:, r, :] = full[r].T


def spec(shape):
    return pl.BlockSpec(shape[:-1] + (LANES,), lambda h, f: (0,) * (len(shape) - 1) + (h,))


def whole(a):
    return pl.BlockSpec(a.shape, lambda h, f: (0,) * a.ndim)


def level_call(kernel, flags, arrays, out_shape, rows, width, aliases, consts=(), ahead=False,
               edge_bands=None):
    bands = arrays[0].shape[-1]
    ll_shape = (rows // 2, width // 2, bands)
    edge_shape = (2, width // 2 + (width // 4 if ahead else 0), edge_bands or bands)
    outs = (out_shape, ll_shape, edge_shape, edge_shape)
    grid_spec = pltpu.PrefetchScalarGridSpec(
        num_scalar_prefetch=1,
        grid=(bands // LANES,),
        in_specs=[spec(a.shape) for a in arrays] + [whole(c) for c in consts],
        out_specs=tuple(spec(o) for o in outs),
        scratch_shapes=[
            pltpu.VMEM((rows + 2 * EDGE, width, LANES), jnp.float32),
            pltpu.VMEM((2, rows // 2, width, LANES), jnp.float32),
        ],
    )
    return pl.pallas_call(
        kernel,
        grid_spec=grid_spec,
        out_shape=tuple(jax.ShapeDtypeStruct(o, jnp.float32) for o in outs),
        input_output_aliases=aliases,
        compiler_params=pltpu.CompilerParams(vmem_limit_bytes=100 * 1024 * 1024),
    )(flags, *arrays, *consts)


def np_partials(x):
    a1, b1 = alpha_one, beta_one
    n = x.shape[0]
    s_pen, d_pen, s_last, d_last = x[n - 4], x[n - 3], x[n - 2], x[n - 1]
    to_next = np.stack([s_last + b1 * (d_pen + a1 * (s_pen + s_last)), d_last + a1 * s_last])
    to_prev = np.stack([x[0], x[1] + a1 * (x[0] + x[2])])
    return to_next, to_prev


def np_lift(v, axis):
    a1, b1, a2, b2 = alpha_one, beta_one, alpha_two, beta_two
    v = np.moveaxis(v, axis, 0)
    s, d = v[0::2].copy(), v[1::2].copy()

    def nxt(u):
        return np.concatenate([u[1:], u[-1:]])

    def prv(u):
        return np.concatenate([u[:1], u[:-1]])

    d = d + a1 * (s + nxt(s))
    s = s + b1 * (prv(d) + d)
    d = d + a2 * (s + nxt(s))
    s = s + b2 * (prv(d) + d)
    return np.moveaxis(s / scale_k, 0, axis), np.moveaxis(d * scale_k, 0, axis)


def np_ll(level, from_prev, from_next):
    a1 = alpha_one
    b, a = from_prev
    s, dp = from_next
    z = np.zeros_like(b)
    ext = np.concatenate([np.stack([z, -a1 * b, b, a - a1 * b]), level,
                          np.stack([s, dp - a1 * s, z, z])])
    rows_s, _ = np_lift(ext, 0)
    lo = EDGE // 2
    rows_s = rows_s[lo : lo + level.shape[0] // 2]
    ll, _ = np_lift(rows_s, 1)
    return ll


@functools.lru_cache(maxsize=None)
def next_level_maps(rows, width):
    zero_edge = np.zeros((2, width))
    own = np.zeros((rows, width, 4, width // 2))
    for r in range(rows):
        for w in range(width):
            unit = np.zeros((rows, width))
            unit[r, w] = 1.0
            ll = np_ll(unit, zero_edge, zero_edge)
            tn, tp = np_partials(ll)
            own[r, w] = np.concatenate([tn, tp])
    from_below = np.zeros((2, width, 2, width // 2))
    from_above = np.zeros((2, width, 2, width // 2))
    zero = np.zeros((rows, width))
    for p in range(2):
        for w in range(width):
            unit = np.zeros((2, width))
            unit[p, w] = 1.0
            from_below[p, w] = np_partials(np_ll(zero, zero_edge, unit))[0]
            from_above[p, w] = np_partials(np_ll(zero, unit, zero_edge))[1]
    return tuple(m.astype(np.float32) for m in (own, from_below, from_above))


def to_core_mate(x):
    return lax.ppermute(x, "cols", [(0, 1), (1, 0)])


def diagonal(x, by):
    rows = lax.axis_size("rows")
    pairs = [
        (r * 2 + c, (r + by) * 2 + 1 - c)
        for r in range(rows)
        for c in range(2)
        if 0 <= r + by < rows
    ]
    return lax.ppermute(x, ("rows", "cols"), pairs)


def on_device(radiance, decorrelation):
    bands, rows, width = radiance.shape
    padded_bands = -(-bands // LANES) * LANES
    on_left = lax.axis_index("cols") == 0
    flags = jnp.stack(
        [
            on_left,
            lax.axis_index("rows") == 0,
            lax.axis_index("rows") == lax.axis_size("rows") - 1,
        ]
    ).astype(jnp.int32)
    weights = jnp.pad(decorrelation, ((0, padded_bands - bands), (0, 0)))

    def facing(x):
        return jnp.where(on_left, x[:, width - HALO :], x[:, :HALO])

    def mix(x):
        return jnp.einsum("crw,bc->rwb", x, weights, precision=lax.Precision.HIGHEST,
                          preferred_element_type=jnp.float32)

    own = mix(radiance)
    mixed_next, mixed_prev = partials(own, 0)

    def real(x):
        return x[..., :bands]

    p_own = shifted(real(mixed_next), "rows", 1)
    n_own = shifted(real(mixed_prev), "rows", -1)
    p_halo = diagonal(real(facing(mixed_next)), 1)
    n_halo = diagonal(real(facing(mixed_prev)), -1)
    halo = to_core_mate(real(facing(own)))
    ext_width = width + HALO
    out_shape = (rows, width, padded_bands)
    assert LEVELS == 3
    own_map, below_map, above_map = next_level_maps(rows // 2, ext_width // 2)
    ahead_map = jnp.asarray(own_map.reshape(-1, own_map.shape[2] * own_map.shape[3]).T)
    out, level, tn, tp = level_call(
        first_kernel, flags,
        [own, halo, p_own, p_halo, n_own, n_halo],
        out_shape, rows, ext_width, {}, consts=(ahead_map,), ahead=True, edge_bands=bands)
    r, w = level.shape[0], level.shape[1]
    got_prev = shifted(tn, "rows", 1)
    got_next = shifted(tp, "rows", -1)
    sent_next, sent_prev = tn, tp
    middle, level, tn, tp = level_call(
        functools.partial(next_kernel, stride=1), flags,
        [level, got_prev, got_next], (rows // 2, width // 2, padded_bands), r, w, {})
    below = jnp.asarray(below_map.reshape(-1, below_map.shape[2] * below_map.shape[3]).T)
    above = jnp.asarray(above_map.reshape(-1, above_map.shape[2] * above_map.shape[3]).T)
    return last_call(flags, [level, got_prev, got_next, sent_next, sent_prev, out, middle],
                     (below, above), bands, 4)


def last_call(flags, arrays, consts, bands, stride):
    level, out, middle = arrays[0], arrays[-2], arrays[-1]
    arrays = arrays[:-2]
    rows, width = level.shape[0], level.shape[1]
    final_shape = (bands, out.shape[0], out.shape[1])
    grid_spec = pltpu.PrefetchScalarGridSpec(
        num_scalar_prefetch=1,
        grid=(out.shape[-1] // LANES,),
        in_specs=[spec(a.shape) for a in arrays] + [whole(c) for c in consts]
        + [spec(out.shape), spec(middle.shape)],
        out_specs=pl.BlockSpec((LANES,) + final_shape[1:], lambda h, f: (h, 0, 0)),
        scratch_shapes=[
            pltpu.VMEM((rows + 2 * EDGE, width, LANES), jnp.float32),
            pltpu.VMEM((2, rows // 2, width, LANES), jnp.float32),
            pltpu.VMEM(out.shape[:-1] + (LANES,), jnp.float32),
            pltpu.VMEM((rows // 2, width // 2, LANES), jnp.float32),
            pltpu.VMEM((2, width // 2, LANES), jnp.float32),
            pltpu.VMEM((2, width // 2, LANES), jnp.float32),
        ],
    )
    return pl.pallas_call(
        functools.partial(last_kernel, stride=stride),
        grid_spec=grid_spec,
        out_shape=jax.ShapeDtypeStruct(final_shape, jnp.float32),
        compiler_params=pltpu.CompilerParams(vmem_limit_bytes=100 * 1024 * 1024),
    )(flags, *arrays, *consts, out, middle)


def solution(mesh):
    assert mesh.shape["cols"] == 2
    placed = (P(None, ("groups", "rows"), "cols"), P())
    return jax.shard_map(
        on_device,
        mesh=mesh,
        in_specs=placed,
        out_specs=P(None, ("groups", "rows"), "cols"),
        check_vma=False,
    )
```

```python
import functools

import numpy as np
import jax
import jax.numpy as jnp
from jax import lax
from jax.experimental import pallas as pl
from jax.experimental.pallas import tpu as pltpu
from jax.sharding import PartitionSpec as P

LEVELS = 3
HALO = 32
EDGE = 4
LANES = 128


alpha_one = -1.586134342059924
beta_one = -0.052980118572961
alpha_two = 0.882911075530934
beta_two = 0.443506852043971
scale_k = 1.230174104914001


def shifted(x, axis, by):
    size = lax.axis_size(axis)
    pairs = [(i, i + by) for i in range(size) if 0 <= i + by < size]
    return lax.ppermute(x, axis, pairs)


def partials(x, axis):
    a1, b1 = alpha_one, beta_one
    n = x.shape[axis]

    def row(i):
        return lax.slice_in_dim(x, i, i + 1, axis=axis)

    s_pen, d_pen, s_last, d_last = row(n - 4), row(n - 3), row(n - 2), row(n - 1)
    s0, d0, s1 = row(0), row(1), row(2)
    to_next = jnp.concatenate(
        [s_last + b1 * (d_pen + a1 * (s_pen + s_last)), d_last + a1 * s_last], axis=axis
    )
    to_prev = jnp.concatenate([s0, d0 + a1 * (s0 + s1)], axis=axis)
    return to_next, to_prev


def fill_rows(ext, flags, from_prev, from_next, rows):
    a1 = alpha_one
    first = flags[1] == 1
    last = flags[2] == 1
    base = EDGE + rows

    @pl.when(first)
    def _():
        ext[0:EDGE] = jnp.concatenate(
            [ext[2 * EDGE - k : 2 * EDGE - k + 1] for k in range(EDGE)], axis=0
        )

    @pl.when(jnp.logical_not(first))
    def _():
        b, a = from_prev[0:1], from_prev[1:2]
        ext[0:EDGE] = jnp.concatenate([jnp.zeros_like(b), -a1 * b, b, a - a1 * b], axis=0)

    @pl.when(last)
    def _():
        ext[base : base + EDGE] = jnp.concatenate(
            [ext[base - 2 - k : base - 1 - k] for k in range(EDGE)], axis=0
        )

    @pl.when(jnp.logical_not(last))
    def _():
        s, dp = from_next[0:1], from_next[1:2]
        z = jnp.zeros_like(s)
        ext[base : base + EDGE] = jnp.concatenate([s, dp - a1 * s, z, z], axis=0)


def lift_block(flags, ext, half, out_ref, ll_ref, tn_ref, tp_ref, rows, width, stride,
               ahead_map=None):
    hr, hw = rows // 2, width // 2
    a1, b1, a2, b2 = alpha_one, beta_one, alpha_two, beta_two
    n = hr + EDGE
    pairs = ext[...].reshape(n, 2, width, LANES)
    s = pairs[:, 0]
    d = pairs[:, 1]

    def nxt0(v):
        return jnp.concatenate([v[1:], v[-1:]], axis=0)

    def prv0(v):
        return jnp.concatenate([v[:1], v[:-1]], axis=0)

    d = d + a1 * (s + nxt0(s))
    s = s + b1 * (prv0(d) + d)
    d = d + a2 * (s + nxt0(s))
    s = s + b2 * (prv0(d) + d)
    lo = EDGE // 2
    half[0] = s[lo : lo + hr] / scale_k
    half[1] = d[lo : lo + hr] * scale_k

    col = lax.broadcasted_iota(jnp.int32, (hr, hw, LANES), 1)

    def nxt1(v):
        return jnp.where(col == hw - 1, v, pltpu.roll(v, hw - 1, 1))

    def prv1(v):
        return jnp.where(col == 0, v, pltpu.roll(v, 1, 1))

    step = 2 * stride
    own_hw = out_ref.shape[1] // step
    on_left = flags[0] == 1

    def store(pr, e, o):
        rows_at = pl.ds(pr * stride, hr, stride=step)

        @pl.when(on_left)
        def _():
            out_ref[rows_at, pl.ds(0, own_hw, stride=step), :] = e[:, :own_hw]
            out_ref[rows_at, pl.ds(stride, own_hw, stride=step), :] = o[:, :own_hw]

        @pl.when(jnp.logical_not(on_left))
        def _():
            out_ref[rows_at, pl.ds(0, own_hw, stride=step), :] = e[:, hw - own_hw :]
            out_ref[rows_at, pl.ds(stride, own_hw, stride=step), :] = o[:, hw - own_hw :]

    for pr in range(2):
        e = half[pr, :, pl.ds(0, hw, stride=2), :]
        o = half[pr, :, pl.ds(1, hw, stride=2), :]
        o = o + a1 * (e + nxt1(e))
        e = e + b1 * (prv1(o) + o)
        o = o + a2 * (e + nxt1(e))
        e = e + b2 * (prv1(o) + o)
        e = e / scale_k
        o = o * scale_k
        store(pr, e, o)
        if pr == 0:
            ll_ref[...] = e
            to_next, to_prev = partials(e, 0)
            if ahead_map is None:
                tn_ref[...] = to_next
                tp_ref[...] = to_prev
            else:
                quarter = hw // 2
                used = hr - EDGE
                flat = e.reshape(hr * hw, LANES)
                ahead_next = jnp.dot(ahead_map[0: 2 * quarter, EDGE * hw :], flat[EDGE * hw :],
                                     precision=lax.Precision.HIGHEST,
                                     preferred_element_type=jnp.float32)
                ahead_prev = jnp.dot(ahead_map[2 * quarter :, : used * hw], flat[: used * hw],
                                     precision=lax.Precision.HIGHEST,
                                     preferred_element_type=jnp.float32)
                tn_ref[:, :hw] = to_next
                tn_ref[:, hw:] = ahead_next.reshape(2, quarter, LANES)
                tp_ref[:, :hw] = to_prev
                tp_ref[:, hw:] = ahead_prev.reshape(2, quarter, LANES)


def first_kernel(flags, own, halo, prev_own, prev_halo, next_own, next_halo, ahead_map,
                 out_ref, ll_ref, tn_ref, tp_ref, ext, half):
    rows, h = own.shape[0], halo.shape[1]
    width = own.shape[1] + h
    on_left = flags[0] == 1

    @pl.when(on_left)
    def _():
        ext[EDGE : EDGE + rows, 0 : width - h] = own[...]
        ext[EDGE : EDGE + rows, width - h : width] = halo[...]

    @pl.when(jnp.logical_not(on_left))
    def _():
        ext[EDGE : EDGE + rows, 0:h] = halo[...]
        ext[EDGE : EDGE + rows, h:width] = own[...]

    def joined(o, hh):
        return jnp.where(on_left, jnp.concatenate([o[...], hh[...]], axis=1),
                         jnp.concatenate([hh[...], o[...]], axis=1))

    fill_rows(ext, flags, joined(prev_own, prev_halo), joined(next_own, next_halo), rows)
    lift_block(flags, ext, half, out_ref, ll_ref, tn_ref, tp_ref, rows, width, 1, ahead_map)


def next_kernel(flags, x_ref, from_prev, from_next,
                out_ref, ll_ref, tn_ref, tp_ref, ext, half, *, stride):
    rows, width = x_ref.shape[0], x_ref.shape[1]
    ext[EDGE : EDGE + rows] = x_ref[...]
    fill_rows(ext, flags, from_prev[:, :width], from_next[:, :width], rows)
    lift_block(flags, ext, half, out_ref, ll_ref, tn_ref, tp_ref, rows, width, stride)


def last_kernel(flags, x_ref, got_prev, got_next, sent_next, sent_prev, below_map, above_map,
                prev_out, middle, final_ref, ext, half, ll, tn, tp, *, stride):
    rows, width = x_ref.shape[0], x_ref.shape[1]
    wide = 2 * width

    def share(m, sent):
        part = jnp.dot(m[...], sent[:, :wide].reshape(2 * wide, LANES),
                       precision=lax.Precision.HIGHEST, preferred_element_type=jnp.float32)
        return part.reshape(2, width, LANES)

    full = prev_out
    mr, mw = middle.shape[0], middle.shape[1]
    full[pl.ds(0, mr, stride=2), pl.ds(0, mw, stride=2), :] = middle[...]
    ext[EDGE : EDGE + rows] = x_ref[...]
    from_prev = got_prev[:, wide:] + share(below_map, sent_prev)
    from_next = got_next[:, wide:] + share(above_map, sent_next)
    fill_rows(ext, flags, from_prev, from_next, rows)
    lift_block(flags, ext, half, full, ll, tn, tp, rows, width, stride)
    for r in range(full.shape[0]):
        final_ref[:, r, :] = full[r].T


def spec(shape):
    return pl.BlockSpec(shape[:-1] + (LANES,), lambda h, f: (0,) * (len(shape) - 1) + (h,))


def whole(a):
    return pl.BlockSpec(a.shape, lambda h, f: (0,) * a.ndim)


def level_call(kernel, flags, arrays, out_shape, rows, width, aliases, consts=(), ahead=False):
    bands = arrays[0].shape[-1]
    ll_shape = (rows // 2, width // 2, bands)
    edge_shape = (2, width // 2 + (width // 4 if ahead else 0), bands)
    outs = (out_shape, ll_shape, edge_shape, edge_shape)
    grid_spec = pltpu.PrefetchScalarGridSpec(
        num_scalar_prefetch=1,
        grid=(bands // LANES,),
        in_specs=[spec(a.shape) for a in arrays] + [whole(c) for c in consts],
        out_specs=tuple(spec(o) for o in outs),
        scratch_shapes=[
            pltpu.VMEM((rows + 2 * EDGE, width, LANES), jnp.float32),
            pltpu.VMEM((2, rows // 2, width, LANES), jnp.float32),
        ],
    )
    return pl.pallas_call(
        kernel,
        grid_spec=grid_spec,
        out_shape=tuple(jax.ShapeDtypeStruct(o, jnp.float32) for o in outs),
        input_output_aliases=aliases,
        compiler_params=pltpu.CompilerParams(vmem_limit_bytes=100 * 1024 * 1024),
    )(flags, *arrays, *consts)


def np_partials(x):
    a1, b1 = alpha_one, beta_one
    n = x.shape[0]
    s_pen, d_pen, s_last, d_last = x[n - 4], x[n - 3], x[n - 2], x[n - 1]
    to_next = np.stack([s_last + b1 * (d_pen + a1 * (s_pen + s_last)), d_last + a1 * s_last])
    to_prev = np.stack([x[0], x[1] + a1 * (x[0] + x[2])])
    return to_next, to_prev


def np_lift(v, axis):
    a1, b1, a2, b2 = alpha_one, beta_one, alpha_two, beta_two
    v = np.moveaxis(v, axis, 0)
    s, d = v[0::2].copy(), v[1::2].copy()

    def nxt(u):
        return np.concatenate([u[1:], u[-1:]])

    def prv(u):
        return np.concatenate([u[:1], u[:-1]])

    d = d + a1 * (s + nxt(s))
    s = s + b1 * (prv(d) + d)
    d = d + a2 * (s + nxt(s))
    s = s + b2 * (prv(d) + d)
    return np.moveaxis(s / scale_k, 0, axis), np.moveaxis(d * scale_k, 0, axis)


def np_ll(level, from_prev, from_next):
    a1 = alpha_one
    b, a = from_prev
    s, dp = from_next
    z = np.zeros_like(b)
    ext = np.concatenate([np.stack([z, -a1 * b, b, a - a1 * b]), level,
                          np.stack([s, dp - a1 * s, z, z])])
    rows_s, _ = np_lift(ext, 0)
    lo = EDGE // 2
    rows_s = rows_s[lo : lo + level.shape[0] // 2]
    ll, _ = np_lift(rows_s, 1)
    return ll


@functools.lru_cache(maxsize=None)
def next_level_maps(rows, width):
    zero_edge = np.zeros((2, width))
    own = np.zeros((rows, width, 4, width // 2))
    for r in range(rows):
        for w in range(width):
            unit = np.zeros((rows, width))
            unit[r, w] = 1.0
            ll = np_ll(unit, zero_edge, zero_edge)
            tn, tp = np_partials(ll)
            own[r, w] = np.concatenate([tn, tp])
    from_below = np.zeros((2, width, 2, width // 2))
    from_above = np.zeros((2, width, 2, width // 2))
    zero = np.zeros((rows, width))
    for p in range(2):
        for w in range(width):
            unit = np.zeros((2, width))
            unit[p, w] = 1.0
            from_below[p, w] = np_partials(np_ll(zero, zero_edge, unit))[0]
            from_above[p, w] = np_partials(np_ll(zero, unit, zero_edge))[1]
    return tuple(m.astype(np.float32) for m in (own, from_below, from_above))


def to_core_mate(x):
    return lax.ppermute(x, "cols", [(0, 1), (1, 0)])


def diagonal(x, by):
    rows = lax.axis_size("rows")
    pairs = [
        (r * 2 + c, (r + by) * 2 + 1 - c)
        for r in range(rows)
        for c in range(2)
        if 0 <= r + by < rows
    ]
    return lax.ppermute(x, ("rows", "cols"), pairs)


def on_device(radiance, decorrelation):
    bands, rows, width = radiance.shape
    padded_bands = -(-bands // LANES) * LANES
    on_left = lax.axis_index("cols") == 0
    flags = jnp.stack(
        [
            on_left,
            lax.axis_index("rows") == 0,
            lax.axis_index("rows") == lax.axis_size("rows") - 1,
        ]
    ).astype(jnp.int32)
    weights = jnp.pad(decorrelation, ((0, padded_bands - bands), (0, 0)))

    def facing(x):
        return jnp.where(on_left, x[:, width - HALO :], x[:, :HALO])

    def mix(x):
        return jnp.einsum("crw,bc->rwb", x, weights, precision=lax.Precision.HIGHEST,
                          preferred_element_type=jnp.float32)

    own = mix(radiance)
    mixed_next, mixed_prev = partials(own, 0)
    p_own = shifted(mixed_next, "rows", 1)
    n_own = shifted(mixed_prev, "rows", -1)
    p_halo = diagonal(facing(mixed_next), 1)
    n_halo = diagonal(facing(mixed_prev), -1)
    halo = to_core_mate(facing(own))
    ext_width = width + HALO
    out_shape = (rows, width, padded_bands)
    assert LEVELS == 3
    own_map, below_map, above_map = next_level_maps(rows // 2, ext_width // 2)
    ahead_map = jnp.asarray(own_map.reshape(-1, own_map.shape[2] * own_map.shape[3]).T)
    out, level, tn, tp = level_call(
        first_kernel, flags,
        [own, halo, p_own, p_halo, n_own, n_halo],
        out_shape, rows, ext_width, {}, consts=(ahead_map,), ahead=True)
    r, w = level.shape[0], level.shape[1]
    got_prev = shifted(tn, "rows", 1)
    got_next = shifted(tp, "rows", -1)
    sent_next, sent_prev = tn, tp
    middle, level, tn, tp = level_call(
        functools.partial(next_kernel, stride=1), flags,
        [level, got_prev, got_next], (rows // 2, width // 2, padded_bands), r, w, {})
    below = jnp.asarray(below_map.reshape(-1, below_map.shape[2] * below_map.shape[3]).T)
    above = jnp.asarray(above_map.reshape(-1, above_map.shape[2] * above_map.shape[3]).T)
    return last_call(flags, [level, got_prev, got_next, sent_next, sent_prev, out, middle],
                     (below, above), bands, 4)


def last_call(flags, arrays, consts, bands, stride):
    level, out, middle = arrays[0], arrays[-2], arrays[-1]
    arrays = arrays[:-2]
    rows, width = level.shape[0], level.shape[1]
    final_shape = (bands, out.shape[0], out.shape[1])
    grid_spec = pltpu.PrefetchScalarGridSpec(
        num_scalar_prefetch=1,
        grid=(out.shape[-1] // LANES,),
        in_specs=[spec(a.shape) for a in arrays] + [whole(c) for c in consts]
        + [spec(out.shape), spec(middle.shape)],
        out_specs=pl.BlockSpec((LANES,) + final_shape[1:], lambda h, f: (h, 0, 0)),
        scratch_shapes=[
            pltpu.VMEM((rows + 2 * EDGE, width, LANES), jnp.float32),
            pltpu.VMEM((2, rows // 2, width, LANES), jnp.float32),
            pltpu.VMEM((rows // 2, width // 2, LANES), jnp.float32),
            pltpu.VMEM((2, width // 2, LANES), jnp.float32),
            pltpu.VMEM((2, width // 2, LANES), jnp.float32),
        ],
    )
    return pl.pallas_call(
        functools.partial(last_kernel, stride=stride),
        grid_spec=grid_spec,
        out_shape=jax.ShapeDtypeStruct(final_shape, jnp.float32),
        compiler_params=pltpu.CompilerParams(vmem_limit_bytes=100 * 1024 * 1024),
    )(flags, *arrays, *consts, out, middle)


def solution(mesh):
    assert mesh.shape["cols"] == 2
    placed = (P(None, ("groups", "rows"), "cols"), P())
    return jax.shard_map(
        on_device,
        mesh=mesh,
        in_specs=placed,
        out_specs=P(None, ("groups", "rows"), "cols"),
        check_vma=False,
    )
```

```python
import functools

import numpy as np
import jax
import jax.numpy as jnp
from jax import lax
from jax.experimental import pallas as pl
from jax.experimental.pallas import tpu as pltpu
from jax.sharding import PartitionSpec as P

LEVELS = 3
HALO = 32
EDGE = 4
LANES = 128


alpha_one = -1.586134342059924
beta_one = -0.052980118572961
alpha_two = 0.882911075530934
beta_two = 0.443506852043971
scale_k = 1.230174104914001


def shifted(x, axis, by):
    size = lax.axis_size(axis)
    pairs = [(i, i + by) for i in range(size) if 0 <= i + by < size]
    return lax.ppermute(x, axis, pairs)


def partials(x, axis):
    a1, b1 = alpha_one, beta_one
    n = x.shape[axis]

    def row(i):
        return lax.slice_in_dim(x, i, i + 1, axis=axis)

    s_pen, d_pen, s_last, d_last = row(n - 4), row(n - 3), row(n - 2), row(n - 1)
    s0, d0, s1 = row(0), row(1), row(2)
    to_next = jnp.concatenate(
        [s_last + b1 * (d_pen + a1 * (s_pen + s_last)), d_last + a1 * s_last], axis=axis
    )
    to_prev = jnp.concatenate([s0, d0 + a1 * (s0 + s1)], axis=axis)
    return to_next, to_prev


def fill_rows(ext, flags, from_prev, from_next, rows):
    a1 = alpha_one
    first = flags[1] == 1
    last = flags[2] == 1
    base = EDGE + rows

    @pl.when(first)
    def _():
        ext[0:EDGE] = jnp.concatenate(
            [ext[2 * EDGE - k : 2 * EDGE - k + 1] for k in range(EDGE)], axis=0
        )

    @pl.when(jnp.logical_not(first))
    def _():
        b, a = from_prev[0:1], from_prev[1:2]
        ext[0:EDGE] = jnp.concatenate([jnp.zeros_like(b), -a1 * b, b, a - a1 * b], axis=0)

    @pl.when(last)
    def _():
        ext[base : base + EDGE] = jnp.concatenate(
            [ext[base - 2 - k : base - 1 - k] for k in range(EDGE)], axis=0
        )

    @pl.when(jnp.logical_not(last))
    def _():
        s, dp = from_next[0:1], from_next[1:2]
        z = jnp.zeros_like(s)
        ext[base : base + EDGE] = jnp.concatenate([s, dp - a1 * s, z, z], axis=0)


def lift_block(flags, ext, half, out_ref, ll_ref, tn_ref, tp_ref, rows, width, stride,
               ahead_map=None):
    hr, hw = rows // 2, width // 2
    a1, b1, a2, b2 = alpha_one, beta_one, alpha_two, beta_two
    n = hr + EDGE
    pairs = ext[...].reshape(n, 2, width, LANES)
    s = pairs[:, 0]
    d = pairs[:, 1]

    def nxt0(v):
        return jnp.concatenate([v[1:], v[-1:]], axis=0)

    def prv0(v):
        return jnp.concatenate([v[:1], v[:-1]], axis=0)

    d = d + a1 * (s + nxt0(s))
    s = s + b1 * (prv0(d) + d)
    d = d + a2 * (s + nxt0(s))
    s = s + b2 * (prv0(d) + d)
    lo = EDGE // 2
    half[0] = s[lo : lo + hr] / scale_k
    half[1] = d[lo : lo + hr] * scale_k

    col = lax.broadcasted_iota(jnp.int32, (hr, hw, LANES), 1)

    def nxt1(v):
        return jnp.where(col == hw - 1, v, pltpu.roll(v, hw - 1, 1))

    def prv1(v):
        return jnp.where(col == 0, v, pltpu.roll(v, 1, 1))

    step = 2 * stride
    own_hw = out_ref.shape[1] // step
    on_left = flags[0] == 1

    def store(pr, e, o):
        rows_at = pl.ds(pr * stride, hr, stride=step)

        @pl.when(on_left)
        def _():
            out_ref[rows_at, pl.ds(0, own_hw, stride=step), :] = e[:, :own_hw]
            out_ref[rows_at, pl.ds(stride, own_hw, stride=step), :] = o[:, :own_hw]

        @pl.when(jnp.logical_not(on_left))
        def _():
            out_ref[rows_at, pl.ds(0, own_hw, stride=step), :] = e[:, hw - own_hw :]
            out_ref[rows_at, pl.ds(stride, own_hw, stride=step), :] = o[:, hw - own_hw :]

    for pr in range(2):
        e = half[pr, :, pl.ds(0, hw, stride=2), :]
        o = half[pr, :, pl.ds(1, hw, stride=2), :]
        o = o + a1 * (e + nxt1(e))
        e = e + b1 * (prv1(o) + o)
        o = o + a2 * (e + nxt1(e))
        e = e + b2 * (prv1(o) + o)
        e = e / scale_k
        o = o * scale_k
        store(pr, e, o)
        if pr == 0:
            ll_ref[...] = e
            to_next, to_prev = partials(e, 0)
            if ahead_map is None:
                tn_ref[...] = to_next
                tp_ref[...] = to_prev
            else:
                quarter = hw // 2
                used = hr - EDGE
                flat = e.reshape(hr * hw, LANES)
                ahead_next = jnp.dot(ahead_map[0: 2 * quarter, EDGE * hw :], flat[EDGE * hw :],
                                     precision=lax.Precision.HIGHEST,
                                     preferred_element_type=jnp.float32)
                ahead_prev = jnp.dot(ahead_map[2 * quarter :, : used * hw], flat[: used * hw],
                                     precision=lax.Precision.HIGHEST,
                                     preferred_element_type=jnp.float32)
                tn_ref[:, :hw] = to_next
                tn_ref[:, hw:] = ahead_next.reshape(2, quarter, LANES)
                tp_ref[:, :hw] = to_prev
                tp_ref[:, hw:] = ahead_prev.reshape(2, quarter, LANES)


def first_kernel(flags, own, halo, prev_own, prev_halo, next_own, next_halo, ahead_map,
                 out_ref, ll_ref, tn_ref, tp_ref, ext, half):
    rows, h = own.shape[0], halo.shape[1]
    width = own.shape[1] + h
    on_left = flags[0] == 1

    @pl.when(on_left)
    def _():
        ext[EDGE : EDGE + rows, 0 : width - h] = own[...]
        ext[EDGE : EDGE + rows, width - h : width] = halo[...]

    @pl.when(jnp.logical_not(on_left))
    def _():
        ext[EDGE : EDGE + rows, 0:h] = halo[...]
        ext[EDGE : EDGE + rows, h:width] = own[...]

    def joined(o, hh):
        return jnp.where(on_left, jnp.concatenate([o[...], hh[...]], axis=1),
                         jnp.concatenate([hh[...], o[...]], axis=1))

    fill_rows(ext, flags, joined(prev_own, prev_halo), joined(next_own, next_halo), rows)
    lift_block(flags, ext, half, out_ref, ll_ref, tn_ref, tp_ref, rows, width, 1, ahead_map)


def next_kernel(flags, x_ref, from_prev, from_next,
                out_ref, ll_ref, tn_ref, tp_ref, ext, half, *, stride):
    rows, width = x_ref.shape[0], x_ref.shape[1]
    ext[EDGE : EDGE + rows] = x_ref[...]
    fill_rows(ext, flags, from_prev[:, :width], from_next[:, :width], rows)
    lift_block(flags, ext, half, out_ref, ll_ref, tn_ref, tp_ref, rows, width, stride)


def last_kernel(flags, x_ref, got_prev, got_next, sent_next, sent_prev, below_map, above_map,
                prev_out, middle, final_ref, ext, half, ll, tn, tp, *, stride):
    rows, width = x_ref.shape[0], x_ref.shape[1]
    wide = 2 * width

    def share(m, sent):
        part = jnp.dot(m[...], sent[:, :wide].reshape(2 * wide, LANES),
                       precision=lax.Precision.HIGHEST, preferred_element_type=jnp.float32)
        return part.reshape(2, width, LANES)

    full = prev_out
    mr, mw = middle.shape[0], middle.shape[1]
    full[pl.ds(0, mr, stride=2), pl.ds(0, mw, stride=2), :] = middle[...]
    ext[EDGE : EDGE + rows] = x_ref[...]
    from_prev = got_prev[:, wide:] + share(below_map, sent_prev)
    from_next = got_next[:, wide:] + share(above_map, sent_next)
    fill_rows(ext, flags, from_prev, from_next, rows)
    lift_block(flags, ext, half, full, ll, tn, tp, rows, width, stride)
    final_ref[...] = jnp.transpose(full[...], (2, 0, 1))


def spec(shape):
    return pl.BlockSpec(shape[:-1] + (LANES,), lambda h, f: (0,) * (len(shape) - 1) + (h,))


def whole(a):
    return pl.BlockSpec(a.shape, lambda h, f: (0,) * a.ndim)


def level_call(kernel, flags, arrays, out_shape, rows, width, aliases, consts=(), ahead=False):
    bands = arrays[0].shape[-1]
    ll_shape = (rows // 2, width // 2, bands)
    edge_shape = (2, width // 2 + (width // 4 if ahead else 0), bands)
    outs = (out_shape, ll_shape, edge_shape, edge_shape)
    grid_spec = pltpu.PrefetchScalarGridSpec(
        num_scalar_prefetch=1,
        grid=(bands // LANES,),
        in_specs=[spec(a.shape) for a in arrays] + [whole(c) for c in consts],
        out_specs=tuple(spec(o) for o in outs),
        scratch_shapes=[
            pltpu.VMEM((rows + 2 * EDGE, width, LANES), jnp.float32),
            pltpu.VMEM((2, rows // 2, width, LANES), jnp.float32),
        ],
    )
    return pl.pallas_call(
        kernel,
        grid_spec=grid_spec,
        out_shape=tuple(jax.ShapeDtypeStruct(o, jnp.float32) for o in outs),
        input_output_aliases=aliases,
        compiler_params=pltpu.CompilerParams(vmem_limit_bytes=100 * 1024 * 1024),
    )(flags, *arrays, *consts)


def np_partials(x):
    a1, b1 = alpha_one, beta_one
    n = x.shape[0]
    s_pen, d_pen, s_last, d_last = x[n - 4], x[n - 3], x[n - 2], x[n - 1]
    to_next = np.stack([s_last + b1 * (d_pen + a1 * (s_pen + s_last)), d_last + a1 * s_last])
    to_prev = np.stack([x[0], x[1] + a1 * (x[0] + x[2])])
    return to_next, to_prev


def np_lift(v, axis):
    a1, b1, a2, b2 = alpha_one, beta_one, alpha_two, beta_two
    v = np.moveaxis(v, axis, 0)
    s, d = v[0::2].copy(), v[1::2].copy()

    def nxt(u):
        return np.concatenate([u[1:], u[-1:]])

    def prv(u):
        return np.concatenate([u[:1], u[:-1]])

    d = d + a1 * (s + nxt(s))
    s = s + b1 * (prv(d) + d)
    d = d + a2 * (s + nxt(s))
    s = s + b2 * (prv(d) + d)
    return np.moveaxis(s / scale_k, 0, axis), np.moveaxis(d * scale_k, 0, axis)


def np_ll(level, from_prev, from_next):
    a1 = alpha_one
    b, a = from_prev
    s, dp = from_next
    z = np.zeros_like(b)
    ext = np.concatenate([np.stack([z, -a1 * b, b, a - a1 * b]), level,
                          np.stack([s, dp - a1 * s, z, z])])
    rows_s, _ = np_lift(ext, 0)
    lo = EDGE // 2
    rows_s = rows_s[lo : lo + level.shape[0] // 2]
    ll, _ = np_lift(rows_s, 1)
    return ll


@functools.lru_cache(maxsize=None)
def next_level_maps(rows, width):
    zero_edge = np.zeros((2, width))
    own = np.zeros((rows, width, 4, width // 2))
    for r in range(rows):
        for w in range(width):
            unit = np.zeros((rows, width))
            unit[r, w] = 1.0
            ll = np_ll(unit, zero_edge, zero_edge)
            tn, tp = np_partials(ll)
            own[r, w] = np.concatenate([tn, tp])
    from_below = np.zeros((2, width, 2, width // 2))
    from_above = np.zeros((2, width, 2, width // 2))
    zero = np.zeros((rows, width))
    for p in range(2):
        for w in range(width):
            unit = np.zeros((2, width))
            unit[p, w] = 1.0
            from_below[p, w] = np_partials(np_ll(zero, zero_edge, unit))[0]
            from_above[p, w] = np_partials(np_ll(zero, unit, zero_edge))[1]
    return tuple(m.astype(np.float32) for m in (own, from_below, from_above))


def to_core_mate(x):
    return lax.ppermute(x, "cols", [(0, 1), (1, 0)])


def diagonal(x, by):
    rows = lax.axis_size("rows")
    pairs = [
        (r * 2 + c, (r + by) * 2 + 1 - c)
        for r in range(rows)
        for c in range(2)
        if 0 <= r + by < rows
    ]
    return lax.ppermute(x, ("rows", "cols"), pairs)


def on_device(radiance, decorrelation):
    bands, rows, width = radiance.shape
    padded_bands = -(-bands // LANES) * LANES
    on_left = lax.axis_index("cols") == 0
    flags = jnp.stack(
        [
            on_left,
            lax.axis_index("rows") == 0,
            lax.axis_index("rows") == lax.axis_size("rows") - 1,
        ]
    ).astype(jnp.int32)
    weights = jnp.pad(decorrelation, ((0, padded_bands - bands), (0, 0)))

    def facing(x):
        return jnp.where(on_left, x[:, width - HALO :], x[:, :HALO])

    def mix(x):
        return jnp.einsum("crw,bc->rwb", x, weights, precision=lax.Precision.HIGHEST,
                          preferred_element_type=jnp.float32)

    own = mix(radiance)
    mixed_next, mixed_prev = partials(own, 0)
    p_own = shifted(mixed_next, "rows", 1)
    n_own = shifted(mixed_prev, "rows", -1)
    p_halo = diagonal(facing(mixed_next), 1)
    n_halo = diagonal(facing(mixed_prev), -1)
    halo = to_core_mate(facing(own))
    ext_width = width + HALO
    out_shape = (rows, width, padded_bands)
    assert LEVELS == 3
    own_map, below_map, above_map = next_level_maps(rows // 2, ext_width // 2)
    ahead_map = jnp.asarray(own_map.reshape(-1, own_map.shape[2] * own_map.shape[3]).T)
    out, level, tn, tp = level_call(
        first_kernel, flags,
        [own, halo, p_own, p_halo, n_own, n_halo],
        out_shape, rows, ext_width, {}, consts=(ahead_map,), ahead=True)
    r, w = level.shape[0], level.shape[1]
    got_prev = shifted(tn, "rows", 1)
    got_next = shifted(tp, "rows", -1)
    sent_next, sent_prev = tn, tp
    middle, level, tn, tp = level_call(
        functools.partial(next_kernel, stride=1), flags,
        [level, got_prev, got_next], (rows // 2, width // 2, padded_bands), r, w, {})
    below = jnp.asarray(below_map.reshape(-1, below_map.shape[2] * below_map.shape[3]).T)
    above = jnp.asarray(above_map.reshape(-1, above_map.shape[2] * above_map.shape[3]).T)
    return last_call(flags, [level, got_prev, got_next, sent_next, sent_prev, out, middle],
                     (below, above), bands, 4)


def last_call(flags, arrays, consts, bands, stride):
    level, out, middle = arrays[0], arrays[-2], arrays[-1]
    arrays = arrays[:-2]
    rows, width = level.shape[0], level.shape[1]
    final_shape = (bands, out.shape[0], out.shape[1])
    grid_spec = pltpu.PrefetchScalarGridSpec(
        num_scalar_prefetch=1,
        grid=(out.shape[-1] // LANES,),
        in_specs=[spec(a.shape) for a in arrays] + [whole(c) for c in consts]
        + [spec(out.shape), spec(middle.shape)],
        out_specs=pl.BlockSpec((LANES,) + final_shape[1:], lambda h, f: (h, 0, 0)),
        scratch_shapes=[
            pltpu.VMEM((rows + 2 * EDGE, width, LANES), jnp.float32),
            pltpu.VMEM((2, rows // 2, width, LANES), jnp.float32),
            pltpu.VMEM((rows // 2, width // 2, LANES), jnp.float32),
            pltpu.VMEM((2, width // 2, LANES), jnp.float32),
            pltpu.VMEM((2, width // 2, LANES), jnp.float32),
        ],
    )
    return pl.pallas_call(
        functools.partial(last_kernel, stride=stride),
        grid_spec=grid_spec,
        out_shape=jax.ShapeDtypeStruct(final_shape, jnp.float32),
        compiler_params=pltpu.CompilerParams(vmem_limit_bytes=100 * 1024 * 1024),
    )(flags, *arrays, *consts, out, middle)


def solution(mesh):
    assert mesh.shape["cols"] == 2
    placed = (P(None, ("groups", "rows"), "cols"), P())
    return jax.shard_map(
        on_device,
        mesh=mesh,
        in_specs=placed,
        out_specs=P(None, ("groups", "rows"), "cols"),
        check_vma=False,
    )
```

```python
import functools

import numpy as np
import jax
import jax.numpy as jnp
from jax import lax
from jax.experimental import pallas as pl
from jax.experimental.pallas import tpu as pltpu
from jax.sharding import PartitionSpec as P

LEVELS = 3
HALO = 32
EDGE = 4
LANES = 128


alpha_one = -1.586134342059924
beta_one = -0.052980118572961
alpha_two = 0.882911075530934
beta_two = 0.443506852043971
scale_k = 1.230174104914001


def shifted(x, axis, by):
    size = lax.axis_size(axis)
    pairs = [(i, i + by) for i in range(size) if 0 <= i + by < size]
    return lax.ppermute(x, axis, pairs)


def partials(x, axis):
    a1, b1 = alpha_one, beta_one
    n = x.shape[axis]

    def row(i):
        return lax.slice_in_dim(x, i, i + 1, axis=axis)

    s_pen, d_pen, s_last, d_last = row(n - 4), row(n - 3), row(n - 2), row(n - 1)
    s0, d0, s1 = row(0), row(1), row(2)
    to_next = jnp.concatenate(
        [s_last + b1 * (d_pen + a1 * (s_pen + s_last)), d_last + a1 * s_last], axis=axis
    )
    to_prev = jnp.concatenate([s0, d0 + a1 * (s0 + s1)], axis=axis)
    return to_next, to_prev


def fill_rows(ext, flags, from_prev, from_next, rows):
    a1 = alpha_one
    first = flags[1] == 1
    last = flags[2] == 1
    base = EDGE + rows

    @pl.when(first)
    def _():
        ext[0:EDGE] = jnp.concatenate(
            [ext[2 * EDGE - k : 2 * EDGE - k + 1] for k in range(EDGE)], axis=0
        )

    @pl.when(jnp.logical_not(first))
    def _():
        b, a = from_prev[0:1], from_prev[1:2]
        ext[0:EDGE] = jnp.concatenate([jnp.zeros_like(b), -a1 * b, b, a - a1 * b], axis=0)

    @pl.when(last)
    def _():
        ext[base : base + EDGE] = jnp.concatenate(
            [ext[base - 2 - k : base - 1 - k] for k in range(EDGE)], axis=0
        )

    @pl.when(jnp.logical_not(last))
    def _():
        s, dp = from_next[0:1], from_next[1:2]
        z = jnp.zeros_like(s)
        ext[base : base + EDGE] = jnp.concatenate([s, dp - a1 * s, z, z], axis=0)


def lift_block(flags, ext, half, out_ref, ll_ref, tn_ref, tp_ref, rows, width, stride,
               ahead_map=None):
    hr, hw = rows // 2, width // 2
    a1, b1, a2, b2 = alpha_one, beta_one, alpha_two, beta_two
    n = hr + EDGE
    pairs = ext[...].reshape(n, 2, width, LANES)
    s = pairs[:, 0]
    d = pairs[:, 1]

    def nxt0(v):
        return jnp.concatenate([v[1:], v[-1:]], axis=0)

    def prv0(v):
        return jnp.concatenate([v[:1], v[:-1]], axis=0)

    d = d + a1 * (s + nxt0(s))
    s = s + b1 * (prv0(d) + d)
    d = d + a2 * (s + nxt0(s))
    s = s + b2 * (prv0(d) + d)
    lo = EDGE // 2
    half[0] = s[lo : lo + hr] / scale_k
    half[1] = d[lo : lo + hr] * scale_k

    col = lax.broadcasted_iota(jnp.int32, (hr, hw, LANES), 1)

    def nxt1(v):
        return jnp.where(col == hw - 1, v, pltpu.roll(v, hw - 1, 1))

    def prv1(v):
        return jnp.where(col == 0, v, pltpu.roll(v, 1, 1))

    step = 2 * stride
    own_hw = out_ref.shape[1] // step
    on_left = flags[0] == 1

    def store(pr, e, o):
        rows_at = pl.ds(pr * stride, hr, stride=step)

        def put(lo):
            ee, oo = e[:, lo : lo + own_hw], o[:, lo : lo + own_hw]
            if stride == 1:
                both = jnp.stack([ee, oo], axis=2).reshape(hr, 2 * own_hw, LANES)
                out_ref[rows_at] = both
            else:
                out_ref[rows_at, pl.ds(0, own_hw, stride=step), :] = ee
                out_ref[rows_at, pl.ds(stride, own_hw, stride=step), :] = oo

        @pl.when(on_left)
        def _():
            put(0)

        @pl.when(jnp.logical_not(on_left))
        def _():
            put(hw - own_hw)

    for pr in range(2):
        e = half[pr, :, pl.ds(0, hw, stride=2), :]
        o = half[pr, :, pl.ds(1, hw, stride=2), :]
        o = o + a1 * (e + nxt1(e))
        e = e + b1 * (prv1(o) + o)
        o = o + a2 * (e + nxt1(e))
        e = e + b2 * (prv1(o) + o)
        e = e / scale_k
        o = o * scale_k
        store(pr, e, o)
        if pr == 0:
            ll_ref[...] = e
            to_next, to_prev = partials(e, 0)
            if ahead_map is None:
                tn_ref[...] = to_next
                tp_ref[...] = to_prev
            else:
                quarter = hw // 2
                used = hr - EDGE
                flat = e.reshape(hr * hw, LANES)
                ahead_next = jnp.dot(ahead_map[0: 2 * quarter, EDGE * hw :], flat[EDGE * hw :],
                                     precision=lax.Precision.HIGHEST,
                                     preferred_element_type=jnp.float32)
                ahead_prev = jnp.dot(ahead_map[2 * quarter :, : used * hw], flat[: used * hw],
                                     precision=lax.Precision.HIGHEST,
                                     preferred_element_type=jnp.float32)
                tn_ref[:, :hw] = to_next
                tn_ref[:, hw:] = ahead_next.reshape(2, quarter, LANES)
                tp_ref[:, :hw] = to_prev
                tp_ref[:, hw:] = ahead_prev.reshape(2, quarter, LANES)


def first_kernel(flags, own, halo, prev_own, prev_halo, next_own, next_halo, ahead_map,
                 out_ref, ll_ref, tn_ref, tp_ref, ext, half):
    rows, h = own.shape[0], halo.shape[1]
    width = own.shape[1] + h
    on_left = flags[0] == 1

    @pl.when(on_left)
    def _():
        ext[EDGE : EDGE + rows, 0 : width - h] = own[...]
        ext[EDGE : EDGE + rows, width - h : width] = halo[...]

    @pl.when(jnp.logical_not(on_left))
    def _():
        ext[EDGE : EDGE + rows, 0:h] = halo[...]
        ext[EDGE : EDGE + rows, h:width] = own[...]

    def joined(o, hh):
        return jnp.where(on_left, jnp.concatenate([o[...], hh[...]], axis=1),
                         jnp.concatenate([hh[...], o[...]], axis=1))

    fill_rows(ext, flags, joined(prev_own, prev_halo), joined(next_own, next_halo), rows)
    lift_block(flags, ext, half, out_ref, ll_ref, tn_ref, tp_ref, rows, width, 1, ahead_map)


def next_kernel(flags, x_ref, from_prev, from_next,
                out_ref, ll_ref, tn_ref, tp_ref, ext, half, *, stride):
    rows, width = x_ref.shape[0], x_ref.shape[1]
    ext[EDGE : EDGE + rows] = x_ref[...]
    fill_rows(ext, flags, from_prev[:, :width], from_next[:, :width], rows)
    lift_block(flags, ext, half, out_ref, ll_ref, tn_ref, tp_ref, rows, width, stride)


def last_kernel(flags, x_ref, got_prev, got_next, sent_next, sent_prev, below_map, above_map,
                prev_out, middle, final_ref, ext, half, ll, tn, tp, *, stride):
    rows, width = x_ref.shape[0], x_ref.shape[1]
    wide = 2 * width

    def share(m, sent):
        part = jnp.dot(m[...], sent[:, :wide].reshape(2 * wide, LANES),
                       precision=lax.Precision.HIGHEST, preferred_element_type=jnp.float32)
        return part.reshape(2, width, LANES)

    full = prev_out
    mr, mw = middle.shape[0], middle.shape[1]
    full[pl.ds(0, mr, stride=2), pl.ds(0, mw, stride=2), :] = middle[...]
    ext[EDGE : EDGE + rows] = x_ref[...]
    from_prev = got_prev[:, wide:] + share(below_map, sent_prev)
    from_next = got_next[:, wide:] + share(above_map, sent_next)
    fill_rows(ext, flags, from_prev, from_next, rows)
    lift_block(flags, ext, half, full, ll, tn, tp, rows, width, stride)
    final_ref[...] = jnp.transpose(full[...], (2, 0, 1))


def spec(shape):
    return pl.BlockSpec(shape[:-1] + (LANES,), lambda h, f: (0,) * (len(shape) - 1) + (h,))


def whole(a):
    return pl.BlockSpec(a.shape, lambda h, f: (0,) * a.ndim)


def level_call(kernel, flags, arrays, out_shape, rows, width, aliases, consts=(), ahead=False):
    bands = arrays[0].shape[-1]
    ll_shape = (rows // 2, width // 2, bands)
    edge_shape = (2, width // 2 + (width // 4 if ahead else 0), bands)
    outs = (out_shape, ll_shape, edge_shape, edge_shape)
    grid_spec = pltpu.PrefetchScalarGridSpec(
        num_scalar_prefetch=1,
        grid=(bands // LANES,),
        in_specs=[spec(a.shape) for a in arrays] + [whole(c) for c in consts],
        out_specs=tuple(spec(o) for o in outs),
        scratch_shapes=[
            pltpu.VMEM((rows + 2 * EDGE, width, LANES), jnp.float32),
            pltpu.VMEM((2, rows // 2, width, LANES), jnp.float32),
        ],
    )
    return pl.pallas_call(
        kernel,
        grid_spec=grid_spec,
        out_shape=tuple(jax.ShapeDtypeStruct(o, jnp.float32) for o in outs),
        input_output_aliases=aliases,
        compiler_params=pltpu.CompilerParams(vmem_limit_bytes=100 * 1024 * 1024),
    )(flags, *arrays, *consts)


def np_partials(x):
    a1, b1 = alpha_one, beta_one
    n = x.shape[0]
    s_pen, d_pen, s_last, d_last = x[n - 4], x[n - 3], x[n - 2], x[n - 1]
    to_next = np.stack([s_last + b1 * (d_pen + a1 * (s_pen + s_last)), d_last + a1 * s_last])
    to_prev = np.stack([x[0], x[1] + a1 * (x[0] + x[2])])
    return to_next, to_prev


def np_lift(v, axis):
    a1, b1, a2, b2 = alpha_one, beta_one, alpha_two, beta_two
    v = np.moveaxis(v, axis, 0)
    s, d = v[0::2].copy(), v[1::2].copy()

    def nxt(u):
        return np.concatenate([u[1:], u[-1:]])

    def prv(u):
        return np.concatenate([u[:1], u[:-1]])

    d = d + a1 * (s + nxt(s))
    s = s + b1 * (prv(d) + d)
    d = d + a2 * (s + nxt(s))
    s = s + b2 * (prv(d) + d)
    return np.moveaxis(s / scale_k, 0, axis), np.moveaxis(d * scale_k, 0, axis)


def np_ll(level, from_prev, from_next):
    a1 = alpha_one
    b, a = from_prev
    s, dp = from_next
    z = np.zeros_like(b)
    ext = np.concatenate([np.stack([z, -a1 * b, b, a - a1 * b]), level,
                          np.stack([s, dp - a1 * s, z, z])])
    rows_s, _ = np_lift(ext, 0)
    lo = EDGE // 2
    rows_s = rows_s[lo : lo + level.shape[0] // 2]
    ll, _ = np_lift(rows_s, 1)
    return ll


@functools.lru_cache(maxsize=None)
def next_level_maps(rows, width):
    zero_edge = np.zeros((2, width))
    own = np.zeros((rows, width, 4, width // 2))
    for r in range(rows):
        for w in range(width):
            unit = np.zeros((rows, width))
            unit[r, w] = 1.0
            ll = np_ll(unit, zero_edge, zero_edge)
            tn, tp = np_partials(ll)
            own[r, w] = np.concatenate([tn, tp])
    from_below = np.zeros((2, width, 2, width // 2))
    from_above = np.zeros((2, width, 2, width // 2))
    zero = np.zeros((rows, width))
    for p in range(2):
        for w in range(width):
            unit = np.zeros((2, width))
            unit[p, w] = 1.0
            from_below[p, w] = np_partials(np_ll(zero, zero_edge, unit))[0]
            from_above[p, w] = np_partials(np_ll(zero, unit, zero_edge))[1]
    return tuple(m.astype(np.float32) for m in (own, from_below, from_above))


def to_core_mate(x):
    return lax.ppermute(x, "cols", [(0, 1), (1, 0)])


def diagonal(x, by):
    rows = lax.axis_size("rows")
    pairs = [
        (r * 2 + c, (r + by) * 2 + 1 - c)
        for r in range(rows)
        for c in range(2)
        if 0 <= r + by < rows
    ]
    return lax.ppermute(x, ("rows", "cols"), pairs)


def on_device(radiance, decorrelation):
    bands, rows, width = radiance.shape
    padded_bands = -(-bands // LANES) * LANES
    on_left = lax.axis_index("cols") == 0
    flags = jnp.stack(
        [
            on_left,
            lax.axis_index("rows") == 0,
            lax.axis_index("rows") == lax.axis_size("rows") - 1,
        ]
    ).astype(jnp.int32)
    weights = jnp.pad(decorrelation, ((0, padded_bands - bands), (0, 0)))

    def facing(x):
        return jnp.where(on_left, x[:, width - HALO :], x[:, :HALO])

    def mix(x):
        return jnp.einsum("crw,bc->rwb", x, weights, precision=lax.Precision.HIGHEST,
                          preferred_element_type=jnp.float32)

    own = mix(radiance)
    mixed_next, mixed_prev = partials(own, 0)
    p_own = shifted(mixed_next, "rows", 1)
    n_own = shifted(mixed_prev, "rows", -1)
    p_halo = diagonal(facing(mixed_next), 1)
    n_halo = diagonal(facing(mixed_prev), -1)
    halo = to_core_mate(facing(own))
    ext_width = width + HALO
    out_shape = (rows, width, padded_bands)
    assert LEVELS == 3
    own_map, below_map, above_map = next_level_maps(rows // 2, ext_width // 2)
    ahead_map = jnp.asarray(own_map.reshape(-1, own_map.shape[2] * own_map.shape[3]).T)
    out, level, tn, tp = level_call(
        first_kernel, flags,
        [own, halo, p_own, p_halo, n_own, n_halo],
        out_shape, rows, ext_width, {}, consts=(ahead_map,), ahead=True)
    r, w = level.shape[0], level.shape[1]
    got_prev = shifted(tn, "rows", 1)
    got_next = shifted(tp, "rows", -1)
    sent_next, sent_prev = tn, tp
    middle, level, tn, tp = level_call(
        functools.partial(next_kernel, stride=1), flags,
        [level, got_prev, got_next], (rows // 2, width // 2, padded_bands), r, w, {})
    below = jnp.asarray(below_map.reshape(-1, below_map.shape[2] * below_map.shape[3]).T)
    above = jnp.asarray(above_map.reshape(-1, above_map.shape[2] * above_map.shape[3]).T)
    return last_call(flags, [level, got_prev, got_next, sent_next, sent_prev, out, middle],
                     (below, above), bands, 4)


def last_call(flags, arrays, consts, bands, stride):
    level, out, middle = arrays[0], arrays[-2], arrays[-1]
    arrays = arrays[:-2]
    rows, width = level.shape[0], level.shape[1]
    final_shape = (bands, out.shape[0], out.shape[1])
    grid_spec = pltpu.PrefetchScalarGridSpec(
        num_scalar_prefetch=1,
        grid=(out.shape[-1] // LANES,),
        in_specs=[spec(a.shape) for a in arrays] + [whole(c) for c in consts]
        + [spec(out.shape), spec(middle.shape)],
        out_specs=pl.BlockSpec((LANES,) + final_shape[1:], lambda h, f: (h, 0, 0)),
        scratch_shapes=[
            pltpu.VMEM((rows + 2 * EDGE, width, LANES), jnp.float32),
            pltpu.VMEM((2, rows // 2, width, LANES), jnp.float32),
            pltpu.VMEM((rows // 2, width // 2, LANES), jnp.float32),
            pltpu.VMEM((2, width // 2, LANES), jnp.float32),
            pltpu.VMEM((2, width // 2, LANES), jnp.float32),
        ],
    )
    return pl.pallas_call(
        functools.partial(last_kernel, stride=stride),
        grid_spec=grid_spec,
        out_shape=jax.ShapeDtypeStruct(final_shape, jnp.float32),
        compiler_params=pltpu.CompilerParams(vmem_limit_bytes=100 * 1024 * 1024),
    )(flags, *arrays, *consts, out, middle)


def solution(mesh):
    assert mesh.shape["cols"] == 2
    placed = (P(None, ("groups", "rows"), "cols"), P())
    return jax.shard_map(
        on_device,
        mesh=mesh,
        in_specs=placed,
        out_specs=P(None, ("groups", "rows"), "cols"),
        check_vma=False,
    )
```

```python
import functools

import numpy as np
import jax
import jax.numpy as jnp
from jax import lax
from jax.experimental import pallas as pl
from jax.experimental.pallas import tpu as pltpu
from jax.sharding import PartitionSpec as P

LEVELS = 3
HALO = 32
EDGE = 4
LANES = 128


alpha_one = -1.586134342059924
beta_one = -0.052980118572961
alpha_two = 0.882911075530934
beta_two = 0.443506852043971
scale_k = 1.230174104914001


def shifted(x, axis, by):
    size = lax.axis_size(axis)
    pairs = [(i, i + by) for i in range(size) if 0 <= i + by < size]
    return lax.ppermute(x, axis, pairs)


def partials(x, axis):
    a1, b1 = alpha_one, beta_one
    n = x.shape[axis]

    def row(i):
        return lax.slice_in_dim(x, i, i + 1, axis=axis)

    s_pen, d_pen, s_last, d_last = row(n - 4), row(n - 3), row(n - 2), row(n - 1)
    s0, d0, s1 = row(0), row(1), row(2)
    to_next = jnp.concatenate(
        [s_last + b1 * (d_pen + a1 * (s_pen + s_last)), d_last + a1 * s_last], axis=axis
    )
    to_prev = jnp.concatenate([s0, d0 + a1 * (s0 + s1)], axis=axis)
    return to_next, to_prev


def fill_rows(ext, flags, from_prev, from_next, rows):
    a1 = alpha_one
    first = flags[1] == 1
    last = flags[2] == 1
    base = EDGE + rows

    @pl.when(first)
    def _():
        ext[0:EDGE] = jnp.concatenate(
            [ext[2 * EDGE - k : 2 * EDGE - k + 1] for k in range(EDGE)], axis=0
        )

    @pl.when(jnp.logical_not(first))
    def _():
        b, a = from_prev[0:1], from_prev[1:2]
        ext[0:EDGE] = jnp.concatenate([jnp.zeros_like(b), -a1 * b, b, a - a1 * b], axis=0)

    @pl.when(last)
    def _():
        ext[base : base + EDGE] = jnp.concatenate(
            [ext[base - 2 - k : base - 1 - k] for k in range(EDGE)], axis=0
        )

    @pl.when(jnp.logical_not(last))
    def _():
        s, dp = from_next[0:1], from_next[1:2]
        z = jnp.zeros_like(s)
        ext[base : base + EDGE] = jnp.concatenate([s, dp - a1 * s, z, z], axis=0)


def lift_block(flags, ext, half, out_ref, ll_ref, tn_ref, tp_ref, rows, width, stride,
               ahead_map=None):
    hr, hw = rows // 2, width // 2
    a1, b1, a2, b2 = alpha_one, beta_one, alpha_two, beta_two
    n = hr + EDGE
    pairs = ext[...].reshape(n, 2, width, LANES)
    s = pairs[:, 0]
    d = pairs[:, 1]

    def nxt0(v):
        return jnp.concatenate([v[1:], v[-1:]], axis=0)

    def prv0(v):
        return jnp.concatenate([v[:1], v[:-1]], axis=0)

    d = d + a1 * (s + nxt0(s))
    s = s + b1 * (prv0(d) + d)
    d = d + a2 * (s + nxt0(s))
    s = s + b2 * (prv0(d) + d)
    lo = EDGE // 2
    half[0] = s[lo : lo + hr] / scale_k
    half[1] = d[lo : lo + hr] * scale_k

    col = lax.broadcasted_iota(jnp.int32, (hr, hw, LANES), 1)

    def nxt1(v):
        return jnp.where(col == hw - 1, v, pltpu.roll(v, hw - 1, 1))

    def prv1(v):
        return jnp.where(col == 0, v, pltpu.roll(v, 1, 1))

    step = 2 * stride
    own_hw = out_ref.shape[1] // step
    on_left = flags[0] == 1

    def store(pr, e, o):
        rows_at = pl.ds(pr * stride, hr, stride=step)

        @pl.when(on_left)
        def _():
            out_ref[rows_at, pl.ds(0, own_hw, stride=step), :] = e[:, :own_hw]
            out_ref[rows_at, pl.ds(stride, own_hw, stride=step), :] = o[:, :own_hw]

        @pl.when(jnp.logical_not(on_left))
        def _():
            out_ref[rows_at, pl.ds(0, own_hw, stride=step), :] = e[:, hw - own_hw :]
            out_ref[rows_at, pl.ds(stride, own_hw, stride=step), :] = o[:, hw - own_hw :]

    for pr in range(2):
        e = half[pr, :, pl.ds(0, hw, stride=2), :]
        o = half[pr, :, pl.ds(1, hw, stride=2), :]
        o = o + a1 * (e + nxt1(e))
        e = e + b1 * (prv1(o) + o)
        o = o + a2 * (e + nxt1(e))
        e = e + b2 * (prv1(o) + o)
        e = e / scale_k
        o = o * scale_k
        store(pr, e, o)
        if pr == 0:
            ll_ref[...] = e
            if tn_ref is None:
                continue
            to_next, to_prev = partials(e, 0)
            if ahead_map is None:
                tn_ref[...] = to_next
                tp_ref[...] = to_prev
            else:
                quarter = hw // 2
                used = hr - EDGE
                flat = e.reshape(hr * hw, LANES)
                ahead_next = jnp.dot(ahead_map[0: 2 * quarter, EDGE * hw :], flat[EDGE * hw :],
                                     precision=lax.Precision.HIGHEST,
                                     preferred_element_type=jnp.float32)
                ahead_prev = jnp.dot(ahead_map[2 * quarter :, : used * hw], flat[: used * hw],
                                     precision=lax.Precision.HIGHEST,
                                     preferred_element_type=jnp.float32)
                tn_ref[:, :hw] = to_next
                tn_ref[:, hw:] = ahead_next.reshape(2, quarter, LANES)
                tp_ref[:, :hw] = to_prev
                tp_ref[:, hw:] = ahead_prev.reshape(2, quarter, LANES)


def first_kernel(flags, own, halo, prev_own, prev_halo, next_own, next_halo, ahead_map,
                 out_ref, ll_ref, tn_ref, tp_ref, ext, half):
    rows, h = own.shape[0], halo.shape[1]
    width = own.shape[1] + h
    on_left = flags[0] == 1

    @pl.when(on_left)
    def _():
        ext[EDGE : EDGE + rows, 0 : width - h] = own[...]
        ext[EDGE : EDGE + rows, width - h : width] = halo[...]

    @pl.when(jnp.logical_not(on_left))
    def _():
        ext[EDGE : EDGE + rows, 0:h] = halo[...]
        ext[EDGE : EDGE + rows, h:width] = own[...]

    def joined(o, hh):
        return jnp.where(on_left, jnp.concatenate([o[...], hh[...]], axis=1),
                         jnp.concatenate([hh[...], o[...]], axis=1))

    fill_rows(ext, flags, joined(prev_own, prev_halo), joined(next_own, next_halo), rows)
    lift_block(flags, ext, half, out_ref, ll_ref, tn_ref, tp_ref, rows, width, 1, ahead_map)


def next_kernel(flags, x_ref, from_prev, from_next,
                out_ref, ll_ref, ext, half, *, stride):
    tn_ref = tp_ref = None
    rows, width = x_ref.shape[0], x_ref.shape[1]
    ext[EDGE : EDGE + rows] = x_ref[...]
    fill_rows(ext, flags, from_prev[:, :width], from_next[:, :width], rows)
    lift_block(flags, ext, half, out_ref, ll_ref, tn_ref, tp_ref, rows, width, stride)


def last_kernel(flags, x_ref, got_prev, got_next, sent_next, sent_prev, below_map, above_map,
                prev_out, middle, final_ref, ext, half, ll, tn, tp, *, stride):
    rows, width = x_ref.shape[0], x_ref.shape[1]
    wide = 2 * width

    def share(m, sent):
        part = jnp.dot(m[...], sent[:, :wide].reshape(2 * wide, LANES),
                       precision=lax.Precision.HIGHEST, preferred_element_type=jnp.float32)
        return part.reshape(2, width, LANES)

    full = prev_out
    mr, mw = middle.shape[0], middle.shape[1]
    full[pl.ds(0, mr, stride=2), pl.ds(0, mw, stride=2), :] = middle[...]
    ext[EDGE : EDGE + rows] = x_ref[...]
    from_prev = got_prev[:, wide:] + share(below_map, sent_prev)
    from_next = got_next[:, wide:] + share(above_map, sent_next)
    fill_rows(ext, flags, from_prev, from_next, rows)
    lift_block(flags, ext, half, full, ll, tn, tp, rows, width, stride)
    final_ref[...] = jnp.transpose(full[...], (2, 0, 1))


def spec(shape):
    return pl.BlockSpec(shape[:-1] + (LANES,), lambda h, f: (0,) * (len(shape) - 1) + (h,))


def whole(a):
    return pl.BlockSpec(a.shape, lambda h, f: (0,) * a.ndim)


def level_call(kernel, flags, arrays, out_shape, rows, width, aliases, consts=(), ahead=False,
               edges=True):
    bands = arrays[0].shape[-1]
    ll_shape = (rows // 2, width // 2, bands)
    edge_shape = (2, width // 2 + (width // 4 if ahead else 0), bands)
    outs = (out_shape, ll_shape, edge_shape, edge_shape) if edges else (out_shape, ll_shape)
    grid_spec = pltpu.PrefetchScalarGridSpec(
        num_scalar_prefetch=1,
        grid=(bands // LANES,),
        in_specs=[spec(a.shape) for a in arrays] + [whole(c) for c in consts],
        out_specs=tuple(spec(o) for o in outs),
        scratch_shapes=[
            pltpu.VMEM((rows + 2 * EDGE, width, LANES), jnp.float32),
            pltpu.VMEM((2, rows // 2, width, LANES), jnp.float32),
        ],
    )
    return pl.pallas_call(
        kernel,
        grid_spec=grid_spec,
        out_shape=tuple(jax.ShapeDtypeStruct(o, jnp.float32) for o in outs),
        input_output_aliases=aliases,
        compiler_params=pltpu.CompilerParams(vmem_limit_bytes=100 * 1024 * 1024),
    )(flags, *arrays, *consts)


def np_partials(x):
    a1, b1 = alpha_one, beta_one
    n = x.shape[0]
    s_pen, d_pen, s_last, d_last = x[n - 4], x[n - 3], x[n - 2], x[n - 1]
    to_next = np.stack([s_last + b1 * (d_pen + a1 * (s_pen + s_last)), d_last + a1 * s_last])
    to_prev = np.stack([x[0], x[1] + a1 * (x[0] + x[2])])
    return to_next, to_prev


def np_lift(v, axis):
    a1, b1, a2, b2 = alpha_one, beta_one, alpha_two, beta_two
    v = np.moveaxis(v, axis, 0)
    s, d = v[0::2].copy(), v[1::2].copy()

    def nxt(u):
        return np.concatenate([u[1:], u[-1:]])

    def prv(u):
        return np.concatenate([u[:1], u[:-1]])

    d = d + a1 * (s + nxt(s))
    s = s + b1 * (prv(d) + d)
    d = d + a2 * (s + nxt(s))
    s = s + b2 * (prv(d) + d)
    return np.moveaxis(s / scale_k, 0, axis), np.moveaxis(d * scale_k, 0, axis)


def np_ll(level, from_prev, from_next):
    a1 = alpha_one
    b, a = from_prev
    s, dp = from_next
    z = np.zeros_like(b)
    ext = np.concatenate([np.stack([z, -a1 * b, b, a - a1 * b]), level,
                          np.stack([s, dp - a1 * s, z, z])])
    rows_s, _ = np_lift(ext, 0)
    lo = EDGE // 2
    rows_s = rows_s[lo : lo + level.shape[0] // 2]
    ll, _ = np_lift(rows_s, 1)
    return ll


@functools.lru_cache(maxsize=None)
def next_level_maps(rows, width):
    zero_edge = np.zeros((2, width))
    own = np.zeros((rows, width, 4, width // 2))
    for r in range(rows):
        for w in range(width):
            unit = np.zeros((rows, width))
            unit[r, w] = 1.0
            ll = np_ll(unit, zero_edge, zero_edge)
            tn, tp = np_partials(ll)
            own[r, w] = np.concatenate([tn, tp])
    from_below = np.zeros((2, width, 2, width // 2))
    from_above = np.zeros((2, width, 2, width // 2))
    zero = np.zeros((rows, width))
    for p in range(2):
        for w in range(width):
            unit = np.zeros((2, width))
            unit[p, w] = 1.0
            from_below[p, w] = np_partials(np_ll(zero, zero_edge, unit))[0]
            from_above[p, w] = np_partials(np_ll(zero, unit, zero_edge))[1]
    return tuple(m.astype(np.float32) for m in (own, from_below, from_above))


def to_core_mate(x):
    return lax.ppermute(x, "cols", [(0, 1), (1, 0)])


def diagonal(x, by):
    rows = lax.axis_size("rows")
    pairs = [
        (r * 2 + c, (r + by) * 2 + 1 - c)
        for r in range(rows)
        for c in range(2)
        if 0 <= r + by < rows
    ]
    return lax.ppermute(x, ("rows", "cols"), pairs)


def on_device(radiance, decorrelation):
    bands, rows, width = radiance.shape
    padded_bands = -(-bands // LANES) * LANES
    on_left = lax.axis_index("cols") == 0
    flags = jnp.stack(
        [
            on_left,
            lax.axis_index("rows") == 0,
            lax.axis_index("rows") == lax.axis_size("rows") - 1,
        ]
    ).astype(jnp.int32)
    weights = jnp.pad(decorrelation, ((0, padded_bands - bands), (0, 0)))

    def facing(x):
        return jnp.where(on_left, x[:, width - HALO :], x[:, :HALO])

    def mix(x):
        return jnp.einsum("crw,bc->rwb", x, weights, precision=lax.Precision.HIGHEST,
                          preferred_element_type=jnp.float32)

    own = mix(radiance)
    mixed_next, mixed_prev = partials(own, 0)
    p_own = shifted(mixed_next, "rows", 1)
    n_own = shifted(mixed_prev, "rows", -1)
    p_halo = diagonal(facing(mixed_next), 1)
    n_halo = diagonal(facing(mixed_prev), -1)
    halo = to_core_mate(facing(own))
    ext_width = width + HALO
    out_shape = (rows, width, padded_bands)
    assert LEVELS == 3
    own_map, below_map, above_map = next_level_maps(rows // 2, ext_width // 2)
    ahead_map = jnp.asarray(own_map.reshape(-1, own_map.shape[2] * own_map.shape[3]).T)
    out, level, tn, tp = level_call(
        first_kernel, flags,
        [own, halo, p_own, p_halo, n_own, n_halo],
        out_shape, rows, ext_width, {}, consts=(ahead_map,), ahead=True)
    r, w = level.shape[0], level.shape[1]
    got_prev = shifted(tn, "rows", 1)
    got_next = shifted(tp, "rows", -1)
    sent_next, sent_prev = tn, tp
    middle, level = level_call(
        functools.partial(next_kernel, stride=1), flags,
        [level, got_prev, got_next], (rows // 2, width // 2, padded_bands), r, w, {},
        edges=False)
    below = jnp.asarray(below_map.reshape(-1, below_map.shape[2] * below_map.shape[3]).T)
    above = jnp.asarray(above_map.reshape(-1, above_map.shape[2] * above_map.shape[3]).T)
    return last_call(flags, [level, got_prev, got_next, sent_next, sent_prev, out, middle],
                     (below, above), bands, 4)


def last_call(flags, arrays, consts, bands, stride):
    level, out, middle = arrays[0], arrays[-2], arrays[-1]
    arrays = arrays[:-2]
    rows, width = level.shape[0], level.shape[1]
    final_shape = (bands, out.shape[0], out.shape[1])
    grid_spec = pltpu.PrefetchScalarGridSpec(
        num_scalar_prefetch=1,
        grid=(out.shape[-1] // LANES,),
        in_specs=[spec(a.shape) for a in arrays] + [whole(c) for c in consts]
        + [spec(out.shape), spec(middle.shape)],
        out_specs=pl.BlockSpec((LANES,) + final_shape[1:], lambda h, f: (h, 0, 0)),
        scratch_shapes=[
            pltpu.VMEM((rows + 2 * EDGE, width, LANES), jnp.float32),
            pltpu.VMEM((2, rows // 2, width, LANES), jnp.float32),
            pltpu.VMEM((rows // 2, width // 2, LANES), jnp.float32),
            pltpu.VMEM((2, width // 2, LANES), jnp.float32),
            pltpu.VMEM((2, width // 2, LANES), jnp.float32),
        ],
    )
    return pl.pallas_call(
        functools.partial(last_kernel, stride=stride),
        grid_spec=grid_spec,
        out_shape=jax.ShapeDtypeStruct(final_shape, jnp.float32),
        compiler_params=pltpu.CompilerParams(vmem_limit_bytes=100 * 1024 * 1024),
    )(flags, *arrays, *consts, out, middle)


def solution(mesh):
    assert mesh.shape["cols"] == 2
    placed = (P(None, ("groups", "rows"), "cols"), P())
    return jax.shard_map(
        on_device,
        mesh=mesh,
        in_specs=placed,
        out_specs=P(None, ("groups", "rows"), "cols"),
        check_vma=False,
    )
```
